512 devices in a mesh: guide: 2 (over core), seq: 64 (over x, z), tp: 4 (over y).
Axes of the slice: x: 4, y: 4, z: 16, core: 2. Of those that a mesh axis runs over, the one named last changes fastest.
Arguments:
- hidden: bfloat16 [2, 32, 2048], P('guide'), may hold values from -6 to 6
- attn_gain: float32 [2048], replicated, may hold values from 0.25 to 1.75
- final_gain: float32 [2048], replicated, may hold values from 0.25 to 1.75
- query_gain: float32 [64], replicated, may hold values from 0.5 to 6
- new_key_gain: float32 [64], replicated, may hold values from 0.5 to 3
- query_weight: bfloat16 [2048, 1280], P('seq', 'tp'), may hold values from -1 to 1
- key_value_weight: bfloat16 [2048, 640], P('seq'), may hold values from -0.125 to 0.125
- output_weight: bfloat16 [1280, 2048], P('tp'), may hold values from -0.15625 to 0.15625
- head_weight: bfloat16 [2048, 32000], P('seq', 'tp'), may hold values from -0.125 to 0.125
- page_cache: bfloat16 [2, 768, 128, 640], P('guide', 'seq'), may hold values from -12 to 12
- cache_length: int32 [2, 32], P('guide'), may hold values from 1 to 16384, as said below
- page_table: int32 [2, 32, 128], P('guide'), may hold values from -1 to 767, as said below
Outputs:
- guided: float32 [32, 32000], P('guide', 'tp')
The draws below stay inside these ranges and needn't reach their ends.
Inputs may be any that keep to these rules, and one draw needn't show every extreme that they name: `cache_length`: in each group one request holds exactly 16384 tokens. page_table[g, i, p] is the slot of page_cache[g] (seq index times 12 plus local slot) that holds tokens p * 128 to p * 128 + 127 of request i, for p below ceil(cache_length[g, i] / 128); it is -1 beyond. A slot holds at most one page; many slots are empty.
All inputs are finite; a program needn't handle non-finite values.
Results may differ from the reference program's by a relative error of at most 0.0093.
Values sent between devices are 32-bit elements; how exact they have to be, the bound alone decides.
No kernel may reach another device: no remote copies, remote signals or barrier semaphores. Data moves between devices by JAX's collectives and lax.ppermute only.
A program may use at most 64 MiB of HBM per device.

```python
import math
import jax
import jax.numpy as jnp
from jax import lax

MODEL_WIDTH = 2048
QUERY_HEADS = 20
KEY_VALUE_HEADS = 5
HEAD_SIZE = 64
V = 32000
PAGE_TOKENS = 128
GROUP_REQUESTS = 32
SLOTS = 12
GROUP_PAGE_SLOTS = 768
LONGEST_PAGES = 128


def plan_cache(key):
    length_list = []
    map_list = []
    long_list = []
    extra_cap = min(LONGEST_PAGES - 1, (GROUP_PAGE_SLOTS - LONGEST_PAGES) // (GROUP_REQUESTS - 1) - 1)
    for group_at in range(2):
        group_key = jax.random.fold_in(jax.random.fold_in(key, 4051), group_at)
        first_draw = jax.random.randint(jax.random.fold_in(group_key, 1), (GROUP_REQUESTS,), 0, extra_cap + 1)
        second_draw = jax.random.randint(jax.random.fold_in(group_key, 2), (GROUP_REQUESTS,), 0, extra_cap + 1)
        extra_pages = first_draw * second_draw // max(extra_cap, 1)
        long_request = jax.random.randint(jax.random.fold_in(group_key, 3), (), 0, GROUP_REQUESTS)
        is_long = jnp.arange(GROUP_REQUESTS) == long_request
        counts = jnp.where(is_long, LONGEST_PAGES, 1 + extra_pages)
        last_fill = jax.random.randint(jax.random.fold_in(group_key, 4), (GROUP_REQUESTS,), 1, PAGE_TOKENS + 1)
        lengths = jnp.where(is_long, LONGEST_PAGES * PAGE_TOKENS, (counts - 1) * PAGE_TOKENS + last_fill)
        device_bias = jax.random.randint(jax.random.fold_in(group_key, 5), (GROUP_PAGE_SLOTS // SLOTS,), 0, 4)
        jitter = jax.random.randint(jax.random.fold_in(group_key, 6), (GROUP_PAGE_SLOTS,), 0, 1024)
        slot_score = jnp.repeat(device_bias, SLOTS) * 4194304 + jitter * 2048 + jnp.arange(GROUP_PAGE_SLOTS)
        slot_order = jnp.argsort(slot_score)
        offsets = jnp.cumsum(counts) - counts
        page_number = jnp.arange(LONGEST_PAGES)
        flat_index = offsets[:, None] + page_number[None, :]
        picked = jnp.take(slot_order, jnp.clip(flat_index, 0, GROUP_PAGE_SLOTS - 1))
        page_map = jnp.where(page_number[None, :] < counts[:, None], picked, -1)
        length_list.append(lengths.astype(jnp.int32))
        map_list.append(page_map.astype(jnp.int32))
        long_list.append(long_request.astype(jnp.int32))
    return (jnp.stack(length_list).astype(jnp.int32), jnp.stack(map_list).astype(jnp.int32))


def draw_cache_length(key, part):
    return plan_cache(key)[0]


def draw_page_table(key, part):
    return plan_cache(key)[1]


def draw_query_gain(key, part):
    gain_key = jax.random.fold_in(key, 7201)
    value_rows = jnp.exp(jax.random.uniform(gain_key, (HEAD_SIZE,), jnp.float32, jnp.log(0.5), jnp.log(2.0)))
    return value_rows.astype(jnp.float32)


def draw_query_weight(key, part):
    randomized_portion = jax.random.truncated_normal(jax.random.fold_in(key, 7101), -4.0, 4.0, (MODEL_WIDTH, QUERY_HEADS * HEAD_SIZE), jnp.float32) * MODEL_WIDTH ** (-0.5)
    return randomized_portion.astype(jnp.bfloat16)


def draw_page_cache(key, part):
    value_rows = jax.random.truncated_normal(jax.random.fold_in(key, 7303), -6.0, 6.0, (2, GROUP_PAGE_SLOTS, PAGE_TOKENS, 2 * KEY_VALUE_HEADS * HEAD_SIZE), jnp.float32)
    return value_rows.astype(jnp.bfloat16)


def levels(own_key, shape, split, low, largest):
    def one(dim, parts):
        heights = jax.random.uniform(jax.random.fold_in(jax.random.fold_in(own_key, 6), dim), (parts,), jnp.float32, low / len(split), largest / len(split))
        return jnp.repeat(jnp.exp(heights), shape[dim] // parts).reshape((-1,) + (1,) * (len(shape) - dim - 1))

    level = one(*split[0])
    for cut in split[1:]:
        level = level * one(*cut)
    return level


def noise(own_key, dims, scale, reach, pieces=(), dtype=jnp.bfloat16):
    factor_of = levels(own_key, dims, pieces, -0.22, 0.18) if pieces else 1.0
    result = jax.random.normal(own_key, dims, jnp.float32) * scale * factor_of
    return jnp.minimum(jnp.maximum(result, -reach), reach).astype(dtype)


def setup_inputs(seed: int = 0) -> dict:
    keys = jax.random.split(jax.random.key(seed), 13)
    return {
        "hidden": noise(keys[0], (2, GROUP_REQUESTS, MODEL_WIDTH), 1.0, 6.0, ((0, 2),)),
        "attn_gain": jnp.clip(1.0 + 0.15 * jax.random.normal(keys[1], (MODEL_WIDTH,), jnp.float32), 0.25, 1.75),
        "final_gain": jnp.clip(1.0 + 0.15 * jax.random.normal(keys[2], (MODEL_WIDTH,), jnp.float32), 0.25, 1.75),
        "query_gain": draw_query_gain(jax.random.fold_in(keys[12], 71), 0),
        "new_key_gain": jnp.clip(jnp.exp(jax.random.uniform(keys[4], (HEAD_SIZE,), jnp.float32, math.log(0.5), math.log(3.0))), 0.5, 3.0),
        "query_weight": draw_query_weight(jax.random.fold_in(keys[12], 71), 0),
        "key_value_weight": noise(keys[6], (MODEL_WIDTH, 2 * KEY_VALUE_HEADS * HEAD_SIZE), MODEL_WIDTH ** -0.5, 0.125, ((0, 64),)),
        "output_weight": noise(keys[7], (QUERY_HEADS * HEAD_SIZE, MODEL_WIDTH), (QUERY_HEADS * HEAD_SIZE) ** -0.5, 0.15625, ((0, 4),)),
        "head_weight": noise(keys[8], (MODEL_WIDTH, V), MODEL_WIDTH ** -0.5, 0.125, ((0, 64), (1, 4))),
        "page_cache": draw_page_cache(jax.random.fold_in(keys[12], 71), 0),
        "cache_length": draw_cache_length(jax.random.fold_in(keys[12], 71), 0),
        "page_table": draw_page_table(jax.random.fold_in(keys[12], 71), 0),
    }


GUIDE_WEIGHT = 2.5
NORM_EPS = 1e-06
NEG_FILL = -1e+30

def norm_rows(token_rows, scale_gain):
    mean_square = lax.optimization_barrier(jnp.mean(token_rows * token_rows, axis=-1, keepdims=True))
    return (token_rows * lax.rsqrt(mean_square + NORM_EPS) * scale_gain.astype(jnp.float32)).astype(jnp.bfloat16)

def per_head_norm(vectors, head_gain):
    mean_square = lax.optimization_barrier(jnp.mean(vectors * vectors, axis=-1, keepdims=True))
    return vectors * lax.rsqrt(mean_square + NORM_EPS) * head_gain.astype(jnp.float32)

def rotate(vectors, positions):
    half_dim = vectors.shape[-1] // 2
    frequency = 10000.0 ** (-jnp.arange(half_dim).astype(jnp.float32) / half_dim)
    angles = positions.astype(jnp.float32)[:, None] * frequency[None, :]
    cosine = jnp.cos(angles)[:, None, :]
    sine_part = jnp.sin(angles)[:, None, :]
    first_half = vectors[..., :half_dim]
    second_half = vectors[..., half_dim:]
    return jnp.concatenate([first_half * cosine - second_half * sine_part, second_half * cosine + first_half * sine_part], axis=-1)

def attend_group(queries, key_new, fresh_value, cache_for_group, lengths, page_map):
    group_width = QUERY_HEADS // KEY_VALUE_HEADS
    scale = 1.0 / HEAD_SIZE ** 0.5

    def attend_request(inputs):
        query_row, key_row, value_row, length, page_slots = inputs
        slot_index_list = jnp.clip(page_slots, 0, GROUP_PAGE_SLOTS - 1)
        page_tile = cache_for_group[slot_index_list].reshape(LONGEST_PAGES * PAGE_TOKENS, 2, KEY_VALUE_HEADS, HEAD_SIZE)
        key_full = jnp.repeat(page_tile[:, 0].astype(jnp.float32), group_width, axis=1)
        value_full = jnp.repeat(page_tile[:, 1].astype(jnp.float32), group_width, axis=1)
        query_wide = query_row.astype(jnp.float32)
        scores = jnp.einsum('hd,nhd->hn', query_wide, key_full) * scale
        is_valid = jnp.arange(LONGEST_PAGES * PAGE_TOKENS) < length
        scores = jnp.where(is_valid[None, :], scores, NEG_FILL)
        key_self = jnp.repeat(key_row.astype(jnp.float32), group_width, axis=0)
        value_self = jnp.repeat(value_row.astype(jnp.float32), group_width, axis=0)
        self_score = lax.optimization_barrier(jnp.sum(query_wide * key_self, axis=1)) * scale
        row_max = jnp.maximum(lax.optimization_barrier(jnp.max(scores, axis=1)), self_score)
        weights = jnp.where(is_valid[None, :], jnp.exp(scores - row_max[:, None]), 0.0).astype(jnp.bfloat16)
        weights = lax.optimization_barrier(weights).astype(jnp.float32)
        self_weight = jnp.exp(self_score - row_max)
        denominator = lax.optimization_barrier(jnp.sum(weights, axis=1)) + self_weight
        weighted = jnp.einsum('hn,nhd->hd', weights, value_full) + self_weight[:, None] * value_self
        return (weighted / denominator[:, None]).astype(jnp.bfloat16)
    return lax.map(attend_request, (queries, key_new, fresh_value, lengths, page_map))

def reference(hidden, attn_gain, final_gain, query_gain, new_key_gain, query_weight, key_value_weight, output_weight, head_weight, page_cache, cache_length, page_table):
    group_logits = []
    for group_at in range(2):
        token_rows = hidden[group_at].astype(jnp.float32)
        normed = norm_rows(token_rows, attn_gain)
        queries = jnp.dot(normed, query_weight, preferred_element_type=jnp.float32).reshape(GROUP_REQUESTS, QUERY_HEADS, HEAD_SIZE)
        key_value = jnp.dot(normed, key_value_weight, preferred_element_type=jnp.float32)
        positions = cache_length[group_at]
        query_normed = per_head_norm(queries, query_gain)
        normalized_key = per_head_norm(key_value[:, :KEY_VALUE_HEADS * HEAD_SIZE].reshape(GROUP_REQUESTS, KEY_VALUE_HEADS, HEAD_SIZE), new_key_gain)
        query_rot = rotate(query_normed, positions).astype(jnp.bfloat16)
        key_new = rotate(normalized_key, positions).astype(jnp.bfloat16)
        fresh_value = key_value[:, KEY_VALUE_HEADS * HEAD_SIZE:].reshape(GROUP_REQUESTS, KEY_VALUE_HEADS, HEAD_SIZE).astype(jnp.bfloat16)
        attended = attend_group(query_rot, key_new, fresh_value, page_cache[group_at], positions, page_table[group_at])
        attended = attended.reshape(GROUP_REQUESTS, QUERY_HEADS * HEAD_SIZE)
        residual = token_rows + jnp.dot(attended, output_weight, preferred_element_type=jnp.float32)
        final_rows = norm_rows(residual, final_gain)
        group_logits.append(jnp.dot(final_rows, head_weight, preferred_element_type=jnp.float32))
    conditional = group_logits[0]
    unconditional = group_logits[1]
    return unconditional + GUIDE_WEIGHT * (conditional - unconditional)
```

```python
import jax
import jax.numpy as jnp
from jax import lax
from jax.sharding import PartitionSpec as P

QUERY_HEADS = 20
KEY_VALUE_HEADS = 5
HEAD_SIZE = 64


GUIDE_WEIGHT = 2.5
NORM_EPS = 1e-06
NEG_FILL = -1e30


def from_partner(value, axis, stride):
    mask = 2**stride
    pairs = [(source, source ^ mask) for source in range(lax.axis_size(axis))]
    return lax.ppermute(value, axis, pairs)


def norm_rows(token_rows, scale_gain):
    mean_square = jnp.mean(token_rows * token_rows, axis=-1, keepdims=True)
    return (token_rows * lax.rsqrt(mean_square + NORM_EPS) * scale_gain).astype(jnp.bfloat16)


def per_head_norm(vectors, head_gain):
    mean_square = jnp.mean(vectors * vectors, axis=-1, keepdims=True)
    return vectors * lax.rsqrt(mean_square + NORM_EPS) * head_gain


def rotate(vectors, positions):
    half_dim = vectors.shape[-1] // 2
    frequency = 10000.0 ** (-jnp.arange(half_dim).astype(jnp.float32) / half_dim)
    angles = positions.astype(jnp.float32)[:, None] * frequency[None, :]
    cosine = jnp.cos(angles)[:, None, :]
    sine_part = jnp.sin(angles)[:, None, :]
    first_half = vectors[..., :half_dim]
    second_half = vectors[..., half_dim:]
    return jnp.concatenate(
        [
            first_half * cosine - second_half * sine_part,
            second_half * cosine + first_half * sine_part,
        ],
        axis=-1,
    )


def all_reduce(value, axis):
    count = lax.axis_size(axis)
    flat = value.reshape(-1)
    chunk = -(-flat.size // count)
    chunk = -(-chunk // 128) * 128
    flat = jnp.pad(flat, (0, count * chunk - flat.size))
    parts = lax.all_to_all(flat.reshape(count, chunk), axis, 0, 0, tiled=True)
    total = jnp.sum(parts, axis=0, keepdims=True)
    whole = lax.all_to_all(jnp.broadcast_to(total, (count, chunk)), axis, 0, 0, tiled=True)
    return whole.reshape(-1)[: value.size].reshape(value.shape)


def spread_units(units, count, fill):
    per = -(-units.shape[0] // count)
    padding = [(0, count * per - units.shape[0])] + [(0, 0)] * (units.ndim - 1)
    return jnp.pad(units, padding, constant_values=fill).reshape((count, per) + units.shape[1:])


def merge_attention(local_max, local_total, local_weighted, self_score, fresh_value, axis):
    count = lax.axis_size(axis)
    me = lax.axis_index(axis)
    unit_count = local_max.shape[0]
    stats = jnp.concatenate([local_max[:, None], local_total[:, None], local_weighted], axis=1)
    spread = spread_units(stats, count, 0.0)
    spread = spread.at[:, :, 0].set(spread_units(local_max, count, NEG_FILL))
    parts = lax.all_to_all(spread, axis, 0, 0, tiled=True)
    part_max = parts[:, :, 0]
    merged_max = jnp.max(part_max, axis=0)
    rescale = jnp.exp(part_max - merged_max[None, :])
    merged_total = jnp.sum(rescale * parts[:, :, 1], axis=0)
    merged_weighted = jnp.sum(rescale[:, :, None] * parts[:, :, 2:], axis=0)
    own_score = lax.dynamic_index_in_dim(spread_units(self_score, count, 0.0), me, 0, keepdims=False)
    own_value = lax.dynamic_index_in_dim(spread_units(fresh_value, count, 0.0), me, 0, keepdims=False)
    row_max = jnp.maximum(merged_max, own_score)
    old_scale = jnp.exp(merged_max - row_max)
    self_weight = jnp.exp(own_score - row_max)
    denominator = merged_total * old_scale + self_weight
    weighted = merged_weighted * old_scale[:, None] + self_weight[:, None] * own_value
    fraction = jnp.concatenate([weighted, denominator[:, None]], axis=1)
    gathered = lax.all_to_all(
        jnp.broadcast_to(fraction[None], (count,) + fraction.shape), axis, 0, 0, tiled=True
    ).reshape(-1, fraction.shape[-1])[:unit_count]
    return (gathered[:, :-1] / gathered[:, -1:]).astype(jnp.bfloat16)


def shards(
    hidden,
    attn_gain,
    final_gain,
    query_gain,
    new_key_gain,
    query_weight,
    key_value_weight,
    output_weight,
    head_weight,
    page_cache,
    cache_length,
    page_table,
):
    token_rows = hidden[0].astype(jnp.float32)
    lengths = cache_length[0]
    page_map = page_table[0]
    nearby_cache = page_cache[0]
    request_number = token_rows.shape[0]
    half_rows = request_number // 2
    part_width = query_weight.shape[0]
    nearby_heads = query_weight.shape[1] // HEAD_SIZE
    query_width = query_weight.shape[1]
    scale = 1.0 / HEAD_SIZE**0.5
    shard_index = lax.axis_index("seq")
    normed = norm_rows(token_rows, attn_gain)
    normed_part = lax.dynamic_slice_in_dim(normed, shard_index * part_width, part_width, 1)
    projected = all_reduce(
        jnp.concatenate(
            [
                jnp.dot(normed_part, query_weight, preferred_element_type=jnp.float32),
                jnp.dot(normed_part, key_value_weight, preferred_element_type=jnp.float32),
            ],
            axis=1,
        ),
        "seq",
    )
    query_sum = projected[:, :query_width]
    key_value_sum = projected[:, query_width:]
    head_mapping = (lax.axis_index("tp") * nearby_heads + jnp.arange(nearby_heads)) // (
        QUERY_HEADS // KEY_VALUE_HEADS
    )
    query_normed = per_head_norm(
        query_sum.reshape(request_number, nearby_heads, HEAD_SIZE), query_gain
    )
    normalized_key = per_head_norm(
        key_value_sum[:, : KEY_VALUE_HEADS * HEAD_SIZE].reshape(
            request_number, KEY_VALUE_HEADS, HEAD_SIZE
        ),
        new_key_gain,
    )
    query_rot = rotate(query_normed, lengths).astype(jnp.bfloat16)
    key_all = rotate(normalized_key, lengths)
    value_complete = key_value_sum[:, KEY_VALUE_HEADS * HEAD_SIZE :].reshape(
        request_number, KEY_VALUE_HEADS, HEAD_SIZE
    )
    key_new = jnp.take(key_all, head_mapping, axis=1).astype(jnp.bfloat16)
    fresh_value = jnp.take(value_complete, head_mapping, axis=1).astype(jnp.bfloat16)
    slot_number = nearby_cache.shape[0]
    page_token_count = nearby_cache.shape[1]
    global_slot = shard_index * slot_number + jnp.arange(slot_number)
    matches = page_map[:, :, None] == global_slot[None, None, :]
    owner_mask = jnp.any(matches, axis=1)
    page_number = jnp.sum(
        jnp.where(matches, jnp.arange(page_map.shape[1])[None, :, None], 0), axis=(0, 1)
    )
    owner_req = jnp.sum(jnp.where(owner_mask, jnp.arange(request_number)[:, None], 0), axis=0)
    slot_live = jnp.any(owner_mask, axis=0)
    owner_length = jnp.take(lengths, owner_req)
    positions = page_number[:, None] * page_token_count + jnp.arange(page_token_count)[None, :]
    is_valid = slot_live[:, None] & (positions < owner_length[:, None])
    key_tile = nearby_cache[:, :, : KEY_VALUE_HEADS * HEAD_SIZE].reshape(
        slot_number, page_token_count, KEY_VALUE_HEADS, HEAD_SIZE
    )
    value_tile = nearby_cache[:, :, KEY_VALUE_HEADS * HEAD_SIZE :].reshape(
        slot_number, page_token_count, KEY_VALUE_HEADS, HEAD_SIZE
    )
    key_heads = jnp.take(key_tile, head_mapping, axis=2)
    value_heads = jnp.take(value_tile, head_mapping, axis=2)
    slot_query = jnp.take(query_rot, owner_req, axis=0)
    scores = (
        jnp.einsum("shd,skhd->shk", slot_query, key_heads, preferred_element_type=jnp.float32)
        * scale
    )
    scores = jnp.where(is_valid[:, None, :], scores, NEG_FILL)
    slot_max = jnp.max(scores, axis=2)
    request_max = jnp.max(jnp.where(owner_mask[:, :, None], slot_max[None, :, :], NEG_FILL), axis=1)
    owner_max = jnp.take(request_max, owner_req, axis=0)
    weights = jnp.where(is_valid[:, None, :], jnp.exp(scores - owner_max[:, :, None]), 0.0).astype(
        jnp.bfloat16
    )
    slot_total = jnp.sum(weights.astype(jnp.float32), axis=2)
    slot_weighted = jnp.einsum(
        "shk,skhd->shd", weights, value_heads, preferred_element_type=jnp.float32
    )
    owner_float = owner_mask.astype(jnp.float32)
    request_total = jnp.dot(owner_float, slot_total, precision=lax.Precision.HIGHEST)
    request_weighted = jnp.einsum(
        "rs,shd->rhd", owner_float, slot_weighted, precision=lax.Precision.HIGHEST
    )
    self_score = (
        jnp.sum(query_rot.astype(jnp.float32) * key_new.astype(jnp.float32), axis=2) * scale
    )
    unit_count = request_number * nearby_heads
    attended = merge_attention(
        request_max.reshape(unit_count),
        request_total.reshape(unit_count),
        request_weighted.reshape(unit_count, HEAD_SIZE),
        self_score.reshape(unit_count),
        fresh_value.astype(jnp.float32).reshape(unit_count, HEAD_SIZE),
        "seq",
    ).reshape(request_number, nearby_heads * HEAD_SIZE)
    output_part = jnp.dot(attended, output_weight, preferred_element_type=jnp.float32)
    output_sum = lax.psum(output_part, "tp")
    residual = token_rows + output_sum
    mean_square = jnp.mean(residual * residual, axis=-1, keepdims=True)
    row_scale = lax.rsqrt(mean_square + NORM_EPS)
    gain_part = lax.dynamic_slice_in_dim(final_gain, shard_index * part_width, part_width, 0)
    residual_part = lax.dynamic_slice_in_dim(residual, shard_index * part_width, part_width, 1)
    scaled_part = jnp.concatenate([residual_part, row_scale], axis=1)
    guide_index = lax.axis_index("guide")
    outgoing = lax.dynamic_slice_in_dim(scaled_part, (1 - guide_index) * half_rows, half_rows, 0)
    incoming = from_partner(outgoing, "guide", 0)
    own = lax.dynamic_slice_in_dim(scaled_part, guide_index * half_rows, half_rows, 0)
    paired = (incoming[:, :-1] * incoming[:, -1:] * gain_part).astype(jnp.bfloat16)
    own_rows = (own[:, :-1] * own[:, -1:] * gain_part).astype(jnp.bfloat16)
    conditional = jnp.where(guide_index == 0, own_rows, paired)
    unconditional = jnp.where(guide_index == 0, paired, own_rows)
    both = jnp.concatenate([conditional, unconditional], axis=0)
    logit_part = jnp.dot(both, head_weight, preferred_element_type=jnp.float32)
    conditional_part = logit_part[:half_rows]
    unconditional_part = logit_part[half_rows:]
    guided_part = unconditional_part + GUIDE_WEIGHT * (conditional_part - unconditional_part)
    return all_reduce(guided_part, "seq")


def solution(mesh):
    in_specs = (
        P("guide", None, None),
        P(),
        P(),
        P(),
        P(),
        P("seq", "tp"),
        P("seq", None),
        P("tp", None),
        P("seq", "tp"),
        P("guide", "seq", None, None),
        P("guide", None),
        P("guide", None, None),
    )
    out_specs = P("guide", "tp")
    return jax.shard_map(shards, mesh=mesh, in_specs=in_specs, out_specs=out_specs, check_vma=False)
```

```python
import jax
import jax.numpy as jnp
from jax import lax
from jax.sharding import PartitionSpec as P

QUERY_HEADS = 20
KEY_VALUE_HEADS = 5
HEAD_SIZE = 64


GUIDE_WEIGHT = 2.5
NORM_EPS = 1e-06
NEG_FILL = -1e30


def norm_rows(token_rows, scale_gain):
    mean_square = jnp.mean(token_rows * token_rows, axis=-1, keepdims=True)
    return (token_rows * lax.rsqrt(mean_square + NORM_EPS) * scale_gain).astype(jnp.bfloat16)


def per_head_norm(vectors, head_gain):
    mean_square = jnp.mean(vectors * vectors, axis=-1, keepdims=True)
    return vectors * lax.rsqrt(mean_square + NORM_EPS) * head_gain


def rotate(vectors, positions):
    half_dim = vectors.shape[-1] // 2
    frequency = 10000.0 ** (-jnp.arange(half_dim).astype(jnp.float32) / half_dim)
    angles = positions.astype(jnp.float32)[:, None] * frequency[None, :]
    cosine = jnp.cos(angles)[:, None, :]
    sine_part = jnp.sin(angles)[:, None, :]
    first_half = vectors[..., :half_dim]
    second_half = vectors[..., half_dim:]
    return jnp.concatenate(
        [
            first_half * cosine - second_half * sine_part,
            second_half * cosine + first_half * sine_part,
        ],
        axis=-1,
    )


def all_reduce(value, axis):
    count = lax.axis_size(axis)
    flat = value.reshape(-1)
    chunk = -(-flat.size // count)
    chunk = -(-chunk // 128) * 128
    flat = jnp.pad(flat, (0, count * chunk - flat.size))
    parts = lax.all_to_all(flat.reshape(count, chunk), axis, 0, 0, tiled=True)
    total = jnp.sum(parts, axis=0, keepdims=True)
    whole = lax.all_to_all(jnp.broadcast_to(total, (count, chunk)), axis, 0, 0, tiled=True)
    return whole.reshape(-1)[: value.size].reshape(value.shape)


def spread_units(units, count, fill):
    per = -(-units.shape[0] // count)
    padding = [(0, count * per - units.shape[0])] + [(0, 0)] * (units.ndim - 1)
    return jnp.pad(units, padding, constant_values=fill).reshape((count, per) + units.shape[1:])


def merge_attention(local_max, local_total, local_weighted, self_score, fresh_value, axis):
    count = lax.axis_size(axis)
    me = lax.axis_index(axis)
    unit_count = local_max.shape[0]
    stats = jnp.concatenate([local_max[:, None], local_total[:, None], local_weighted], axis=1)
    spread = spread_units(stats, count, 0.0)
    spread = spread.at[:, :, 0].set(spread_units(local_max, count, NEG_FILL))
    parts = lax.all_to_all(spread, axis, 0, 0, tiled=True)
    part_max = parts[:, :, 0]
    merged_max = jnp.max(part_max, axis=0)
    rescale = jnp.exp(part_max - merged_max[None, :])
    merged_total = jnp.sum(rescale * parts[:, :, 1], axis=0)
    merged_weighted = jnp.sum(rescale[:, :, None] * parts[:, :, 2:], axis=0)
    own_score = lax.dynamic_index_in_dim(spread_units(self_score, count, 0.0), me, 0, keepdims=False)
    own_value = lax.dynamic_index_in_dim(spread_units(fresh_value, count, 0.0), me, 0, keepdims=False)
    row_max = jnp.maximum(merged_max, own_score)
    old_scale = jnp.exp(merged_max - row_max)
    self_weight = jnp.exp(own_score - row_max)
    denominator = merged_total * old_scale + self_weight
    weighted = merged_weighted * old_scale[:, None] + self_weight[:, None] * own_value
    fraction = jnp.concatenate([weighted, denominator[:, None]], axis=1)
    gathered = lax.all_to_all(
        jnp.broadcast_to(fraction[None], (count,) + fraction.shape), axis, 0, 0, tiled=True
    ).reshape(-1, fraction.shape[-1])[:unit_count]
    return (gathered[:, :-1] / gathered[:, -1:]).astype(jnp.bfloat16)


def shards(
    hidden,
    attn_gain,
    final_gain,
    query_gain,
    new_key_gain,
    query_weight,
    key_value_weight,
    output_weight,
    head_weight,
    page_cache,
    cache_length,
    page_table,
):
    token_rows = hidden[0].astype(jnp.float32)
    lengths = cache_length[0]
    page_map = page_table[0]
    nearby_cache = page_cache[0]
    request_number = token_rows.shape[0]
    half_rows = request_number // 2
    part_width = query_weight.shape[0]
    nearby_heads = query_weight.shape[1] // HEAD_SIZE
    query_width = query_weight.shape[1]
    scale = 1.0 / HEAD_SIZE**0.5
    shard_index = lax.axis_index("seq")
    normed = norm_rows(token_rows, attn_gain)
    normed_part = lax.dynamic_slice_in_dim(normed, shard_index * part_width, part_width, 1)
    projected = all_reduce(
        jnp.concatenate(
            [
                jnp.dot(normed_part, query_weight, preferred_element_type=jnp.float32),
                jnp.dot(normed_part, key_value_weight, preferred_element_type=jnp.float32),
            ],
            axis=1,
        ),
        "seq",
    )
    query_sum = projected[:, :query_width]
    key_value_sum = projected[:, query_width:]
    head_mapping = (lax.axis_index("tp") * nearby_heads + jnp.arange(nearby_heads)) // (
        QUERY_HEADS // KEY_VALUE_HEADS
    )
    query_normed = per_head_norm(
        query_sum.reshape(request_number, nearby_heads, HEAD_SIZE), query_gain
    )
    normalized_key = per_head_norm(
        key_value_sum[:, : KEY_VALUE_HEADS * HEAD_SIZE].reshape(
            request_number, KEY_VALUE_HEADS, HEAD_SIZE
        ),
        new_key_gain,
    )
    query_rot = rotate(query_normed, lengths).astype(jnp.bfloat16)
    key_all = rotate(normalized_key, lengths)
    value_complete = key_value_sum[:, KEY_VALUE_HEADS * HEAD_SIZE :].reshape(
        request_number, KEY_VALUE_HEADS, HEAD_SIZE
    )
    key_new = jnp.take(key_all, head_mapping, axis=1).astype(jnp.bfloat16)
    fresh_value = jnp.take(value_complete, head_mapping, axis=1).astype(jnp.bfloat16)
    slot_number = nearby_cache.shape[0]
    page_token_count = nearby_cache.shape[1]
    global_slot = shard_index * slot_number + jnp.arange(slot_number)
    matches = page_map[:, :, None] == global_slot[None, None, :]
    owner_mask = jnp.any(matches, axis=1)
    page_number = jnp.sum(
        jnp.where(matches, jnp.arange(page_map.shape[1])[None, :, None], 0), axis=(0, 1)
    )
    owner_req = jnp.sum(jnp.where(owner_mask, jnp.arange(request_number)[:, None], 0), axis=0)
    slot_live = jnp.any(owner_mask, axis=0)
    owner_length = jnp.take(lengths, owner_req)
    positions = page_number[:, None] * page_token_count + jnp.arange(page_token_count)[None, :]
    is_valid = slot_live[:, None] & (positions < owner_length[:, None])
    key_tile = nearby_cache[:, :, : KEY_VALUE_HEADS * HEAD_SIZE].reshape(
        slot_number, page_token_count, KEY_VALUE_HEADS, HEAD_SIZE
    )
    value_tile = nearby_cache[:, :, KEY_VALUE_HEADS * HEAD_SIZE :].reshape(
        slot_number, page_token_count, KEY_VALUE_HEADS, HEAD_SIZE
    )
    key_heads = jnp.take(key_tile, head_mapping, axis=2)
    value_heads = jnp.take(value_tile, head_mapping, axis=2)
    slot_query = jnp.take(query_rot, owner_req, axis=0)
    scores = (
        jnp.einsum("shd,skhd->shk", slot_query, key_heads, preferred_element_type=jnp.float32)
        * scale
    )
    scores = jnp.where(is_valid[:, None, :], scores, NEG_FILL)
    slot_max = jnp.max(scores, axis=2)
    request_max = jnp.max(jnp.where(owner_mask[:, :, None], slot_max[None, :, :], NEG_FILL), axis=1)
    owner_max = jnp.take(request_max, owner_req, axis=0)
    weights = jnp.where(is_valid[:, None, :], jnp.exp(scores - owner_max[:, :, None]), 0.0).astype(
        jnp.bfloat16
    )
    slot_total = jnp.sum(weights.astype(jnp.float32), axis=2)
    slot_weighted = jnp.einsum(
        "shk,skhd->shd", weights, value_heads, preferred_element_type=jnp.float32
    )
    owner_float = owner_mask.astype(jnp.float32)
    request_total = jnp.dot(owner_float, slot_total, precision=lax.Precision.HIGHEST)
    request_weighted = jnp.einsum(
        "rs,shd->rhd", owner_float, slot_weighted, precision=lax.Precision.HIGHEST
    )
    self_score = (
        jnp.sum(query_rot.astype(jnp.float32) * key_new.astype(jnp.float32), axis=2) * scale
    )
    unit_count = request_number * nearby_heads
    attended = merge_attention(
        request_max.reshape(unit_count),
        request_total.reshape(unit_count),
        request_weighted.reshape(unit_count, HEAD_SIZE),
        self_score.reshape(unit_count),
        fresh_value.astype(jnp.float32).reshape(unit_count, HEAD_SIZE),
        "seq",
    ).reshape(request_number, nearby_heads * HEAD_SIZE)
    output_part = jnp.dot(attended, output_weight, preferred_element_type=jnp.float32)
    output_part = output_part + jnp.where(lax.axis_index("tp") == 0, token_rows, 0.0)
    guide_count = lax.axis_size("guide")
    tp_count = lax.axis_size("tp")
    outgoing = jnp.broadcast_to(
        output_part.reshape(guide_count, 1, half_rows, -1),
        (guide_count, tp_count, half_rows, output_part.shape[1]),
    ).reshape(guide_count * tp_count, half_rows, -1)
    incoming = lax.all_to_all(outgoing, ("guide", "tp"), 0, 0, tiled=True)
    residual = jnp.sum(incoming.reshape(guide_count, tp_count, half_rows, -1), axis=1)
    final_rows = norm_rows(residual, final_gain)
    final_part = lax.dynamic_slice_in_dim(final_rows, shard_index * part_width, part_width, 2)
    both = final_part.reshape(guide_count * half_rows, part_width)
    logit_part = jnp.dot(both, head_weight, preferred_element_type=jnp.float32)
    conditional_part = logit_part[:half_rows]
    unconditional_part = logit_part[half_rows:]
    guided_part = unconditional_part + GUIDE_WEIGHT * (conditional_part - unconditional_part)
    return all_reduce(guided_part, "seq")


def solution(mesh):
    in_specs = (
        P("guide", None, None),
        P(),
        P(),
        P(),
        P(),
        P("seq", "tp"),
        P("seq", None),
        P("tp", None),
        P("seq", "tp"),
        P("guide", "seq", None, None),
        P("guide", None),
        P("guide", None, None),
    )
    out_specs = P("guide", "tp")
    return jax.shard_map(shards, mesh=mesh, in_specs=in_specs, out_specs=out_specs, check_vma=False)
```

```python
import jax
import jax.numpy as jnp
from jax import lax
from jax.sharding import PartitionSpec as P

QUERY_HEADS = 20
KEY_VALUE_HEADS = 5
HEAD_SIZE = 64


GUIDE_WEIGHT = 2.5
NORM_EPS = 1e-06
NEG_FILL = -1e30


def norm_rows(token_rows, scale_gain):
    mean_square = jnp.mean(token_rows * token_rows, axis=-1, keepdims=True)
    return (token_rows * lax.rsqrt(mean_square + NORM_EPS) * scale_gain).astype(jnp.bfloat16)


def per_head_norm(vectors, head_gain):
    mean_square = jnp.mean(vectors * vectors, axis=-1, keepdims=True)
    return vectors * lax.rsqrt(mean_square + NORM_EPS) * head_gain


def rotate(vectors, positions):
    half_dim = vectors.shape[-1] // 2
    frequency = 10000.0 ** (-jnp.arange(half_dim).astype(jnp.float32) / half_dim)
    angles = positions.astype(jnp.float32)[:, None] * frequency[None, :]
    cosine = jnp.cos(angles)[:, None, :]
    sine_part = jnp.sin(angles)[:, None, :]
    first_half = vectors[..., :half_dim]
    second_half = vectors[..., half_dim:]
    return jnp.concatenate(
        [
            first_half * cosine - second_half * sine_part,
            second_half * cosine + first_half * sine_part,
        ],
        axis=-1,
    )


def all_reduce(value, axis):
    count = lax.axis_size(axis)
    flat = value.reshape(-1)
    chunk = -(-flat.size // count)
    chunk = -(-chunk // 128) * 128
    flat = jnp.pad(flat, (0, count * chunk - flat.size))
    parts = lax.all_to_all(flat.reshape(count, chunk), axis, 0, 0, tiled=True)
    total = jnp.sum(parts, axis=0, keepdims=True)
    whole = lax.all_to_all(jnp.broadcast_to(total, (count, chunk)), axis, 0, 0, tiled=True)
    return whole.reshape(-1)[: value.size].reshape(value.shape)


def spread_units(units, count, fill):
    per = -(-units.shape[0] // count)
    padding = [(0, count * per - units.shape[0])] + [(0, 0)] * (units.ndim - 1)
    return jnp.pad(units, padding, constant_values=fill).reshape((count, per) + units.shape[1:])


def merge_attention(local_max, local_total, local_weighted, self_score, fresh_value, axis):
    count = lax.axis_size(axis)
    me = lax.axis_index(axis)
    unit_count = local_max.shape[0]
    stats = jnp.concatenate([local_max[:, None], local_total[:, None], local_weighted], axis=1)
    spread = spread_units(stats, count, 0.0)
    spread = spread.at[:, :, 0].set(spread_units(local_max, count, NEG_FILL))
    parts = lax.all_to_all(spread, axis, 0, 0, tiled=True)
    part_max = parts[:, :, 0]
    merged_max = jnp.max(part_max, axis=0)
    rescale = jnp.exp(part_max - merged_max[None, :])
    merged_total = jnp.sum(rescale * parts[:, :, 1], axis=0)
    merged_weighted = jnp.sum(rescale[:, :, None] * parts[:, :, 2:], axis=0)
    own_score = lax.dynamic_index_in_dim(spread_units(self_score, count, 0.0), me, 0, keepdims=False)
    own_value = lax.dynamic_index_in_dim(spread_units(fresh_value, count, 0.0), me, 0, keepdims=False)
    row_max = jnp.maximum(merged_max, own_score)
    old_scale = jnp.exp(merged_max - row_max)
    self_weight = jnp.exp(own_score - row_max)
    denominator = merged_total * old_scale + self_weight
    weighted = merged_weighted * old_scale[:, None] + self_weight[:, None] * own_value
    fraction = jnp.concatenate([weighted, denominator[:, None]], axis=1)
    gathered = lax.all_to_all(
        jnp.broadcast_to(fraction[None], (count,) + fraction.shape), axis, 0, 0, tiled=True
    ).reshape(-1, fraction.shape[-1])[:unit_count]
    return (gathered[:, :-1] / gathered[:, -1:]).astype(jnp.bfloat16)


def shards(
    hidden,
    attn_gain,
    final_gain,
    query_gain,
    new_key_gain,
    query_weight,
    key_value_weight,
    output_weight,
    head_weight,
    page_cache,
    cache_length,
    page_table,
):
    token_rows = hidden[0].astype(jnp.float32)
    lengths = cache_length[0]
    page_map = page_table[0]
    nearby_cache = page_cache[0]
    request_number = token_rows.shape[0]
    half_rows = request_number // 2
    part_width = query_weight.shape[0]
    nearby_heads = query_weight.shape[1] // HEAD_SIZE
    query_width = query_weight.shape[1]
    scale = 1.0 / HEAD_SIZE**0.5
    shard_index = lax.axis_index("seq")
    normed = norm_rows(token_rows, attn_gain)
    normed_part = lax.dynamic_slice_in_dim(normed, shard_index * part_width, part_width, 1)
    projected = all_reduce(
        jnp.concatenate(
            [
                jnp.dot(normed_part, query_weight, preferred_element_type=jnp.float32),
                jnp.dot(normed_part, key_value_weight, preferred_element_type=jnp.float32),
            ],
            axis=1,
        ),
        "seq",
    )
    query_sum = projected[:, :query_width]
    key_value_sum = projected[:, query_width:]
    head_mapping = (lax.axis_index("tp") * nearby_heads + jnp.arange(nearby_heads)) // (
        QUERY_HEADS // KEY_VALUE_HEADS
    )
    query_normed = per_head_norm(
        query_sum.reshape(request_number, nearby_heads, HEAD_SIZE), query_gain
    )
    normalized_key = per_head_norm(
        key_value_sum[:, : KEY_VALUE_HEADS * HEAD_SIZE].reshape(
            request_number, KEY_VALUE_HEADS, HEAD_SIZE
        ),
        new_key_gain,
    )
    query_rot = rotate(query_normed, lengths).astype(jnp.bfloat16)
    key_all = rotate(normalized_key, lengths)
    value_complete = key_value_sum[:, KEY_VALUE_HEADS * HEAD_SIZE :].reshape(
        request_number, KEY_VALUE_HEADS, HEAD_SIZE
    )
    key_new = jnp.take(key_all, head_mapping, axis=1).astype(jnp.bfloat16)
    fresh_value = jnp.take(value_complete, head_mapping, axis=1).astype(jnp.bfloat16)
    slot_number = nearby_cache.shape[0]
    page_token_count = nearby_cache.shape[1]
    global_slot = shard_index * slot_number + jnp.arange(slot_number)
    matches = page_map[:, :, None] == global_slot[None, None, :]
    owner_mask = jnp.any(matches, axis=1)
    page_number = jnp.sum(
        jnp.where(matches, jnp.arange(page_map.shape[1])[None, :, None], 0), axis=(0, 1)
    )
    owner_req = jnp.sum(jnp.where(owner_mask, jnp.arange(request_number)[:, None], 0), axis=0)
    slot_live = jnp.any(owner_mask, axis=0)
    owner_length = jnp.take(lengths, owner_req)
    positions = page_number[:, None] * page_token_count + jnp.arange(page_token_count)[None, :]
    is_valid = slot_live[:, None] & (positions < owner_length[:, None])
    key_tile = nearby_cache[:, :, : KEY_VALUE_HEADS * HEAD_SIZE].reshape(
        slot_number, page_token_count, KEY_VALUE_HEADS, HEAD_SIZE
    )
    value_tile = nearby_cache[:, :, KEY_VALUE_HEADS * HEAD_SIZE :].reshape(
        slot_number, page_token_count, KEY_VALUE_HEADS, HEAD_SIZE
    )
    key_heads = jnp.take(key_tile, head_mapping, axis=2)
    value_heads = jnp.take(value_tile, head_mapping, axis=2)
    slot_query = jnp.take(query_rot, owner_req, axis=0)
    scores = (
        jnp.einsum("shd,skhd->shk", slot_query, key_heads, preferred_element_type=jnp.float32)
        * scale
    )
    scores = jnp.where(is_valid[:, None, :], scores, NEG_FILL)
    slot_max = jnp.max(scores, axis=2)
    request_max = jnp.max(jnp.where(owner_mask[:, :, None], slot_max[None, :, :], NEG_FILL), axis=1)
    owner_max = jnp.take(request_max, owner_req, axis=0)
    weights = jnp.where(is_valid[:, None, :], jnp.exp(scores - owner_max[:, :, None]), 0.0).astype(
        jnp.bfloat16
    )
    slot_total = jnp.sum(weights.astype(jnp.float32), axis=2)
    slot_weighted = jnp.einsum(
        "shk,skhd->shd", weights, value_heads, preferred_element_type=jnp.float32
    )
    owner_float = owner_mask.astype(jnp.float32)
    request_total = jnp.dot(owner_float, slot_total, precision=lax.Precision.HIGHEST)
    request_weighted = jnp.einsum(
        "rs,shd->rhd", owner_float, slot_weighted, precision=lax.Precision.HIGHEST
    )
    self_score = (
        jnp.sum(query_rot.astype(jnp.float32) * key_new.astype(jnp.float32), axis=2) * scale
    )
    unit_count = request_number * nearby_heads
    attended = merge_attention(
        request_max.reshape(unit_count),
        request_total.reshape(unit_count),
        request_weighted.reshape(unit_count, HEAD_SIZE),
        self_score.reshape(unit_count),
        fresh_value.astype(jnp.float32).reshape(unit_count, HEAD_SIZE),
        "seq",
    ).reshape(request_number, nearby_heads * HEAD_SIZE)
    output_part = jnp.dot(attended, output_weight, preferred_element_type=jnp.float32)
    output_part = output_part + jnp.where(lax.axis_index("tp") == 0, token_rows, 0.0)
    guide_count = lax.axis_size("guide")
    tp_count = lax.axis_size("tp")
    guide_index = lax.axis_index("guide")
    group_rows = []
    for guide_shift in range(guide_count):
        target_group = (guide_index + guide_shift) % guide_count
        outgoing = lax.dynamic_slice_in_dim(output_part, target_group * half_rows, half_rows, 0)
        total = outgoing if guide_shift == 0 else None
        for tp_shift in range(tp_count):
            if guide_shift == 0 and tp_shift == 0:
                continue
            pairs = [
                (
                    source_group * tp_count + source_tp,
                    ((source_group + guide_shift) % guide_count) * tp_count
                    + (source_tp + tp_shift) % tp_count,
                )
                for source_group in range(guide_count)
                for source_tp in range(tp_count)
            ]
            arrived = lax.ppermute(outgoing, ("guide", "tp"), pairs)
            total = arrived if total is None else total + arrived
        group_rows.append(total)
    own_group, other_group = group_rows
    residual = jnp.stack(
        [
            jnp.where(guide_index == 0, own_group, other_group),
            jnp.where(guide_index == 0, other_group, own_group),
        ]
    )
    final_rows = norm_rows(residual, final_gain)
    final_part = lax.dynamic_slice_in_dim(final_rows, shard_index * part_width, part_width, 2)
    both = final_part.reshape(guide_count * half_rows, part_width)
    logit_part = jnp.dot(both, head_weight, preferred_element_type=jnp.float32)
    conditional_part = logit_part[:half_rows]
    unconditional_part = logit_part[half_rows:]
    guided_part = unconditional_part + GUIDE_WEIGHT * (conditional_part - unconditional_part)
    return all_reduce(guided_part, "seq")


def solution(mesh):
    in_specs = (
        P("guide", None, None),
        P(),
        P(),
        P(),
        P(),
        P("seq", "tp"),
        P("seq", None),
        P("tp", None),
        P("seq", "tp"),
        P("guide", "seq", None, None),
        P("guide", None),
        P("guide", None, None),
    )
    out_specs = P("guide", "tp")
    return jax.shard_map(shards, mesh=mesh, in_specs=in_specs, out_specs=out_specs, check_vma=False)
```

```python
import jax
import jax.numpy as jnp
from jax import lax
from jax.sharding import PartitionSpec as P

QUERY_HEADS = 20
KEY_VALUE_HEADS = 5
HEAD_SIZE = 64


GUIDE_WEIGHT = 2.5
NORM_EPS = 1e-06
NEG_FILL = -1e30


def norm_rows(token_rows, scale_gain):
    mean_square = jnp.mean(token_rows * token_rows, axis=-1, keepdims=True)
    return (token_rows * lax.rsqrt(mean_square + NORM_EPS) * scale_gain).astype(jnp.bfloat16)


def per_head_norm(vectors, head_gain):
    mean_square = jnp.mean(vectors * vectors, axis=-1, keepdims=True)
    return vectors * lax.rsqrt(mean_square + NORM_EPS) * head_gain


def rotate(vectors, positions):
    half_dim = vectors.shape[-1] // 2
    frequency = 10000.0 ** (-jnp.arange(half_dim).astype(jnp.float32) / half_dim)
    angles = positions.astype(jnp.float32)[:, None] * frequency[None, :]
    cosine = jnp.cos(angles)[:, None, :]
    sine_part = jnp.sin(angles)[:, None, :]
    first_half = vectors[..., :half_dim]
    second_half = vectors[..., half_dim:]
    return jnp.concatenate(
        [
            first_half * cosine - second_half * sine_part,
            second_half * cosine + first_half * sine_part,
        ],
        axis=-1,
    )


def all_reduce(value, axis):
    count = lax.axis_size(axis)
    flat = value.reshape(-1)
    chunk = -(-flat.size // count)
    chunk = -(-chunk // 128) * 128
    flat = jnp.pad(flat, (0, count * chunk - flat.size))
    parts = lax.all_to_all(flat.reshape(count, chunk), axis, 0, 0, tiled=True)
    total = jnp.sum(parts, axis=0, keepdims=True)
    whole = lax.all_to_all(jnp.broadcast_to(total, (count, chunk)), axis, 0, 0, tiled=True)
    return whole.reshape(-1)[: value.size].reshape(value.shape)


def spread_units(units, count, fill):
    per = -(-units.shape[0] // count)
    padding = [(0, count * per - units.shape[0])] + [(0, 0)] * (units.ndim - 1)
    return jnp.pad(units, padding, constant_values=fill).reshape((count, per) + units.shape[1:])


def merge_attention(local_max, local_total, local_weighted, own_score, own_value, axis):
    count = lax.axis_size(axis)
    unit_count = local_max.shape[0]
    spread = jnp.concatenate(
        [
            spread_units(local_max[:, None], count, NEG_FILL),
            spread_units(jnp.concatenate([local_total[:, None], local_weighted], axis=1), count, 0.0),
        ],
        axis=2,
    )
    parts = lax.all_to_all(spread, axis, 0, 0, tiled=True)
    part_max = parts[:, :, 0]
    merged_max = jnp.max(part_max, axis=0)
    rescale = jnp.exp(part_max - merged_max[None, :])
    merged_total = jnp.sum(rescale * parts[:, :, 1], axis=0)
    merged_weighted = jnp.sum(rescale[:, :, None] * parts[:, :, 2:], axis=0)
    row_max = jnp.maximum(merged_max, own_score)
    old_scale = jnp.exp(merged_max - row_max)
    self_weight = jnp.exp(own_score - row_max)
    denominator = merged_total * old_scale + self_weight
    weighted = merged_weighted * old_scale[:, None] + self_weight[:, None] * own_value
    fraction = jnp.concatenate([weighted, denominator[:, None]], axis=1)
    gathered = lax.all_to_all(
        jnp.broadcast_to(fraction[None], (count,) + fraction.shape), axis, 0, 0, tiled=True
    ).reshape(-1, fraction.shape[-1])[:unit_count]
    return (gathered[:, :-1] / gathered[:, -1:]).astype(jnp.bfloat16)


def shards(
    hidden,
    attn_gain,
    final_gain,
    query_gain,
    new_key_gain,
    query_weight,
    key_value_weight,
    output_weight,
    head_weight,
    page_cache,
    cache_length,
    page_table,
):
    token_rows = hidden[0].astype(jnp.float32)
    lengths = cache_length[0]
    page_map = page_table[0]
    nearby_cache = page_cache[0]
    request_number = token_rows.shape[0]
    half_rows = request_number // 2
    part_width = query_weight.shape[0]
    nearby_heads = query_weight.shape[1] // HEAD_SIZE
    query_width = query_weight.shape[1]
    scale = 1.0 / HEAD_SIZE**0.5
    shard_index = lax.axis_index("seq")
    normed = norm_rows(token_rows, attn_gain)
    normed_part = lax.dynamic_slice_in_dim(normed, shard_index * part_width, part_width, 1)
    seq_count = lax.axis_size("seq")
    group_width = QUERY_HEADS // KEY_VALUE_HEADS
    unit_count = request_number * nearby_heads
    unit_per = -(-unit_count // seq_count)
    unit_index = jnp.minimum(jnp.arange(seq_count * unit_per), unit_count - 1)
    unit_request = unit_index // nearby_heads
    unit_kv_head = (lax.axis_index("tp") * nearby_heads + unit_index % nearby_heads) // group_width
    query_part = jnp.dot(normed_part, query_weight, preferred_element_type=jnp.float32)
    key_value_part = jnp.dot(normed_part, key_value_weight, preferred_element_type=jnp.float32)
    unit_key_value = key_value_part.reshape(request_number, 2, KEY_VALUE_HEADS, HEAD_SIZE)[
        unit_request, :, unit_kv_head, :
    ]
    outgoing = jnp.concatenate(
        [
            query_part.reshape(seq_count, -1),
            unit_key_value.reshape(seq_count, unit_per * 2 * HEAD_SIZE),
        ],
        axis=1,
    )
    summed = jnp.sum(lax.all_to_all(outgoing, "seq", 0, 0, tiled=True), axis=0)
    query_chunk = summed[: query_width * request_number // seq_count]
    own_key_value = summed[query_chunk.shape[0] :].reshape(unit_per, 2, HEAD_SIZE)
    query_sum = lax.all_to_all(
        jnp.broadcast_to(query_chunk[None], (seq_count,) + query_chunk.shape), "seq", 0, 0, tiled=True
    ).reshape(request_number, query_width)
    query_normed = per_head_norm(
        query_sum.reshape(request_number, nearby_heads, HEAD_SIZE), query_gain
    )
    query_rot = rotate(query_normed, lengths).astype(jnp.bfloat16)
    own_unit = lax.dynamic_slice_in_dim(unit_index, shard_index * unit_per, unit_per, 0)
    own_positions = jnp.take(lengths, own_unit // nearby_heads)
    own_key = rotate(per_head_norm(own_key_value[:, None, 0], new_key_gain), own_positions)
    own_key = own_key[:, 0].astype(jnp.bfloat16).astype(jnp.float32)
    own_value = own_key_value[:, 1].astype(jnp.bfloat16).astype(jnp.float32)
    own_query = query_rot.reshape(unit_count, HEAD_SIZE)[own_unit].astype(jnp.float32)
    own_score = jnp.sum(own_query * own_key, axis=1) * scale
    head_mapping = (lax.axis_index("tp") * nearby_heads + jnp.arange(nearby_heads)) // group_width
    slot_number = nearby_cache.shape[0]
    page_token_count = nearby_cache.shape[1]
    global_slot = shard_index * slot_number + jnp.arange(slot_number)
    matches = page_map[:, :, None] == global_slot[None, None, :]
    owner_mask = jnp.any(matches, axis=1)
    page_number = jnp.sum(
        jnp.where(matches, jnp.arange(page_map.shape[1])[None, :, None], 0), axis=(0, 1)
    )
    owner_req = jnp.sum(jnp.where(owner_mask, jnp.arange(request_number)[:, None], 0), axis=0)
    slot_live = jnp.any(owner_mask, axis=0)
    owner_length = jnp.take(lengths, owner_req)
    positions = page_number[:, None] * page_token_count + jnp.arange(page_token_count)[None, :]
    is_valid = slot_live[:, None] & (positions < owner_length[:, None])
    key_tile = nearby_cache[:, :, : KEY_VALUE_HEADS * HEAD_SIZE].reshape(
        slot_number, page_token_count, KEY_VALUE_HEADS, HEAD_SIZE
    )
    value_tile = nearby_cache[:, :, KEY_VALUE_HEADS * HEAD_SIZE :].reshape(
        slot_number, page_token_count, KEY_VALUE_HEADS, HEAD_SIZE
    )
    key_heads = jnp.take(key_tile, head_mapping, axis=2)
    value_heads = jnp.take(value_tile, head_mapping, axis=2)
    slot_query = jnp.take(query_rot, owner_req, axis=0)
    scores = (
        jnp.einsum("shd,skhd->shk", slot_query, key_heads, preferred_element_type=jnp.float32)
        * scale
    )
    scores = jnp.where(is_valid[:, None, :], scores, NEG_FILL)
    slot_max = jnp.max(scores, axis=2)
    request_max = jnp.max(jnp.where(owner_mask[:, :, None], slot_max[None, :, :], NEG_FILL), axis=1)
    owner_max = jnp.take(request_max, owner_req, axis=0)
    weights = jnp.where(is_valid[:, None, :], jnp.exp(scores - owner_max[:, :, None]), 0.0).astype(
        jnp.bfloat16
    )
    slot_total = jnp.sum(weights.astype(jnp.float32), axis=2)
    slot_weighted = jnp.einsum(
        "shk,skhd->shd", weights, value_heads, preferred_element_type=jnp.float32
    )
    owner_float = owner_mask.astype(jnp.float32)
    request_total = jnp.dot(owner_float, slot_total, precision=lax.Precision.HIGHEST)
    request_weighted = jnp.einsum(
        "rs,shd->rhd", owner_float, slot_weighted, precision=lax.Precision.HIGHEST
    )
    attended = merge_attention(
        request_max.reshape(unit_count),
        request_total.reshape(unit_count),
        request_weighted.reshape(unit_count, HEAD_SIZE),
        own_score,
        own_value,
        "seq",
    ).reshape(request_number, nearby_heads * HEAD_SIZE)
    output_part = jnp.dot(attended, output_weight, preferred_element_type=jnp.float32)
    output_part = output_part + jnp.where(lax.axis_index("tp") == 0, token_rows, 0.0)
    guide_count = lax.axis_size("guide")
    tp_count = lax.axis_size("tp")
    outgoing = jnp.broadcast_to(
        output_part.reshape(guide_count, 1, half_rows, -1),
        (guide_count, tp_count, half_rows, output_part.shape[1]),
    ).reshape(guide_count * tp_count, half_rows, -1)
    incoming = lax.all_to_all(outgoing, ("guide", "tp"), 0, 0, tiled=True)
    residual = jnp.sum(incoming.reshape(guide_count, tp_count, half_rows, -1), axis=1)
    final_rows = norm_rows(residual, final_gain)
    final_part = lax.dynamic_slice_in_dim(final_rows, shard_index * part_width, part_width, 2)
    both = final_part.reshape(guide_count * half_rows, part_width)
    logit_part = jnp.dot(both, head_weight, preferred_element_type=jnp.float32)
    conditional_part = logit_part[:half_rows]
    unconditional_part = logit_part[half_rows:]
    guided_part = unconditional_part + GUIDE_WEIGHT * (conditional_part - unconditional_part)
    return all_reduce(guided_part, "seq")


def solution(mesh):
    in_specs = (
        P("guide", None, None),
        P(),
        P(),
        P(),
        P(),
        P("seq", "tp"),
        P("seq", None),
        P("tp", None),
        P("seq", "tp"),
        P("guide", "seq", None, None),
        P("guide", None),
        P("guide", None, None),
    )
    out_specs = P("guide", "tp")
    return jax.shard_map(shards, mesh=mesh, in_specs=in_specs, out_specs=out_specs, check_vma=False)
```

```python
import jax
import jax.numpy as jnp
from jax import lax
from jax.sharding import PartitionSpec as P

QUERY_HEADS = 20
KEY_VALUE_HEADS = 5
HEAD_SIZE = 64


GUIDE_WEIGHT = 2.5
NORM_EPS = 1e-06
NEG_FILL = -1e30


def norm_rows(token_rows, scale_gain):
    mean_square = jnp.mean(token_rows * token_rows, axis=-1, keepdims=True)
    return (token_rows * lax.rsqrt(mean_square + NORM_EPS) * scale_gain).astype(jnp.bfloat16)


def per_head_norm(vectors, head_gain):
    mean_square = jnp.mean(vectors * vectors, axis=-1, keepdims=True)
    return vectors * lax.rsqrt(mean_square + NORM_EPS) * head_gain


def rotate(vectors, positions):
    half_dim = vectors.shape[-1] // 2
    frequency = 10000.0 ** (-jnp.arange(half_dim).astype(jnp.float32) / half_dim)
    angles = positions.astype(jnp.float32)[:, None] * frequency[None, :]
    cosine = jnp.cos(angles)[:, None, :]
    sine_part = jnp.sin(angles)[:, None, :]
    first_half = vectors[..., :half_dim]
    second_half = vectors[..., half_dim:]
    return jnp.concatenate(
        [
            first_half * cosine - second_half * sine_part,
            second_half * cosine + first_half * sine_part,
        ],
        axis=-1,
    )


def all_reduce(value, axis):
    count = lax.axis_size(axis)
    flat = value.reshape(-1)
    chunk = -(-flat.size // count)
    chunk = -(-chunk // 128) * 128
    flat = jnp.pad(flat, (0, count * chunk - flat.size))
    parts = lax.all_to_all(flat.reshape(count, chunk), axis, 0, 0, tiled=True)
    total = jnp.sum(parts, axis=0, keepdims=True)
    whole = lax.all_to_all(jnp.broadcast_to(total, (count, chunk)), axis, 0, 0, tiled=True)
    return whole.reshape(-1)[: value.size].reshape(value.shape)


def spread_units(units, count, fill):
    rows, heads = units.shape[:2]
    slots = -(-heads * rows // count) * count // rows
    padding = [(0, 0), (0, slots - heads)] + [(0, 0)] * (units.ndim - 2)
    padded = jnp.pad(units, padding, constant_values=fill)
    return padded.reshape((count, rows * slots // count) + units.shape[2:])


def merge_attention(local_max, local_total, local_weighted, own_score, own_value, axis):
    count = lax.axis_size(axis)
    rows, heads = local_max.shape
    spread = jnp.concatenate(
        [
            spread_units(local_max[:, :, None], count, NEG_FILL),
            spread_units(jnp.concatenate([local_total[:, :, None], local_weighted], axis=2), count, 0.0),
        ],
        axis=2,
    )
    parts = lax.all_to_all(spread, axis, 0, 0, tiled=True)
    part_max = parts[:, :, 0]
    merged_max = jnp.max(part_max, axis=0)
    rescale = jnp.exp(part_max - merged_max[None, :])
    merged_total = jnp.sum(rescale * parts[:, :, 1], axis=0)
    merged_weighted = jnp.sum(rescale[:, :, None] * parts[:, :, 2:], axis=0)
    row_max = jnp.maximum(merged_max, own_score)
    old_scale = jnp.exp(merged_max - row_max)
    self_weight = jnp.exp(own_score - row_max)
    denominator = merged_total * old_scale + self_weight
    weighted = merged_weighted * old_scale[:, None] + self_weight[:, None] * own_value
    fraction = jnp.concatenate([weighted, denominator[:, None]], axis=1)
    gathered = lax.all_to_all(
        jnp.broadcast_to(fraction[None], (count,) + fraction.shape), axis, 0, 0, tiled=True
    ).reshape(rows, -1, fraction.shape[-1])[:, :heads]
    return (gathered[:, :, :-1] / gathered[:, :, -1:]).astype(jnp.bfloat16)


def shards(
    hidden,
    attn_gain,
    final_gain,
    query_gain,
    new_key_gain,
    query_weight,
    key_value_weight,
    output_weight,
    head_weight,
    page_cache,
    cache_length,
    page_table,
):
    token_rows = hidden[0].astype(jnp.float32)
    lengths = cache_length[0]
    page_map = page_table[0]
    nearby_cache = page_cache[0]
    request_number = token_rows.shape[0]
    half_rows = request_number // 2
    part_width = query_weight.shape[0]
    nearby_heads = query_weight.shape[1] // HEAD_SIZE
    query_width = query_weight.shape[1]
    scale = 1.0 / HEAD_SIZE**0.5
    shard_index = lax.axis_index("seq")
    normed = norm_rows(token_rows, attn_gain)
    normed_part = lax.dynamic_slice_in_dim(normed, shard_index * part_width, part_width, 1)
    seq_count = lax.axis_size("seq")
    group_width = QUERY_HEADS // KEY_VALUE_HEADS
    unit_count = request_number * nearby_heads
    slots_per_request = -(-nearby_heads * request_number // seq_count) * seq_count // request_number
    unit_per = request_number * slots_per_request // seq_count
    head_mapping = (lax.axis_index("tp") * nearby_heads + jnp.arange(nearby_heads)) // group_width
    key_weight = key_value_weight[:, : KEY_VALUE_HEADS * HEAD_SIZE].reshape(
        part_width, KEY_VALUE_HEADS, HEAD_SIZE
    )
    value_weight = key_value_weight[:, KEY_VALUE_HEADS * HEAD_SIZE :].reshape(
        part_width, KEY_VALUE_HEADS, HEAD_SIZE
    )
    unit_weight = jnp.stack(
        [
            query_weight.reshape(part_width, nearby_heads, HEAD_SIZE),
            jnp.take(key_weight, head_mapping, axis=1),
            jnp.take(value_weight, head_mapping, axis=1),
        ],
        axis=2,
    )
    unit_weight = jnp.pad(
        unit_weight, ((0, 0), (0, slots_per_request - nearby_heads), (0, 0), (0, 0))
    ).reshape(part_width, -1)
    unit_part = jnp.dot(normed_part, unit_weight, preferred_element_type=jnp.float32)
    summed = jnp.sum(
        lax.all_to_all(unit_part.reshape(seq_count, -1), "seq", 0, 0, tiled=True), axis=0
    ).reshape(unit_per, 3, HEAD_SIZE)
    query_sum = lax.all_to_all(
        jnp.broadcast_to(summed[None, :, 0], (seq_count, unit_per, HEAD_SIZE)), "seq", 0, 0, tiled=True
    ).reshape(request_number, slots_per_request, HEAD_SIZE)[:, :nearby_heads]
    query_normed = per_head_norm(query_sum, query_gain)
    query_rot = rotate(query_normed, lengths).astype(jnp.bfloat16)
    own_position = jnp.take(lengths, shard_index * unit_per // slots_per_request)[None]
    own_query = rotate(per_head_norm(summed[None, :, 0], query_gain), own_position)[0]
    own_query = own_query.astype(jnp.bfloat16).astype(jnp.float32)
    own_key = rotate(per_head_norm(summed[None, :, 1], new_key_gain), own_position)[0]
    own_key = own_key.astype(jnp.bfloat16).astype(jnp.float32)
    own_value = summed[:, 2].astype(jnp.bfloat16).astype(jnp.float32)
    own_score = jnp.sum(own_query * own_key, axis=1) * scale
    slot_number = nearby_cache.shape[0]
    page_token_count = nearby_cache.shape[1]
    global_slot = shard_index * slot_number + jnp.arange(slot_number)
    matches = page_map[:, :, None] == global_slot[None, None, :]
    owner_mask = jnp.any(matches, axis=1)
    page_number = jnp.sum(
        jnp.where(matches, jnp.arange(page_map.shape[1])[None, :, None], 0), axis=(0, 1)
    )
    owner_req = jnp.sum(jnp.where(owner_mask, jnp.arange(request_number)[:, None], 0), axis=0)
    slot_live = jnp.any(owner_mask, axis=0)
    owner_length = jnp.take(lengths, owner_req)
    positions = page_number[:, None] * page_token_count + jnp.arange(page_token_count)[None, :]
    is_valid = slot_live[:, None] & (positions < owner_length[:, None])
    key_tile = nearby_cache[:, :, : KEY_VALUE_HEADS * HEAD_SIZE].reshape(
        slot_number, page_token_count, KEY_VALUE_HEADS, HEAD_SIZE
    )
    value_tile = nearby_cache[:, :, KEY_VALUE_HEADS * HEAD_SIZE :].reshape(
        slot_number, page_token_count, KEY_VALUE_HEADS, HEAD_SIZE
    )
    key_heads = jnp.take(key_tile, head_mapping, axis=2)
    value_heads = jnp.take(value_tile, head_mapping, axis=2)
    slot_query = jnp.take(query_rot, owner_req, axis=0)
    scores = (
        jnp.einsum("shd,skhd->shk", slot_query, key_heads, preferred_element_type=jnp.float32)
        * scale
    )
    scores = jnp.where(is_valid[:, None, :], scores, NEG_FILL)
    slot_max = jnp.max(scores, axis=2)
    request_max = jnp.max(jnp.where(owner_mask[:, :, None], slot_max[None, :, :], NEG_FILL), axis=1)
    owner_max = jnp.take(request_max, owner_req, axis=0)
    weights = jnp.where(is_valid[:, None, :], jnp.exp(scores - owner_max[:, :, None]), 0.0).astype(
        jnp.bfloat16
    )
    slot_total = jnp.sum(weights.astype(jnp.float32), axis=2)
    slot_weighted = jnp.einsum(
        "shk,skhd->shd", weights, value_heads, preferred_element_type=jnp.float32
    )
    owner_float = owner_mask.astype(jnp.float32)
    request_total = jnp.dot(owner_float, slot_total, precision=lax.Precision.HIGHEST)
    request_weighted = jnp.einsum(
        "rs,shd->rhd", owner_float, slot_weighted, precision=lax.Precision.HIGHEST
    )
    attended = merge_attention(
        request_max,
        request_total,
        request_weighted,
        own_score,
        own_value,
        "seq",
    ).reshape(request_number, nearby_heads * HEAD_SIZE)
    output_part = jnp.dot(attended, output_weight, preferred_element_type=jnp.float32)
    output_part = output_part + jnp.where(lax.axis_index("tp") == 0, token_rows, 0.0)
    guide_count = lax.axis_size("guide")
    tp_count = lax.axis_size("tp")
    outgoing = jnp.broadcast_to(
        output_part.reshape(guide_count, 1, half_rows, -1),
        (guide_count, tp_count, half_rows, output_part.shape[1]),
    ).reshape(guide_count * tp_count, half_rows, -1)
    incoming = lax.all_to_all(outgoing, ("guide", "tp"), 0, 0, tiled=True)
    residual = jnp.sum(incoming.reshape(guide_count, tp_count, half_rows, -1), axis=1)
    final_rows = norm_rows(residual, final_gain)
    final_part = lax.dynamic_slice_in_dim(final_rows, shard_index * part_width, part_width, 2)
    both = final_part.reshape(guide_count * half_rows, part_width)
    logit_part = jnp.dot(both, head_weight, preferred_element_type=jnp.float32)
    conditional_part = logit_part[:half_rows]
    unconditional_part = logit_part[half_rows:]
    guided_part = unconditional_part + GUIDE_WEIGHT * (conditional_part - unconditional_part)
    return all_reduce(guided_part, "seq")


def solution(mesh):
    in_specs = (
        P("guide", None, None),
        P(),
        P(),
        P(),
        P(),
        P("seq", "tp"),
        P("seq", None),
        P("tp", None),
        P("seq", "tp"),
        P("guide", "seq", None, None),
        P("guide", None),
        P("guide", None, None),
    )
    out_specs = P("guide", "tp")
    return jax.shard_map(shards, mesh=mesh, in_specs=in_specs, out_specs=out_specs, check_vma=False)
```

```python
import jax
import jax.numpy as jnp
from jax import lax
from jax.sharding import PartitionSpec as P

QUERY_HEADS = 20
KEY_VALUE_HEADS = 5
HEAD_SIZE = 64


GUIDE_WEIGHT = 2.5
NORM_EPS = 1e-06
NEG_FILL = -1e30


def norm_rows(token_rows, scale_gain):
    mean_square = jnp.mean(token_rows * token_rows, axis=-1, keepdims=True)
    return (token_rows * lax.rsqrt(mean_square + NORM_EPS) * scale_gain).astype(jnp.bfloat16)


def per_head_norm(vectors, head_gain):
    mean_square = jnp.mean(vectors * vectors, axis=-1, keepdims=True)
    return vectors * lax.rsqrt(mean_square + NORM_EPS) * head_gain


def rotate(vectors, positions):
    half_dim = vectors.shape[-1] // 2
    frequency = 10000.0 ** (-jnp.arange(half_dim).astype(jnp.float32) / half_dim)
    angles = positions.astype(jnp.float32)[:, None] * frequency[None, :]
    cosine = jnp.cos(angles)[:, None, :]
    sine_part = jnp.sin(angles)[:, None, :]
    first_half = vectors[..., :half_dim]
    second_half = vectors[..., half_dim:]
    return jnp.concatenate(
        [
            first_half * cosine - second_half * sine_part,
            second_half * cosine + first_half * sine_part,
        ],
        axis=-1,
    )


def all_reduce(value, axis):
    count = lax.axis_size(axis)
    flat = value.reshape(-1)
    chunk = -(-flat.size // count)
    chunk = -(-chunk // 128) * 128
    flat = jnp.pad(flat, (0, count * chunk - flat.size))
    parts = lax.all_to_all(flat.reshape(count, chunk), axis, 0, 0, tiled=True)
    total = jnp.sum(parts, axis=0, keepdims=True)
    whole = lax.all_to_all(jnp.broadcast_to(total, (count, chunk)), axis, 0, 0, tiled=True)
    return whole.reshape(-1)[: value.size].reshape(value.shape)


def all_reduce_columns(value, axis):
    count = lax.axis_size(axis)
    rows, columns = value.shape
    if columns % count:
        return all_reduce(value, axis)
    parts = lax.all_to_all(value, axis, 1, 0, tiled=True)
    total = jnp.sum(parts.reshape(count, rows, columns // count), axis=0)
    whole = lax.all_to_all(
        jnp.broadcast_to(total[None], (count, rows, columns // count)), axis, 0, 2, tiled=True
    )
    return whole[0]


def spread_units(units, count, fill):
    per = -(-units.shape[0] // count)
    padding = [(0, count * per - units.shape[0])] + [(0, 0)] * (units.ndim - 1)
    return jnp.pad(units, padding, constant_values=fill).reshape((count, per) + units.shape[1:])


def merge_attention(local_max, local_total, local_weighted, own_score, own_value, axis):
    count = lax.axis_size(axis)
    unit_count = local_max.shape[0]
    spread = jnp.concatenate(
        [
            spread_units(local_max[:, None], count, NEG_FILL),
            spread_units(jnp.concatenate([local_total[:, None], local_weighted], axis=1), count, 0.0),
        ],
        axis=2,
    )
    parts = lax.all_to_all(spread, axis, 0, 0, tiled=True)
    part_max = parts[:, :, 0]
    merged_max = jnp.max(part_max, axis=0)
    rescale = jnp.exp(part_max - merged_max[None, :])
    merged_total = jnp.sum(rescale * parts[:, :, 1], axis=0)
    merged_weighted = jnp.sum(rescale[:, :, None] * parts[:, :, 2:], axis=0)
    row_max = jnp.maximum(merged_max, own_score)
    old_scale = jnp.exp(merged_max - row_max)
    self_weight = jnp.exp(own_score - row_max)
    denominator = merged_total * old_scale + self_weight
    weighted = merged_weighted * old_scale[:, None] + self_weight[:, None] * own_value
    fraction = jnp.concatenate([weighted, denominator[:, None]], axis=1)
    gathered = lax.all_to_all(
        jnp.broadcast_to(fraction.reshape(1, -1), (count, fraction.size)), axis, 0, 0, tiled=True
    ).reshape(-1, fraction.shape[-1])[:unit_count]
    return (gathered[:, :-1] / gathered[:, -1:]).astype(jnp.bfloat16)


def shards(
    hidden,
    attn_gain,
    final_gain,
    query_gain,
    new_key_gain,
    query_weight,
    key_value_weight,
    output_weight,
    head_weight,
    page_cache,
    cache_length,
    page_table,
):
    token_rows = hidden[0].astype(jnp.float32)
    lengths = cache_length[0]
    page_map = page_table[0]
    nearby_cache = page_cache[0]
    request_number = token_rows.shape[0]
    half_rows = request_number // 2
    part_width = query_weight.shape[0]
    nearby_heads = query_weight.shape[1] // HEAD_SIZE
    query_width = query_weight.shape[1]
    scale = 1.0 / HEAD_SIZE**0.5
    shard_index = lax.axis_index("seq")
    normed = norm_rows(token_rows, attn_gain)
    normed_part = lax.dynamic_slice_in_dim(normed, shard_index * part_width, part_width, 1)
    seq_count = lax.axis_size("seq")
    group_width = QUERY_HEADS // KEY_VALUE_HEADS
    unit_count = request_number * nearby_heads
    unit_per = -(-unit_count // seq_count)
    unit_index = jnp.minimum(jnp.arange(seq_count * unit_per), unit_count - 1)
    unit_request = unit_index // nearby_heads
    unit_kv_head = (lax.axis_index("tp") * nearby_heads + unit_index % nearby_heads) // group_width
    query_part = jnp.dot(normed_part, query_weight, preferred_element_type=jnp.float32)
    key_value_part = jnp.dot(normed_part, key_value_weight, preferred_element_type=jnp.float32)
    unit_key_value = key_value_part.reshape(request_number, 2, KEY_VALUE_HEADS, HEAD_SIZE)[
        unit_request, :, unit_kv_head, :
    ]
    outgoing = jnp.concatenate(
        [
            query_part.reshape(seq_count, -1),
            unit_key_value.reshape(seq_count, unit_per * 2 * HEAD_SIZE),
        ],
        axis=1,
    )
    summed = jnp.sum(lax.all_to_all(outgoing, "seq", 0, 0, tiled=True), axis=0)
    query_chunk = summed[: query_width * request_number // seq_count]
    own_key_value = summed[query_chunk.shape[0] :].reshape(unit_per, 2, HEAD_SIZE)
    query_sum = lax.all_to_all(
        jnp.broadcast_to(query_chunk[None], (seq_count,) + query_chunk.shape), "seq", 0, 0, tiled=True
    ).reshape(request_number, query_width)
    query_normed = per_head_norm(
        query_sum.reshape(request_number, nearby_heads, HEAD_SIZE), query_gain
    )
    query_rot = rotate(query_normed, lengths).astype(jnp.bfloat16)
    own_unit = lax.dynamic_slice_in_dim(unit_index, shard_index * unit_per, unit_per, 0)
    own_positions = jnp.take(lengths, own_unit // nearby_heads)
    own_key = rotate(per_head_norm(own_key_value[:, None, 0], new_key_gain), own_positions)
    own_key = own_key[:, 0].astype(jnp.bfloat16).astype(jnp.float32)
    own_value = own_key_value[:, 1].astype(jnp.bfloat16).astype(jnp.float32)
    own_query = query_rot.reshape(unit_count, HEAD_SIZE)[own_unit].astype(jnp.float32)
    own_score = jnp.sum(own_query * own_key, axis=1) * scale
    head_mapping = (lax.axis_index("tp") * nearby_heads + jnp.arange(nearby_heads)) // group_width
    slot_number = nearby_cache.shape[0]
    page_token_count = nearby_cache.shape[1]
    global_slot = shard_index * slot_number + jnp.arange(slot_number)
    matches = page_map[:, :, None] == global_slot[None, None, :]
    owner_mask = jnp.any(matches, axis=1)
    page_number = jnp.sum(
        jnp.where(matches, jnp.arange(page_map.shape[1])[None, :, None], 0), axis=(0, 1)
    )
    owner_req = jnp.sum(jnp.where(owner_mask, jnp.arange(request_number)[:, None], 0), axis=0)
    slot_live = jnp.any(owner_mask, axis=0)
    owner_length = jnp.take(lengths, owner_req)
    positions = page_number[:, None] * page_token_count + jnp.arange(page_token_count)[None, :]
    is_valid = slot_live[:, None] & (positions < owner_length[:, None])
    key_tile = nearby_cache[:, :, : KEY_VALUE_HEADS * HEAD_SIZE].reshape(
        slot_number, page_token_count, KEY_VALUE_HEADS, HEAD_SIZE
    )
    value_tile = nearby_cache[:, :, KEY_VALUE_HEADS * HEAD_SIZE :].reshape(
        slot_number, page_token_count, KEY_VALUE_HEADS, HEAD_SIZE
    )
    key_heads = jnp.take(key_tile, head_mapping, axis=2)
    value_heads = jnp.take(value_tile, head_mapping, axis=2)
    slot_query = jnp.take(query_rot, owner_req, axis=0)
    scores = (
        jnp.einsum("shd,skhd->shk", slot_query, key_heads, preferred_element_type=jnp.float32)
        * scale
    )
    scores = jnp.where(is_valid[:, None, :], scores, NEG_FILL)
    slot_max = jnp.max(scores, axis=2)
    request_max = jnp.max(jnp.where(owner_mask[:, :, None], slot_max[None, :, :], NEG_FILL), axis=1)
    owner_max = jnp.take(request_max, owner_req, axis=0)
    weights = jnp.where(is_valid[:, None, :], jnp.exp(scores - owner_max[:, :, None]), 0.0).astype(
        jnp.bfloat16
    )
    slot_total = jnp.sum(weights.astype(jnp.float32), axis=2)
    slot_weighted = jnp.einsum(
        "shk,skhd->shd", weights, value_heads, preferred_element_type=jnp.float32
    )
    owner_float = owner_mask.astype(jnp.float32)
    request_total = jnp.dot(owner_float, slot_total, precision=lax.Precision.HIGHEST)
    request_weighted = jnp.einsum(
        "rs,shd->rhd", owner_float, slot_weighted, precision=lax.Precision.HIGHEST
    )
    attended = merge_attention(
        request_max.reshape(unit_count),
        request_total.reshape(unit_count),
        request_weighted.reshape(unit_count, HEAD_SIZE),
        own_score,
        own_value,
        "seq",
    ).reshape(request_number, nearby_heads * HEAD_SIZE)
    output_part = jnp.dot(attended, output_weight, preferred_element_type=jnp.float32)
    output_part = output_part + jnp.where(lax.axis_index("tp") == 0, token_rows, 0.0)
    guide_count = lax.axis_size("guide")
    tp_count = lax.axis_size("tp")
    outgoing = jnp.broadcast_to(
        output_part.reshape(guide_count, 1, half_rows, -1),
        (guide_count, tp_count, half_rows, output_part.shape[1]),
    ).reshape(guide_count * tp_count, half_rows, -1)
    incoming = lax.all_to_all(outgoing, ("guide", "tp"), 0, 0, tiled=True)
    residual = jnp.sum(incoming.reshape(guide_count, tp_count, half_rows, -1), axis=1)
    final_rows = norm_rows(residual, final_gain)
    final_part = lax.dynamic_slice_in_dim(final_rows, shard_index * part_width, part_width, 2)
    both = final_part.reshape(guide_count * half_rows, part_width)
    logit_part = jnp.dot(both, head_weight, preferred_element_type=jnp.float32)
    conditional_part = logit_part[:half_rows]
    unconditional_part = logit_part[half_rows:]
    guided_part = unconditional_part + GUIDE_WEIGHT * (conditional_part - unconditional_part)
    return all_reduce_columns(guided_part, "seq")


def solution(mesh):
    in_specs = (
        P("guide", None, None),
        P(),
        P(),
        P(),
        P(),
        P("seq", "tp"),
        P("seq", None),
        P("tp", None),
        P("seq", "tp"),
        P("guide", "seq", None, None),
        P("guide", None),
        P("guide", None, None),
    )
    out_specs = P("guide", "tp")
    return jax.shard_map(shards, mesh=mesh, in_specs=in_specs, out_specs=out_specs, check_vma=False)
```

```python
import functools

import jax
import jax.numpy as jnp
from jax import lax
from jax.experimental import pallas as pl
from jax.sharding import PartitionSpec as P

QUERY_HEADS = 20
KEY_VALUE_HEADS = 5
HEAD_SIZE = 64


GUIDE_WEIGHT = 2.5
NORM_EPS = 1e-06
NEG_FILL = -1e30


def page_attention_kernel(scale, q_ref, owner_t_ref, owner_ref, valid_ref, k_ref, v_ref, out_ref):
    heads = q_ref.shape[0]
    slots = owner_t_ref.shape[0]
    owner_t = owner_t_ref[...] > 0.5
    owner = owner_ref[...] > 0.5
    valid = valid_ref[...] > 0.5
    owner_t_bf = owner_t_ref[...].astype(jnp.bfloat16)
    eye = lax.broadcasted_iota(jnp.int32, (slots, slots), 0) == lax.broadcasted_iota(jnp.int32, (slots, slots), 1)
    for h in range(heads):
        slot_query = jnp.dot(owner_t_bf, q_ref[h], preferred_element_type=jnp.float32).astype(jnp.bfloat16)
        scores = lax.dot_general(slot_query, k_ref[h], (((1,), (1,)), ((), ())), preferred_element_type=jnp.float32) * scale
        scores = jnp.where(valid, scores, NEG_FILL)
        slot_max = jnp.max(scores, axis=1, keepdims=True)
        request_max_row = jnp.max(jnp.where(owner_t, slot_max, NEG_FILL), axis=0, keepdims=True)
        owner_max = jnp.max(jnp.where(owner_t, request_max_row, NEG_FILL), axis=1, keepdims=True)
        weights = jnp.where(valid, jnp.exp(scores - owner_max), 0.0).astype(jnp.bfloat16)
        slot_total = jnp.sum(weights.astype(jnp.float32), axis=1, keepdims=True)
        slot_weighted = jnp.dot(weights, v_ref[h], preferred_element_type=jnp.float32)
        slot_max_row = jnp.max(jnp.where(eye, slot_max, NEG_FILL), axis=0, keepdims=True)
        slot_total_row = jnp.sum(jnp.where(eye, slot_total, 0.0), axis=0, keepdims=True)
        request_max = jnp.max(jnp.where(owner, slot_max_row, NEG_FILL), axis=1, keepdims=True)
        request_total = jnp.sum(jnp.where(owner, slot_total_row, 0.0), axis=1, keepdims=True)
        request_weighted = jnp.dot(owner_ref[...], slot_weighted, precision=lax.Precision.HIGHEST, preferred_element_type=jnp.float32)
        lane = lax.broadcasted_iota(jnp.int32, request_weighted.shape, 1)
        out_ref[h, :, : request_weighted.shape[1]] = request_weighted
        out_ref[h, :, request_weighted.shape[1]:] = jnp.where(lane == 0, request_total, jnp.where(lane == 1, request_max, 0.0))

def page_attention(query_heads, owner_t, owner, valid, key_heads, value_heads, scale):
    heads, requests, size = query_heads.shape
    return pl.pallas_call(
        functools.partial(page_attention_kernel, scale),
        out_shape=jax.ShapeDtypeStruct((heads, requests, 2 * size), jnp.float32),
    )(query_heads, owner_t, owner, valid, key_heads, value_heads)


def norm_rows(token_rows, scale_gain):
    mean_square = jnp.mean(token_rows * token_rows, axis=-1, keepdims=True)
    return (token_rows * lax.rsqrt(mean_square + NORM_EPS) * scale_gain).astype(jnp.bfloat16)


def per_head_norm(vectors, head_gain):
    mean_square = jnp.mean(vectors * vectors, axis=-1, keepdims=True)
    return vectors * lax.rsqrt(mean_square + NORM_EPS) * head_gain


def rotate(vectors, positions):
    half_dim = vectors.shape[-1] // 2
    frequency = 10000.0 ** (-jnp.arange(half_dim).astype(jnp.float32) / half_dim)
    angles = positions.astype(jnp.float32)[:, None] * frequency[None, :]
    cosine = jnp.cos(angles)[:, None, :]
    sine_part = jnp.sin(angles)[:, None, :]
    first_half = vectors[..., :half_dim]
    second_half = vectors[..., half_dim:]
    return jnp.concatenate(
        [
            first_half * cosine - second_half * sine_part,
            second_half * cosine + first_half * sine_part,
        ],
        axis=-1,
    )


def all_reduce(value, axis):
    count = lax.axis_size(axis)
    flat = value.reshape(-1)
    chunk = -(-flat.size // count)
    chunk = -(-chunk // 128) * 128
    flat = jnp.pad(flat, (0, count * chunk - flat.size))
    parts = lax.all_to_all(flat.reshape(count, chunk), axis, 0, 0, tiled=True)
    total = jnp.sum(parts, axis=0, keepdims=True)
    whole = lax.all_to_all(jnp.broadcast_to(total, (count, chunk)), axis, 0, 0, tiled=True)
    return whole.reshape(-1)[: value.size].reshape(value.shape)


def all_reduce_columns(value, axis):
    count = lax.axis_size(axis)
    rows, columns = value.shape
    if columns % count:
        return all_reduce(value, axis)
    parts = lax.all_to_all(value, axis, 1, 0, tiled=True)
    total = jnp.sum(parts.reshape(count, rows, columns // count), axis=0)
    whole = lax.all_to_all(
        jnp.broadcast_to(total[None], (count, rows, columns // count)), axis, 0, 2, tiled=True
    )
    return whole[0]


def spread_units(units, count, fill):
    per = -(-units.shape[0] // count)
    padding = [(0, count * per - units.shape[0])] + [(0, 0)] * (units.ndim - 1)
    return jnp.pad(units, padding, constant_values=fill).reshape((count, per) + units.shape[1:])


def merge_attention(local_max, local_total, local_weighted, own_score, own_value, axis):
    count = lax.axis_size(axis)
    unit_count = local_max.shape[0]
    spread = jnp.concatenate(
        [
            spread_units(local_max[:, None], count, NEG_FILL),
            spread_units(jnp.concatenate([local_total[:, None], local_weighted], axis=1), count, 0.0),
        ],
        axis=2,
    )
    parts = lax.all_to_all(spread, axis, 0, 0, tiled=True)
    part_max = parts[:, :, 0]
    merged_max = jnp.max(part_max, axis=0)
    rescale = jnp.exp(part_max - merged_max[None, :])
    merged_total = jnp.sum(rescale * parts[:, :, 1], axis=0)
    merged_weighted = jnp.sum(rescale[:, :, None] * parts[:, :, 2:], axis=0)
    row_max = jnp.maximum(merged_max, own_score)
    old_scale = jnp.exp(merged_max - row_max)
    self_weight = jnp.exp(own_score - row_max)
    denominator = merged_total * old_scale + self_weight
    weighted = merged_weighted * old_scale[:, None] + self_weight[:, None] * own_value
    fraction = jnp.concatenate([weighted, denominator[:, None]], axis=1)
    gathered = lax.all_to_all(
        jnp.broadcast_to(fraction.reshape(1, -1), (count, fraction.size)), axis, 0, 0, tiled=True
    ).reshape(-1, fraction.shape[-1])[:unit_count]
    return (gathered[:, :-1] / gathered[:, -1:]).astype(jnp.bfloat16)


def shards(
    hidden,
    attn_gain,
    final_gain,
    query_gain,
    new_key_gain,
    query_weight,
    key_value_weight,
    output_weight,
    head_weight,
    page_cache,
    cache_length,
    page_table,
):
    token_rows = hidden[0].astype(jnp.float32)
    lengths = cache_length[0]
    page_map = page_table[0]
    nearby_cache = page_cache[0]
    request_number = token_rows.shape[0]
    half_rows = request_number // 2
    part_width = query_weight.shape[0]
    nearby_heads = query_weight.shape[1] // HEAD_SIZE
    query_width = query_weight.shape[1]
    scale = 1.0 / HEAD_SIZE**0.5
    shard_index = lax.axis_index("seq")
    normed = norm_rows(token_rows, attn_gain)
    normed_part = lax.dynamic_slice_in_dim(normed, shard_index * part_width, part_width, 1)
    seq_count = lax.axis_size("seq")
    group_width = QUERY_HEADS // KEY_VALUE_HEADS
    unit_count = request_number * nearby_heads
    unit_per = -(-unit_count // seq_count)
    unit_index = jnp.minimum(jnp.arange(seq_count * unit_per), unit_count - 1)
    unit_request = unit_index // nearby_heads
    unit_kv_head = (lax.axis_index("tp") * nearby_heads + unit_index % nearby_heads) // group_width
    query_part = jnp.dot(normed_part, query_weight, preferred_element_type=jnp.float32)
    key_value_part = jnp.dot(normed_part, key_value_weight, preferred_element_type=jnp.float32)
    unit_key_value = key_value_part.reshape(request_number, 2, KEY_VALUE_HEADS, HEAD_SIZE)[
        unit_request, :, unit_kv_head, :
    ]
    outgoing = jnp.concatenate(
        [
            query_part.reshape(seq_count, -1),
            unit_key_value.reshape(seq_count, unit_per * 2 * HEAD_SIZE),
        ],
        axis=1,
    )
    summed = jnp.sum(lax.all_to_all(outgoing, "seq", 0, 0, tiled=True), axis=0)
    query_chunk = summed[: query_width * request_number // seq_count]
    own_key_value = summed[query_chunk.shape[0] :].reshape(unit_per, 2, HEAD_SIZE)
    query_sum = lax.all_to_all(
        jnp.broadcast_to(query_chunk[None], (seq_count,) + query_chunk.shape), "seq", 0, 0, tiled=True
    ).reshape(request_number, query_width)
    query_normed = per_head_norm(
        query_sum.reshape(request_number, nearby_heads, HEAD_SIZE), query_gain
    )
    query_rot = rotate(query_normed, lengths).astype(jnp.bfloat16)
    own_unit = lax.dynamic_slice_in_dim(unit_index, shard_index * unit_per, unit_per, 0)
    own_positions = jnp.take(lengths, own_unit // nearby_heads)
    own_key = rotate(per_head_norm(own_key_value[:, None, 0], new_key_gain), own_positions)
    own_key = own_key[:, 0].astype(jnp.bfloat16).astype(jnp.float32)
    own_value = own_key_value[:, 1].astype(jnp.bfloat16).astype(jnp.float32)
    own_query = query_rot.reshape(unit_count, HEAD_SIZE)[own_unit].astype(jnp.float32)
    own_score = jnp.sum(own_query * own_key, axis=1) * scale
    head_mapping = (lax.axis_index("tp") * nearby_heads + jnp.arange(nearby_heads)) // group_width
    slot_number = nearby_cache.shape[0]
    page_token_count = nearby_cache.shape[1]
    global_slot = shard_index * slot_number + jnp.arange(slot_number)
    matches = page_map[:, :, None] == global_slot[None, None, :]
    owner_mask = jnp.any(matches, axis=1)
    page_number = jnp.sum(
        jnp.where(matches, jnp.arange(page_map.shape[1])[None, :, None], 0), axis=(0, 1)
    )
    owner_req = jnp.sum(jnp.where(owner_mask, jnp.arange(request_number)[:, None], 0), axis=0)
    slot_live = jnp.any(owner_mask, axis=0)
    owner_length = jnp.take(lengths, owner_req)
    positions = page_number[:, None] * page_token_count + jnp.arange(page_token_count)[None, :]
    is_valid = slot_live[:, None] & (positions < owner_length[:, None])
    key_tile = nearby_cache[:, :, : KEY_VALUE_HEADS * HEAD_SIZE].reshape(
        slot_number, page_token_count, KEY_VALUE_HEADS, HEAD_SIZE
    )
    value_tile = nearby_cache[:, :, KEY_VALUE_HEADS * HEAD_SIZE :].reshape(
        slot_number, page_token_count, KEY_VALUE_HEADS, HEAD_SIZE
    )
    key_heads = jnp.take(key_tile, head_mapping, axis=2)
    value_heads = jnp.take(value_tile, head_mapping, axis=2)
    padded_slots = -(-slot_number // 8) * 8
    owner = jnp.pad(owner_mask.astype(jnp.float32), ((0, 0), (0, padded_slots - slot_number)))
    block_valid = (
        (jnp.arange(padded_slots)[:, None, None] == jnp.arange(slot_number)[None, :, None])
        & is_valid[None]
    ).reshape(padded_slots, slot_number * page_token_count)
    request_stats = page_attention(
        jnp.transpose(query_rot, (1, 0, 2)),
        owner.T,
        owner,
        block_valid.astype(jnp.float32),
        jnp.transpose(key_heads, (2, 0, 1, 3)).reshape(nearby_heads, -1, HEAD_SIZE),
        jnp.transpose(value_heads, (2, 0, 1, 3)).reshape(nearby_heads, -1, HEAD_SIZE),
        scale,
    )
    request_stats = jnp.transpose(request_stats, (1, 0, 2))
    request_weighted = request_stats[:, :, :HEAD_SIZE]
    request_total = request_stats[:, :, HEAD_SIZE]
    request_max = request_stats[:, :, HEAD_SIZE + 1]
    attended = merge_attention(
        request_max.reshape(unit_count),
        request_total.reshape(unit_count),
        request_weighted.reshape(unit_count, HEAD_SIZE),
        own_score,
        own_value,
        "seq",
    ).reshape(request_number, nearby_heads * HEAD_SIZE)
    output_part = jnp.dot(attended, output_weight, preferred_element_type=jnp.float32)
    output_part = output_part + jnp.where(lax.axis_index("tp") == 0, token_rows, 0.0)
    guide_count = lax.axis_size("guide")
    tp_count = lax.axis_size("tp")
    outgoing = jnp.broadcast_to(
        output_part.reshape(guide_count, 1, half_rows, -1),
        (guide_count, tp_count, half_rows, output_part.shape[1]),
    ).reshape(guide_count * tp_count, half_rows, -1)
    incoming = lax.all_to_all(outgoing, ("guide", "tp"), 0, 0, tiled=True)
    residual = jnp.sum(incoming.reshape(guide_count, tp_count, half_rows, -1), axis=1)
    final_rows = norm_rows(residual, final_gain)
    final_part = lax.dynamic_slice_in_dim(final_rows, shard_index * part_width, part_width, 2)
    both = final_part.reshape(guide_count * half_rows, part_width)
    logit_part = jnp.dot(both, head_weight, preferred_element_type=jnp.float32)
    conditional_part = logit_part[:half_rows]
    unconditional_part = logit_part[half_rows:]
    guided_part = unconditional_part + GUIDE_WEIGHT * (conditional_part - unconditional_part)
    return all_reduce_columns(guided_part, "seq")


def solution(mesh):
    in_specs = (
        P("guide", None, None),
        P(),
        P(),
        P(),
        P(),
        P("seq", "tp"),
        P("seq", None),
        P("tp", None),
        P("seq", "tp"),
        P("guide", "seq", None, None),
        P("guide", None),
        P("guide", None, None),
    )
    out_specs = P("guide", "tp")
    return jax.shard_map(shards, mesh=mesh, in_specs=in_specs, out_specs=out_specs, check_vma=False)
```

```python
import jax
import jax.numpy as jnp
from jax import lax
from jax.sharding import PartitionSpec as P

QUERY_HEADS = 20
KEY_VALUE_HEADS = 5
HEAD_SIZE = 64


GUIDE_WEIGHT = 2.5
NORM_EPS = 1e-06
NEG_FILL = -1e30


def norm_rows(token_rows, scale_gain):
    mean_square = jnp.mean(token_rows * token_rows, axis=-1, keepdims=True)
    return (token_rows * lax.rsqrt(mean_square + NORM_EPS) * scale_gain).astype(jnp.bfloat16)


def per_head_norm(vectors, head_gain):
    mean_square = jnp.mean(vectors * vectors, axis=-1, keepdims=True)
    return vectors * lax.rsqrt(mean_square + NORM_EPS) * head_gain


def rotate(vectors, positions):
    half_dim = vectors.shape[-1] // 2
    frequency = 10000.0 ** (-jnp.arange(half_dim).astype(jnp.float32) / half_dim)
    angles = positions.astype(jnp.float32)[:, None] * frequency[None, :]
    cosine = jnp.cos(angles)[:, None, :]
    sine_part = jnp.sin(angles)[:, None, :]
    first_half = vectors[..., :half_dim]
    second_half = vectors[..., half_dim:]
    return jnp.concatenate(
        [
            first_half * cosine - second_half * sine_part,
            second_half * cosine + first_half * sine_part,
        ],
        axis=-1,
    )


def all_reduce(value, axis):
    count = lax.axis_size(axis)
    flat = value.reshape(-1)
    chunk = -(-flat.size // count)
    chunk = -(-chunk // 128) * 128
    flat = jnp.pad(flat, (0, count * chunk - flat.size))
    parts = lax.all_to_all(flat.reshape(count, chunk), axis, 0, 0, tiled=True)
    total = jnp.sum(parts, axis=0, keepdims=True)
    whole = lax.all_to_all(jnp.broadcast_to(total, (count, chunk)), axis, 0, 0, tiled=True)
    return whole.reshape(-1)[: value.size].reshape(value.shape)


def all_reduce_columns(value, axis):
    count = lax.axis_size(axis)
    rows, columns = value.shape
    if columns % count:
        return all_reduce(value, axis)
    parts = lax.all_to_all(value, axis, 1, 0, tiled=True)
    total = jnp.sum(parts.reshape(count, rows, columns // count), axis=0)
    whole = lax.all_to_all(
        jnp.broadcast_to(total[None], (count, rows, columns // count)), axis, 0, 2, tiled=True
    )
    return whole[0]


def spread_units(units, count, fill):
    per = -(-units.shape[0] // count)
    padding = [(0, count * per - units.shape[0])] + [(0, 0)] * (units.ndim - 1)
    return jnp.pad(units, padding, constant_values=fill).reshape((count, per) + units.shape[1:])


def merge_attention(local_max, local_total, local_weighted, own_score, own_value, axis):
    count = lax.axis_size(axis)
    unit_count = local_max.shape[0]
    spread = jnp.concatenate(
        [
            spread_units(local_max[:, None], count, NEG_FILL),
            spread_units(jnp.concatenate([local_total[:, None], local_weighted], axis=1), count, 0.0),
        ],
        axis=2,
    )
    parts = lax.all_to_all(spread, axis, 0, 0, tiled=True)
    part_max = parts[:, :, 0]
    merged_max = jnp.max(part_max, axis=0)
    rescale = jnp.exp(part_max - merged_max[None, :])
    merged_total = jnp.sum(rescale * parts[:, :, 1], axis=0)
    merged_weighted = jnp.sum(rescale[:, :, None] * parts[:, :, 2:], axis=0)
    row_max = jnp.maximum(merged_max, own_score)
    old_scale = jnp.exp(merged_max - row_max)
    self_weight = jnp.exp(own_score - row_max)
    denominator = merged_total * old_scale + self_weight
    weighted = merged_weighted * old_scale[:, None] + self_weight[:, None] * own_value
    fraction = jnp.concatenate([weighted, denominator[:, None]], axis=1)
    gathered = lax.all_to_all(
        jnp.broadcast_to(fraction.reshape(1, -1), (count, fraction.size)), axis, 0, 0, tiled=True
    ).reshape(-1, fraction.shape[-1])[:unit_count]
    return (gathered[:, :-1] / gathered[:, -1:]).astype(jnp.bfloat16)


def shards(
    hidden,
    attn_gain,
    final_gain,
    query_gain,
    new_key_gain,
    query_weight,
    key_value_weight,
    output_weight,
    head_weight,
    page_cache,
    cache_length,
    page_table,
):
    token_rows = hidden[0].astype(jnp.float32)
    lengths = cache_length[0]
    page_map = page_table[0]
    nearby_cache = page_cache[0]
    request_number = token_rows.shape[0]
    half_rows = request_number // 2
    part_width = query_weight.shape[0]
    nearby_heads = query_weight.shape[1] // HEAD_SIZE
    query_width = query_weight.shape[1]
    scale = 1.0 / HEAD_SIZE**0.5
    shard_index = lax.axis_index("seq")
    normed = norm_rows(token_rows, attn_gain)
    normed_part = lax.dynamic_slice_in_dim(normed, shard_index * part_width, part_width, 1)
    seq_count = lax.axis_size("seq")
    group_width = QUERY_HEADS // KEY_VALUE_HEADS
    unit_count = request_number * nearby_heads
    unit_per = -(-unit_count // seq_count)
    unit_index = jnp.minimum(jnp.arange(seq_count * unit_per), unit_count - 1)
    unit_request = unit_index // nearby_heads
    unit_kv_head = (lax.axis_index("tp") * nearby_heads + unit_index % nearby_heads) // group_width
    query_part = jnp.dot(normed_part, query_weight, preferred_element_type=jnp.float32)
    key_value_part = jnp.dot(normed_part, key_value_weight, preferred_element_type=jnp.float32)
    unit_key_value = key_value_part.reshape(request_number, 2, KEY_VALUE_HEADS, HEAD_SIZE)[
        unit_request, :, unit_kv_head, :
    ]
    outgoing = jnp.concatenate(
        [
            query_part.reshape(seq_count, -1),
            unit_key_value.reshape(seq_count, unit_per * 2 * HEAD_SIZE),
        ],
        axis=1,
    )
    summed = jnp.sum(lax.all_to_all(outgoing, "seq", 0, 0, tiled=True), axis=0)
    query_chunk = summed[: query_width * request_number // seq_count]
    own_key_value = summed[query_chunk.shape[0] :].reshape(unit_per, 2, HEAD_SIZE)
    query_sum = lax.all_to_all(
        jnp.broadcast_to(query_chunk[None], (seq_count,) + query_chunk.shape), "seq", 0, 0, tiled=True
    ).reshape(request_number, query_width)
    query_normed = per_head_norm(
        query_sum.reshape(request_number, nearby_heads, HEAD_SIZE), query_gain
    )
    query_rot = rotate(query_normed, lengths).astype(jnp.bfloat16)
    own_unit = lax.dynamic_slice_in_dim(unit_index, shard_index * unit_per, unit_per, 0)
    own_positions = jnp.take(lengths, own_unit // nearby_heads)
    own_key = rotate(per_head_norm(own_key_value[:, None, 0], new_key_gain), own_positions)
    own_key = own_key[:, 0].astype(jnp.bfloat16).astype(jnp.float32)
    own_value = own_key_value[:, 1].astype(jnp.bfloat16).astype(jnp.float32)
    own_query = query_rot.reshape(unit_count, HEAD_SIZE)[own_unit].astype(jnp.float32)
    own_score = jnp.sum(own_query * own_key, axis=1) * scale
    head_mapping = (lax.axis_index("tp") * nearby_heads + jnp.arange(nearby_heads)) // group_width
    slot_number = nearby_cache.shape[0]
    page_token_count = nearby_cache.shape[1]
    global_slot = shard_index * slot_number + jnp.arange(slot_number)
    matches = page_map[:, :, None] == global_slot[None, None, :]
    owner_mask = jnp.any(matches, axis=1)
    page_number = jnp.sum(
        jnp.where(matches, jnp.arange(page_map.shape[1])[None, :, None], 0), axis=(0, 1)
    )
    owner_req = jnp.sum(jnp.where(owner_mask, jnp.arange(request_number)[:, None], 0), axis=0)
    slot_live = jnp.any(owner_mask, axis=0)
    owner_length = jnp.take(lengths, owner_req)
    positions = page_number[:, None] * page_token_count + jnp.arange(page_token_count)[None, :]
    is_valid = slot_live[:, None] & (positions < owner_length[:, None])
    first_kv = jnp.minimum(head_mapping[0], KEY_VALUE_HEADS - 2)
    second = (head_mapping - first_kv)[None, None, :, None] == 1
    key_pair = lax.dynamic_slice_in_dim(nearby_cache, first_kv * HEAD_SIZE, 2 * HEAD_SIZE, 2)
    value_pair = lax.dynamic_slice_in_dim(
        nearby_cache, (KEY_VALUE_HEADS + first_kv) * HEAD_SIZE, 2 * HEAD_SIZE, 2
    )
    key_heads = jnp.where(second, key_pair[:, :, None, HEAD_SIZE:], key_pair[:, :, None, :HEAD_SIZE])
    value_heads = jnp.where(
        second, value_pair[:, :, None, HEAD_SIZE:], value_pair[:, :, None, :HEAD_SIZE]
    )
    slot_query = jnp.take(query_rot, owner_req, axis=0)
    scores = (
        jnp.einsum("shd,skhd->shk", slot_query, key_heads, preferred_element_type=jnp.float32)
        * scale
    )
    scores = jnp.where(is_valid[:, None, :], scores, NEG_FILL)
    slot_max = jnp.max(scores, axis=2)
    request_max = jnp.max(jnp.where(owner_mask[:, :, None], slot_max[None, :, :], NEG_FILL), axis=1)
    owner_max = jnp.take(request_max, owner_req, axis=0)
    weights = jnp.where(is_valid[:, None, :], jnp.exp(scores - owner_max[:, :, None]), 0.0).astype(
        jnp.bfloat16
    )
    slot_total = jnp.sum(weights.astype(jnp.float32), axis=2)
    slot_weighted = jnp.einsum(
        "shk,skhd->shd", weights, value_heads, preferred_element_type=jnp.float32
    )
    owner_float = owner_mask.astype(jnp.float32)
    request_total = jnp.dot(owner_float, slot_total, precision=lax.Precision.HIGHEST)
    request_weighted = jnp.einsum(
        "rs,shd->rhd", owner_float, slot_weighted, precision=lax.Precision.HIGHEST
    )
    attended = merge_attention(
        request_max.reshape(unit_count),
        request_total.reshape(unit_count),
        request_weighted.reshape(unit_count, HEAD_SIZE),
        own_score,
        own_value,
        "seq",
    ).reshape(request_number, nearby_heads * HEAD_SIZE)
    output_part = jnp.dot(attended, output_weight, preferred_element_type=jnp.float32)
    output_part = output_part + jnp.where(lax.axis_index("tp") == 0, token_rows, 0.0)
    guide_count = lax.axis_size("guide")
    tp_count = lax.axis_size("tp")
    outgoing = jnp.broadcast_to(
        output_part.reshape(guide_count, 1, half_rows, -1),
        (guide_count, tp_count, half_rows, output_part.shape[1]),
    ).reshape(guide_count * tp_count, half_rows, -1)
    incoming = lax.all_to_all(outgoing, ("guide", "tp"), 0, 0, tiled=True)
    residual = jnp.sum(incoming.reshape(guide_count, tp_count, half_rows, -1), axis=1)
    final_rows = norm_rows(residual, final_gain)
    final_part = lax.dynamic_slice_in_dim(final_rows, shard_index * part_width, part_width, 2)
    both = final_part.reshape(guide_count * half_rows, part_width)
    logit_part = jnp.dot(both, head_weight, preferred_element_type=jnp.float32)
    conditional_part = logit_part[:half_rows]
    unconditional_part = logit_part[half_rows:]
    guided_part = unconditional_part + GUIDE_WEIGHT * (conditional_part - unconditional_part)
    return all_reduce_columns(guided_part, "seq")


def solution(mesh):
    in_specs = (
        P("guide", None, None),
        P(),
        P(),
        P(),
        P(),
        P("seq", "tp"),
        P("seq", None),
        P("tp", None),
        P("seq", "tp"),
        P("guide", "seq", None, None),
        P("guide", None),
        P("guide", None, None),
    )
    out_specs = P("guide", "tp")
    return jax.shard_map(shards, mesh=mesh, in_specs=in_specs, out_specs=out_specs, check_vma=False)
```

```python
import jax
import jax.numpy as jnp
from jax import lax
from jax.experimental import pallas as pl
from jax.sharding import PartitionSpec as P

QUERY_HEADS = 20
KEY_VALUE_HEADS = 5
HEAD_SIZE = 64


GUIDE_WEIGHT = 2.5
NORM_EPS = 1e-06
NEG_FILL = -1e30


def project_kernel(rows_ref, weight_ref, out_ref):
    out_ref[...] = jnp.dot(rows_ref[...], weight_ref[...], preferred_element_type=jnp.float32)


def project(rows, weight, block=512):
    count, depth = rows.shape
    width = weight.shape[1]
    return pl.pallas_call(
        project_kernel,
        grid=(width // block,),
        in_specs=[
            pl.BlockSpec((count, depth), lambda j: (0, 0)),
            pl.BlockSpec((depth, block), lambda j: (0, j)),
        ],
        out_specs=pl.BlockSpec((count, block), lambda j: (0, j)),
        out_shape=jax.ShapeDtypeStruct((count, width), jnp.float32),
    )(rows, weight)


def norm_rows(token_rows, scale_gain):
    mean_square = jnp.mean(token_rows * token_rows, axis=-1, keepdims=True)
    return (token_rows * lax.rsqrt(mean_square + NORM_EPS) * scale_gain).astype(jnp.bfloat16)


def per_head_norm(vectors, head_gain):
    mean_square = jnp.mean(vectors * vectors, axis=-1, keepdims=True)
    return vectors * lax.rsqrt(mean_square + NORM_EPS) * head_gain


def rotate(vectors, positions):
    half_dim = vectors.shape[-1] // 2
    frequency = 10000.0 ** (-jnp.arange(half_dim).astype(jnp.float32) / half_dim)
    angles = positions.astype(jnp.float32)[:, None] * frequency[None, :]
    cosine = jnp.cos(angles)[:, None, :]
    sine_part = jnp.sin(angles)[:, None, :]
    first_half = vectors[..., :half_dim]
    second_half = vectors[..., half_dim:]
    return jnp.concatenate(
        [
            first_half * cosine - second_half * sine_part,
            second_half * cosine + first_half * sine_part,
        ],
        axis=-1,
    )


def all_reduce(value, axis):
    count = lax.axis_size(axis)
    flat = value.reshape(-1)
    chunk = -(-flat.size // count)
    chunk = -(-chunk // 128) * 128
    flat = jnp.pad(flat, (0, count * chunk - flat.size))
    parts = lax.all_to_all(flat.reshape(count, chunk), axis, 0, 0, tiled=True)
    total = jnp.sum(parts, axis=0, keepdims=True)
    whole = lax.all_to_all(jnp.broadcast_to(total, (count, chunk)), axis, 0, 0, tiled=True)
    return whole.reshape(-1)[: value.size].reshape(value.shape)


def all_reduce_columns(value, axis):
    count = lax.axis_size(axis)
    rows, columns = value.shape
    if columns % count:
        return all_reduce(value, axis)
    parts = lax.all_to_all(value, axis, 1, 0, tiled=True)
    total = jnp.sum(parts.reshape(count, rows, columns // count), axis=0)
    whole = lax.all_to_all(
        jnp.broadcast_to(total[None], (count, rows, columns // count)), axis, 0, 2, tiled=True
    )
    return whole[0]


def spread_units(units, count, fill):
    per = -(-units.shape[0] // count)
    padding = [(0, count * per - units.shape[0])] + [(0, 0)] * (units.ndim - 1)
    return jnp.pad(units, padding, constant_values=fill).reshape((count, per) + units.shape[1:])


def merge_attention(local_max, local_total, local_weighted, own_score, own_value, axis):
    count = lax.axis_size(axis)
    unit_count = local_max.shape[0]
    spread = jnp.concatenate(
        [
            spread_units(local_max[:, None], count, NEG_FILL),
            spread_units(jnp.concatenate([local_total[:, None], local_weighted], axis=1), count, 0.0),
        ],
        axis=2,
    )
    parts = lax.all_to_all(spread, axis, 0, 0, tiled=True)
    part_max = parts[:, :, 0]
    merged_max = jnp.max(part_max, axis=0)
    rescale = jnp.exp(part_max - merged_max[None, :])
    merged_total = jnp.sum(rescale * parts[:, :, 1], axis=0)
    merged_weighted = jnp.sum(rescale[:, :, None] * parts[:, :, 2:], axis=0)
    row_max = jnp.maximum(merged_max, own_score)
    old_scale = jnp.exp(merged_max - row_max)
    self_weight = jnp.exp(own_score - row_max)
    denominator = merged_total * old_scale + self_weight
    weighted = merged_weighted * old_scale[:, None] + self_weight[:, None] * own_value
    fraction = jnp.concatenate([weighted, denominator[:, None]], axis=1)
    gathered = lax.all_to_all(
        jnp.broadcast_to(fraction.reshape(1, -1), (count, fraction.size)), axis, 0, 0, tiled=True
    ).reshape(-1, fraction.shape[-1])[:unit_count]
    return (gathered[:, :-1] / gathered[:, -1:]).astype(jnp.bfloat16)


def shards(
    hidden,
    attn_gain,
    final_gain,
    query_gain,
    new_key_gain,
    query_weight,
    key_value_weight,
    output_weight,
    head_weight,
    page_cache,
    cache_length,
    page_table,
):
    token_rows = hidden[0].astype(jnp.float32)
    lengths = cache_length[0]
    page_map = page_table[0]
    nearby_cache = page_cache[0]
    request_number = token_rows.shape[0]
    half_rows = request_number // 2
    part_width = query_weight.shape[0]
    nearby_heads = query_weight.shape[1] // HEAD_SIZE
    query_width = query_weight.shape[1]
    scale = 1.0 / HEAD_SIZE**0.5
    shard_index = lax.axis_index("seq")
    normed = norm_rows(token_rows, attn_gain)
    normed_part = lax.dynamic_slice_in_dim(normed, shard_index * part_width, part_width, 1)
    seq_count = lax.axis_size("seq")
    group_width = QUERY_HEADS // KEY_VALUE_HEADS
    unit_count = request_number * nearby_heads
    unit_per = -(-unit_count // seq_count)
    unit_index = jnp.minimum(jnp.arange(seq_count * unit_per), unit_count - 1)
    unit_request = unit_index // nearby_heads
    unit_kv_head = (lax.axis_index("tp") * nearby_heads + unit_index % nearby_heads) // group_width
    query_part = jnp.dot(normed_part, query_weight, preferred_element_type=jnp.float32)
    key_value_part = jnp.dot(normed_part, key_value_weight, preferred_element_type=jnp.float32)
    unit_key_value = key_value_part.reshape(request_number, 2, KEY_VALUE_HEADS, HEAD_SIZE)[
        unit_request, :, unit_kv_head, :
    ]
    outgoing = jnp.concatenate(
        [
            query_part.reshape(seq_count, -1),
            unit_key_value.reshape(seq_count, unit_per * 2 * HEAD_SIZE),
        ],
        axis=1,
    )
    summed = jnp.sum(lax.all_to_all(outgoing, "seq", 0, 0, tiled=True), axis=0)
    query_chunk = summed[: query_width * request_number // seq_count]
    own_key_value = summed[query_chunk.shape[0] :].reshape(unit_per, 2, HEAD_SIZE)
    query_sum = lax.all_to_all(
        jnp.broadcast_to(query_chunk[None], (seq_count,) + query_chunk.shape), "seq", 0, 0, tiled=True
    ).reshape(request_number, query_width)
    query_normed = per_head_norm(
        query_sum.reshape(request_number, nearby_heads, HEAD_SIZE), query_gain
    )
    query_rot = rotate(query_normed, lengths).astype(jnp.bfloat16)
    own_unit = lax.dynamic_slice_in_dim(unit_index, shard_index * unit_per, unit_per, 0)
    own_positions = jnp.take(lengths, own_unit // nearby_heads)
    own_key = rotate(per_head_norm(own_key_value[:, None, 0], new_key_gain), own_positions)
    own_key = own_key[:, 0].astype(jnp.bfloat16).astype(jnp.float32)
    own_value = own_key_value[:, 1].astype(jnp.bfloat16).astype(jnp.float32)
    own_query = query_rot.reshape(unit_count, HEAD_SIZE)[own_unit].astype(jnp.float32)
    own_score = jnp.sum(own_query * own_key, axis=1) * scale
    head_mapping = (lax.axis_index("tp") * nearby_heads + jnp.arange(nearby_heads)) // group_width
    slot_number = nearby_cache.shape[0]
    page_token_count = nearby_cache.shape[1]
    global_slot = shard_index * slot_number + jnp.arange(slot_number)
    matches = page_map[:, :, None] == global_slot[None, None, :]
    owner_mask = jnp.any(matches, axis=1)
    page_number = jnp.sum(
        jnp.where(matches, jnp.arange(page_map.shape[1])[None, :, None], 0), axis=(0, 1)
    )
    owner_req = jnp.sum(jnp.where(owner_mask, jnp.arange(request_number)[:, None], 0), axis=0)
    slot_live = jnp.any(owner_mask, axis=0)
    owner_length = jnp.take(lengths, owner_req)
    positions = page_number[:, None] * page_token_count + jnp.arange(page_token_count)[None, :]
    is_valid = slot_live[:, None] & (positions < owner_length[:, None])
    first_kv = jnp.minimum(head_mapping[0], KEY_VALUE_HEADS - 2)
    second = (head_mapping - first_kv)[None, None, :, None] == 1
    key_pair = lax.dynamic_slice_in_dim(nearby_cache, first_kv * HEAD_SIZE, 2 * HEAD_SIZE, 2)
    value_pair = lax.dynamic_slice_in_dim(
        nearby_cache, (KEY_VALUE_HEADS + first_kv) * HEAD_SIZE, 2 * HEAD_SIZE, 2
    )
    key_heads = jnp.where(second, key_pair[:, :, None, HEAD_SIZE:], key_pair[:, :, None, :HEAD_SIZE])
    value_heads = jnp.where(
        second, value_pair[:, :, None, HEAD_SIZE:], value_pair[:, :, None, :HEAD_SIZE]
    )
    slot_query = jnp.take(query_rot, owner_req, axis=0)
    scores = (
        jnp.einsum("shd,skhd->shk", slot_query, key_heads, preferred_element_type=jnp.float32)
        * scale
    )
    scores = jnp.where(is_valid[:, None, :], scores, NEG_FILL)
    slot_max = jnp.max(scores, axis=2)
    request_max = jnp.max(jnp.where(owner_mask[:, :, None], slot_max[None, :, :], NEG_FILL), axis=1)
    owner_max = jnp.take(request_max, owner_req, axis=0)
    weights = jnp.where(is_valid[:, None, :], jnp.exp(scores - owner_max[:, :, None]), 0.0).astype(
        jnp.bfloat16
    )
    slot_total = jnp.sum(weights.astype(jnp.float32), axis=2)
    slot_weighted = jnp.einsum(
        "shk,skhd->shd", weights, value_heads, preferred_element_type=jnp.float32
    )
    owner_float = owner_mask.astype(jnp.float32)
    request_total = jnp.dot(owner_float, slot_total, precision=lax.Precision.HIGHEST)
    request_weighted = jnp.einsum(
        "rs,shd->rhd", owner_float, slot_weighted, precision=lax.Precision.HIGHEST
    )
    attended = merge_attention(
        request_max.reshape(unit_count),
        request_total.reshape(unit_count),
        request_weighted.reshape(unit_count, HEAD_SIZE),
        own_score,
        own_value,
        "seq",
    ).reshape(request_number, nearby_heads * HEAD_SIZE)
    output_part = project(attended, output_weight)
    output_part = output_part + jnp.where(lax.axis_index("tp") == 0, token_rows, 0.0)
    guide_count = lax.axis_size("guide")
    tp_count = lax.axis_size("tp")
    outgoing = jnp.broadcast_to(
        output_part.reshape(guide_count, 1, half_rows, -1),
        (guide_count, tp_count, half_rows, output_part.shape[1]),
    ).reshape(guide_count * tp_count, half_rows, -1)
    incoming = lax.all_to_all(outgoing, ("guide", "tp"), 0, 0, tiled=True)
    residual = jnp.sum(incoming.reshape(guide_count, tp_count, half_rows, -1), axis=1)
    final_rows = norm_rows(residual, final_gain)
    final_part = lax.dynamic_slice_in_dim(final_rows, shard_index * part_width, part_width, 2)
    both = final_part.reshape(guide_count * half_rows, part_width)
    logit_part = project(both, head_weight, block=head_weight.shape[1])
    conditional_part = logit_part[:half_rows]
    unconditional_part = logit_part[half_rows:]
    guided_part = unconditional_part + GUIDE_WEIGHT * (conditional_part - unconditional_part)
    return all_reduce_columns(guided_part, "seq")


def solution(mesh):
    in_specs = (
        P("guide", None, None),
        P(),
        P(),
        P(),
        P(),
        P("seq", "tp"),
        P("seq", None),
        P("tp", None),
        P("seq", "tp"),
        P("guide", "seq", None, None),
        P("guide", None),
        P("guide", None, None),
    )
    out_specs = P("guide", "tp")
    return jax.shard_map(shards, mesh=mesh, in_specs=in_specs, out_specs=out_specs, check_vma=False)
```

```python
import jax
import jax.numpy as jnp
from jax import lax
from jax.sharding import PartitionSpec as P

QUERY_HEADS = 20
KEY_VALUE_HEADS = 5
HEAD_SIZE = 64


GUIDE_WEIGHT = 2.5
NORM_EPS = 1e-06
NEG_FILL = -1e30


def norm_rows(token_rows, scale_gain):
    mean_square = jnp.mean(token_rows * token_rows, axis=-1, keepdims=True)
    return (token_rows * lax.rsqrt(mean_square + NORM_EPS) * scale_gain).astype(jnp.bfloat16)


def per_head_norm(vectors, head_gain):
    mean_square = jnp.mean(vectors * vectors, axis=-1, keepdims=True)
    return vectors * lax.rsqrt(mean_square + NORM_EPS) * head_gain


def rotate(vectors, positions):
    half_dim = vectors.shape[-1] // 2
    frequency = 10000.0 ** (-jnp.arange(half_dim).astype(jnp.float32) / half_dim)
    angles = positions.astype(jnp.float32)[:, None] * frequency[None, :]
    cosine = jnp.cos(angles)[:, None, :]
    sine_part = jnp.sin(angles)[:, None, :]
    first_half = vectors[..., :half_dim]
    second_half = vectors[..., half_dim:]
    return jnp.concatenate(
        [
            first_half * cosine - second_half * sine_part,
            second_half * cosine + first_half * sine_part,
        ],
        axis=-1,
    )


def all_reduce(value, axis):
    count = lax.axis_size(axis)
    flat = value.reshape(-1)
    chunk = -(-flat.size // count)
    chunk = -(-chunk // 128) * 128
    flat = jnp.pad(flat, (0, count * chunk - flat.size))
    parts = lax.all_to_all(flat.reshape(count, chunk), axis, 0, 0, tiled=True)
    total = jnp.sum(parts, axis=0, keepdims=True)
    whole = lax.all_to_all(jnp.broadcast_to(total, (count, chunk)), axis, 0, 0, tiled=True)
    return whole.reshape(-1)[: value.size].reshape(value.shape)


def spread_units(units, count, fill):
    rows, heads = units.shape[:2]
    slots = -(-heads * rows // count) * count // rows
    padding = [(0, 0), (0, slots - heads)] + [(0, 0)] * (units.ndim - 2)
    padded = jnp.pad(units, padding, constant_values=fill)
    return padded.reshape((count, rows * slots // count) + units.shape[2:])


def merge_attention(local_max, local_total, local_weighted, own_score, own_value, axis):
    count = lax.axis_size(axis)
    rows, heads = local_max.shape
    spread = jnp.concatenate(
        [
            spread_units(local_max[:, :, None], count, NEG_FILL),
            spread_units(jnp.concatenate([local_total[:, :, None], local_weighted], axis=2), count, 0.0),
        ],
        axis=2,
    )
    parts = lax.all_to_all(spread, axis, 0, 0, tiled=True)
    part_max = parts[:, :, 0]
    merged_max = jnp.max(part_max, axis=0)
    rescale = jnp.exp(part_max - merged_max[None, :])
    merged_total = jnp.sum(rescale * parts[:, :, 1], axis=0)
    merged_weighted = jnp.sum(rescale[:, :, None] * parts[:, :, 2:], axis=0)
    row_max = jnp.maximum(merged_max, own_score)
    old_scale = jnp.exp(merged_max - row_max)
    self_weight = jnp.exp(own_score - row_max)
    denominator = merged_total * old_scale + self_weight
    weighted = merged_weighted * old_scale[:, None] + self_weight[:, None] * own_value
    fraction = jnp.concatenate([weighted, denominator[:, None]], axis=1)
    gathered = lax.all_to_all(
        jnp.broadcast_to(fraction[None], (count,) + fraction.shape), axis, 0, 0, tiled=True
    ).reshape(rows, -1, fraction.shape[-1])[:, :heads]
    return (gathered[:, :, :-1] / gathered[:, :, -1:]).astype(jnp.bfloat16)


def shards(
    hidden,
    attn_gain,
    final_gain,
    query_gain,
    new_key_gain,
    query_weight,
    key_value_weight,
    output_weight,
    head_weight,
    page_cache,
    cache_length,
    page_table,
):
    token_rows = hidden[0].astype(jnp.float32)
    lengths = cache_length[0]
    page_map = page_table[0]
    nearby_cache = page_cache[0]
    request_number = token_rows.shape[0]
    half_rows = request_number // 2
    part_width = query_weight.shape[0]
    nearby_heads = query_weight.shape[1] // HEAD_SIZE
    query_width = query_weight.shape[1]
    scale = 1.0 / HEAD_SIZE**0.5
    shard_index = lax.axis_index("seq")
    normed = norm_rows(token_rows, attn_gain)
    normed_part = lax.dynamic_slice_in_dim(normed, shard_index * part_width, part_width, 1)
    seq_count = lax.axis_size("seq")
    group_width = QUERY_HEADS // KEY_VALUE_HEADS
    unit_count = request_number * nearby_heads
    slots_per_request = -(-nearby_heads * request_number // seq_count) * seq_count // request_number
    unit_per = request_number * slots_per_request // seq_count
    head_mapping = (lax.axis_index("tp") * nearby_heads + jnp.arange(nearby_heads)) // group_width
    key_weight = key_value_weight[:, : KEY_VALUE_HEADS * HEAD_SIZE].reshape(
        part_width, KEY_VALUE_HEADS, HEAD_SIZE
    )
    value_weight = key_value_weight[:, KEY_VALUE_HEADS * HEAD_SIZE :].reshape(
        part_width, KEY_VALUE_HEADS, HEAD_SIZE
    )
    unit_weight = jnp.stack(
        [
            query_weight.reshape(part_width, nearby_heads, HEAD_SIZE),
            jnp.take(key_weight, head_mapping, axis=1),
            jnp.take(value_weight, head_mapping, axis=1),
        ],
        axis=2,
    )
    unit_weight = jnp.pad(
        unit_weight, ((0, 0), (0, slots_per_request - nearby_heads), (0, 0), (0, 0))
    ).reshape(part_width, -1)
    unit_part = jnp.dot(normed_part, unit_weight, preferred_element_type=jnp.float32)
    summed = jnp.sum(
        lax.all_to_all(unit_part.reshape(seq_count, -1), "seq", 0, 0, tiled=True), axis=0
    ).reshape(unit_per, 3, HEAD_SIZE)
    query_sum = lax.all_to_all(
        jnp.broadcast_to(summed[None, :, 0], (seq_count, unit_per, HEAD_SIZE)), "seq", 0, 0, tiled=True
    ).reshape(request_number, slots_per_request, HEAD_SIZE)[:, :nearby_heads]
    query_normed = per_head_norm(query_sum, query_gain)
    query_rot = rotate(query_normed, lengths).astype(jnp.bfloat16)
    own_position = jnp.take(lengths, shard_index * unit_per // slots_per_request)[None]
    own_query = rotate(per_head_norm(summed[None, :, 0], query_gain), own_position)[0]
    own_query = own_query.astype(jnp.bfloat16).astype(jnp.float32)
    own_key = rotate(per_head_norm(summed[None, :, 1], new_key_gain), own_position)[0]
    own_key = own_key.astype(jnp.bfloat16).astype(jnp.float32)
    own_value = summed[:, 2].astype(jnp.bfloat16).astype(jnp.float32)
    own_score = jnp.sum(own_query * own_key, axis=1) * scale
    slot_number = nearby_cache.shape[0]
    page_token_count = nearby_cache.shape[1]
    global_slot = shard_index * slot_number + jnp.arange(slot_number)
    matches = page_map[:, :, None] == global_slot[None, None, :]
    owner_mask = jnp.any(matches, axis=1)
    page_number = jnp.sum(
        jnp.where(matches, jnp.arange(page_map.shape[1])[None, :, None], 0), axis=(0, 1)
    )
    owner_req = jnp.sum(jnp.where(owner_mask, jnp.arange(request_number)[:, None], 0), axis=0)
    slot_live = jnp.any(owner_mask, axis=0)
    owner_length = jnp.take(lengths, owner_req)
    positions = page_number[:, None] * page_token_count + jnp.arange(page_token_count)[None, :]
    is_valid = slot_live[:, None] & (positions < owner_length[:, None])
    first_kv = jnp.minimum(head_mapping[0], KEY_VALUE_HEADS - 2)
    second = (head_mapping - first_kv)[None, None, :, None] == 1
    key_pair = lax.dynamic_slice_in_dim(nearby_cache, first_kv * HEAD_SIZE, 2 * HEAD_SIZE, 2)
    value_pair = lax.dynamic_slice_in_dim(
        nearby_cache, (KEY_VALUE_HEADS + first_kv) * HEAD_SIZE, 2 * HEAD_SIZE, 2
    )
    key_heads = jnp.where(second, key_pair[:, :, None, HEAD_SIZE:], key_pair[:, :, None, :HEAD_SIZE])
    value_heads = jnp.where(
        second, value_pair[:, :, None, HEAD_SIZE:], value_pair[:, :, None, :HEAD_SIZE]
    )
    slot_query = jnp.take(query_rot, owner_req, axis=0)
    scores = (
        jnp.einsum("shd,skhd->shk", slot_query, key_heads, preferred_element_type=jnp.float32)
        * scale
    )
    scores = jnp.where(is_valid[:, None, :], scores, NEG_FILL)
    slot_max = jnp.max(scores, axis=2)
    request_max = jnp.max(jnp.where(owner_mask[:, :, None], slot_max[None, :, :], NEG_FILL), axis=1)
    owner_max = jnp.take(request_max, owner_req, axis=0)
    weights = jnp.where(is_valid[:, None, :], jnp.exp(scores - owner_max[:, :, None]), 0.0).astype(
        jnp.bfloat16
    )
    slot_total = jnp.sum(weights.astype(jnp.float32), axis=2)
    slot_weighted = jnp.einsum(
        "shk,skhd->shd", weights, value_heads, preferred_element_type=jnp.float32
    )
    owner_float = owner_mask.astype(jnp.float32)
    request_total = jnp.dot(owner_float, slot_total, precision=lax.Precision.HIGHEST)
    request_weighted = jnp.einsum(
        "rs,shd->rhd", owner_float, slot_weighted, precision=lax.Precision.HIGHEST
    )
    attended = merge_attention(
        request_max,
        request_total,
        request_weighted,
        own_score,
        own_value,
        "seq",
    ).reshape(request_number, nearby_heads * HEAD_SIZE)
    output_part = jnp.dot(attended, output_weight, preferred_element_type=jnp.float32)
    output_part = output_part + jnp.where(lax.axis_index("tp") == 0, token_rows, 0.0)
    guide_count = lax.axis_size("guide")
    tp_count = lax.axis_size("tp")
    outgoing = jnp.broadcast_to(
        output_part.reshape(guide_count, 1, half_rows, -1),
        (guide_count, tp_count, half_rows, output_part.shape[1]),
    ).reshape(guide_count * tp_count, half_rows, -1)
    incoming = lax.all_to_all(outgoing, ("guide", "tp"), 0, 0, tiled=True)
    residual = jnp.sum(incoming.reshape(guide_count, tp_count, half_rows, -1), axis=1)
    final_rows = norm_rows(residual, final_gain)
    final_part = lax.dynamic_slice_in_dim(final_rows, shard_index * part_width, part_width, 2)
    both = final_part.reshape(guide_count * half_rows, part_width)
    logit_part = jnp.dot(both, head_weight, preferred_element_type=jnp.float32)
    conditional_part = logit_part[:half_rows]
    unconditional_part = logit_part[half_rows:]
    guided_part = unconditional_part + GUIDE_WEIGHT * (conditional_part - unconditional_part)
    return all_reduce(guided_part, "seq")


def solution(mesh):
    in_specs = (
        P("guide", None, None),
        P(),
        P(),
        P(),
        P(),
        P("seq", "tp"),
        P("seq", None),
        P("tp", None),
        P("seq", "tp"),
        P("guide", "seq", None, None),
        P("guide", None),
        P("guide", None, None),
    )
    out_specs = P("guide", "tp")
    return jax.shard_map(shards, mesh=mesh, in_specs=in_specs, out_specs=out_specs, check_vma=False)
```

```python
import jax
import jax.numpy as jnp
from jax import lax
from jax.sharding import PartitionSpec as P

QUERY_HEADS = 20
KEY_VALUE_HEADS = 5
HEAD_SIZE = 64


GUIDE_WEIGHT = 2.5
NORM_EPS = 1e-06
NEG_FILL = -1e30


def norm_rows(token_rows, scale_gain):
    mean_square = jnp.mean(token_rows * token_rows, axis=-1, keepdims=True)
    return (token_rows * lax.rsqrt(mean_square + NORM_EPS) * scale_gain).astype(jnp.bfloat16)


def per_head_norm(vectors, head_gain):
    mean_square = jnp.mean(vectors * vectors, axis=-1, keepdims=True)
    return vectors * lax.rsqrt(mean_square + NORM_EPS) * head_gain


def rotate(vectors, positions):
    half_dim = vectors.shape[-1] // 2
    frequency = 10000.0 ** (-jnp.arange(half_dim).astype(jnp.float32) / half_dim)
    angles = positions.astype(jnp.float32)[:, None] * frequency[None, :]
    cosine = jnp.cos(angles)[:, None, :]
    sine_part = jnp.sin(angles)[:, None, :]
    first_half = vectors[..., :half_dim]
    second_half = vectors[..., half_dim:]
    return jnp.concatenate(
        [
            first_half * cosine - second_half * sine_part,
            second_half * cosine + first_half * sine_part,
        ],
        axis=-1,
    )


def all_reduce(value, axis):
    count = lax.axis_size(axis)
    flat = value.reshape(-1)
    chunk = -(-flat.size // count)
    chunk = -(-chunk // 128) * 128
    flat = jnp.pad(flat, (0, count * chunk - flat.size))
    parts = lax.all_to_all(flat.reshape(count, chunk), axis, 0, 0, tiled=True)
    total = jnp.sum(parts, axis=0, keepdims=True)
    whole = lax.all_to_all(jnp.broadcast_to(total, (count, chunk)), axis, 0, 0, tiled=True)
    return whole.reshape(-1)[: value.size].reshape(value.shape)


def all_reduce_columns(value, axis):
    count = lax.axis_size(axis)
    rows, columns = value.shape
    if columns % count:
        return all_reduce(value, axis)
    parts = lax.all_to_all(value, axis, 1, 0, tiled=True)
    total = jnp.sum(parts.reshape(count, rows, columns // count), axis=0)
    whole = lax.all_to_all(
        jnp.broadcast_to(total[None], (count, rows, columns // count)), axis, 0, 2, tiled=True
    )
    return whole[0]


def spread_units(units, count, fill):
    per = -(-units.shape[0] // count)
    padding = [(0, count * per - units.shape[0])] + [(0, 0)] * (units.ndim - 1)
    return jnp.pad(units, padding, constant_values=fill).reshape((count, per) + units.shape[1:])


def merge_attention(local_max, local_total, local_weighted, own_score, own_value, axis):
    count = lax.axis_size(axis)
    unit_count = local_max.shape[0]
    spread = jnp.concatenate(
        [
            spread_units(local_max[:, None], count, NEG_FILL),
            spread_units(jnp.concatenate([local_total[:, None], local_weighted], axis=1), count, 0.0),
        ],
        axis=2,
    )
    parts = lax.all_to_all(spread, axis, 0, 0, tiled=True)
    part_max = parts[:, :, 0]
    merged_max = jnp.max(part_max, axis=0)
    rescale = jnp.exp(part_max - merged_max[None, :])
    merged_total = jnp.sum(rescale * parts[:, :, 1], axis=0)
    merged_weighted = jnp.sum(rescale[:, :, None] * parts[:, :, 2:], axis=0)
    row_max = jnp.maximum(merged_max, own_score)
    old_scale = jnp.exp(merged_max - row_max)
    self_weight = jnp.exp(own_score - row_max)
    denominator = merged_total * old_scale + self_weight
    weighted = merged_weighted * old_scale[:, None] + self_weight[:, None] * own_value
    fraction = jnp.concatenate([weighted, denominator[:, None]], axis=1)
    gathered = lax.all_to_all(
        jnp.broadcast_to(fraction.reshape(1, -1), (count, fraction.size)), axis, 0, 0, tiled=True
    ).reshape(-1, fraction.shape[-1])[:unit_count]
    return (gathered[:, :-1] / gathered[:, -1:]).astype(jnp.bfloat16)


def shards(
    hidden,
    attn_gain,
    final_gain,
    query_gain,
    new_key_gain,
    query_weight,
    key_value_weight,
    output_weight,
    head_weight,
    page_cache,
    cache_length,
    page_table,
):
    token_rows = hidden[0].astype(jnp.float32)
    lengths = cache_length[0]
    page_map = page_table[0]
    nearby_cache = page_cache[0]
    request_number = token_rows.shape[0]
    half_rows = request_number // 2
    part_width = query_weight.shape[0]
    nearby_heads = query_weight.shape[1] // HEAD_SIZE
    query_width = query_weight.shape[1]
    scale = 1.0 / HEAD_SIZE**0.5
    shard_index = lax.axis_index("seq")
    normed = norm_rows(token_rows, attn_gain)
    normed_part = lax.dynamic_slice_in_dim(normed, shard_index * part_width, part_width, 1)
    seq_count = lax.axis_size("seq")
    group_width = QUERY_HEADS // KEY_VALUE_HEADS
    unit_count = request_number * nearby_heads
    unit_per = -(-unit_count // seq_count)
    unit_index = jnp.minimum(jnp.arange(seq_count * unit_per), unit_count - 1)
    unit_request = unit_index // nearby_heads
    unit_kv_head = (lax.axis_index("tp") * nearby_heads + unit_index % nearby_heads) // group_width
    query_part = jnp.dot(normed_part, query_weight, preferred_element_type=jnp.float32)
    key_value_part = jnp.dot(normed_part, key_value_weight, preferred_element_type=jnp.float32)
    unit_key_value = key_value_part.reshape(request_number, 2, KEY_VALUE_HEADS, HEAD_SIZE)[
        unit_request, :, unit_kv_head, :
    ]
    outgoing = jnp.concatenate(
        [
            query_part.reshape(seq_count, -1),
            unit_key_value.reshape(seq_count, unit_per * 2 * HEAD_SIZE),
        ],
        axis=1,
    )
    summed = jnp.sum(lax.all_to_all(outgoing, "seq", 0, 0, tiled=True), axis=0)
    query_chunk = summed[: query_width * request_number // seq_count]
    own_key_value = summed[query_chunk.shape[0] :].reshape(unit_per, 2, HEAD_SIZE)
    query_sum = lax.all_to_all(
        jnp.broadcast_to(query_chunk[None], (seq_count,) + query_chunk.shape), "seq", 0, 0, tiled=True
    ).reshape(request_number, query_width)
    query_normed = per_head_norm(
        query_sum.reshape(request_number, nearby_heads, HEAD_SIZE), query_gain
    )
    query_rot = rotate(query_normed, lengths).astype(jnp.bfloat16)
    own_unit = lax.dynamic_slice_in_dim(unit_index, shard_index * unit_per, unit_per, 0)
    own_positions = jnp.take(lengths, own_unit // nearby_heads)
    own_key = rotate(per_head_norm(own_key_value[:, None, 0], new_key_gain), own_positions)
    own_key = own_key[:, 0].astype(jnp.bfloat16).astype(jnp.float32)
    own_value = own_key_value[:, 1].astype(jnp.bfloat16).astype(jnp.float32)
    own_query = query_rot.reshape(unit_count, HEAD_SIZE)[own_unit].astype(jnp.float32)
    own_score = jnp.sum(own_query * own_key, axis=1) * scale
    head_mapping = (lax.axis_index("tp") * nearby_heads + jnp.arange(nearby_heads)) // group_width
    slot_number = nearby_cache.shape[0]
    page_token_count = nearby_cache.shape[1]
    global_slot = shard_index * slot_number + jnp.arange(slot_number)
    matches = page_map[:, :, None] == global_slot[None, None, :]
    owner_mask = jnp.any(matches, axis=1)
    page_number = jnp.sum(
        jnp.where(matches, jnp.arange(page_map.shape[1])[None, :, None], 0), axis=(0, 1)
    )
    owner_req = jnp.sum(jnp.where(owner_mask, jnp.arange(request_number)[:, None], 0), axis=0)
    slot_live = jnp.any(owner_mask, axis=0)
    owner_length = jnp.take(lengths, owner_req)
    positions = page_number[:, None] * page_token_count + jnp.arange(page_token_count)[None, :]
    is_valid = slot_live[:, None] & (positions < owner_length[:, None])
    first_kv = jnp.minimum(head_mapping[0], KEY_VALUE_HEADS - 2)
    second = (head_mapping - first_kv)[None, None, :, None] == 1
    key_pair = lax.dynamic_slice_in_dim(nearby_cache, first_kv * HEAD_SIZE, 2 * HEAD_SIZE, 2)
    value_pair = lax.dynamic_slice_in_dim(
        nearby_cache, (KEY_VALUE_HEADS + first_kv) * HEAD_SIZE, 2 * HEAD_SIZE, 2
    )
    key_heads = jnp.where(second, key_pair[:, :, None, HEAD_SIZE:], key_pair[:, :, None, :HEAD_SIZE])
    value_heads = jnp.where(
        second, value_pair[:, :, None, HEAD_SIZE:], value_pair[:, :, None, :HEAD_SIZE]
    )
    slot_query = jnp.einsum(
        "rs,rhd->shd", owner_mask.astype(jnp.bfloat16), query_rot, preferred_element_type=jnp.float32
    ).astype(jnp.bfloat16)
    scores = (
        jnp.einsum("shd,skhd->shk", slot_query, key_heads, preferred_element_type=jnp.float32)
        * scale
    )
    scores = jnp.where(is_valid[:, None, :], scores, NEG_FILL)
    slot_max = jnp.max(scores, axis=2)
    request_max = jnp.max(jnp.where(owner_mask[:, :, None], slot_max[None, :, :], NEG_FILL), axis=1)
    owner_max = jnp.max(jnp.where(owner_mask[:, :, None], request_max[:, None, :], NEG_FILL), axis=0)
    weights = jnp.where(is_valid[:, None, :], jnp.exp(scores - owner_max[:, :, None]), 0.0).astype(
        jnp.bfloat16
    )
    slot_total = jnp.sum(weights.astype(jnp.float32), axis=2)
    slot_weighted = jnp.einsum(
        "shk,skhd->shd", weights, value_heads, preferred_element_type=jnp.float32
    )
    owner_float = owner_mask.astype(jnp.float32)
    request_total = jnp.dot(owner_float, slot_total, precision=lax.Precision.HIGHEST)
    request_weighted = jnp.einsum(
        "rs,shd->rhd", owner_float, slot_weighted, precision=lax.Precision.HIGHEST
    )
    attended = merge_attention(
        request_max.reshape(unit_count),
        request_total.reshape(unit_count),
        request_weighted.reshape(unit_count, HEAD_SIZE),
        own_score,
        own_value,
        "seq",
    ).reshape(request_number, nearby_heads * HEAD_SIZE)
    output_part = jnp.dot(attended, output_weight, preferred_element_type=jnp.float32)
    output_part = output_part + jnp.where(lax.axis_index("tp") == 0, token_rows, 0.0)
    guide_count = lax.axis_size("guide")
    tp_count = lax.axis_size("tp")
    outgoing = jnp.broadcast_to(
        output_part.reshape(guide_count, 1, half_rows, -1),
        (guide_count, tp_count, half_rows, output_part.shape[1]),
    ).reshape(guide_count * tp_count, half_rows, -1)
    incoming = lax.all_to_all(outgoing, ("guide", "tp"), 0, 0, tiled=True)
    residual = jnp.sum(incoming.reshape(guide_count, tp_count, half_rows, -1), axis=1)
    final_rows = norm_rows(residual, final_gain)
    final_part = lax.dynamic_slice_in_dim(final_rows, shard_index * part_width, part_width, 2)
    both = final_part.reshape(guide_count * half_rows, part_width)
    logit_part = jnp.dot(both, head_weight, preferred_element_type=jnp.float32)
    conditional_part = logit_part[:half_rows]
    unconditional_part = logit_part[half_rows:]
    guided_part = unconditional_part + GUIDE_WEIGHT * (conditional_part - unconditional_part)
    return all_reduce_columns(guided_part, "seq")


def solution(mesh):
    in_specs = (
        P("guide", None, None),
        P(),
        P(),
        P(),
        P(),
        P("seq", "tp"),
        P("seq", None),
        P("tp", None),
        P("seq", "tp"),
        P("guide", "seq", None, None),
        P("guide", None),
        P("guide", None, None),
    )
    out_specs = P("guide", "tp")
    return jax.shard_map(shards, mesh=mesh, in_specs=in_specs, out_specs=out_specs, check_vma=False)
```

```python
import jax
import jax.numpy as jnp
from jax import lax
from jax.sharding import PartitionSpec as P

QUERY_HEADS = 20
KEY_VALUE_HEADS = 5
HEAD_SIZE = 64


GUIDE_WEIGHT = 2.5
NORM_EPS = 1e-06
NEG_FILL = -1e30


def norm_rows(token_rows, scale_gain):
    mean_square = jnp.mean(token_rows * token_rows, axis=-1, keepdims=True)
    return (token_rows * lax.rsqrt(mean_square + NORM_EPS) * scale_gain).astype(jnp.bfloat16)


def per_head_norm(vectors, head_gain):
    mean_square = jnp.mean(vectors * vectors, axis=-1, keepdims=True)
    return vectors * lax.rsqrt(mean_square + NORM_EPS) * head_gain


def rotate(vectors, positions):
    half_dim = vectors.shape[-1] // 2
    frequency = 10000.0 ** (-jnp.arange(half_dim).astype(jnp.float32) / half_dim)
    angles = positions.astype(jnp.float32)[:, None] * frequency[None, :]
    cosine = jnp.cos(angles)[:, None, :]
    sine_part = jnp.sin(angles)[:, None, :]
    first_half = vectors[..., :half_dim]
    second_half = vectors[..., half_dim:]
    return jnp.concatenate(
        [
            first_half * cosine - second_half * sine_part,
            second_half * cosine + first_half * sine_part,
        ],
        axis=-1,
    )


def all_reduce(value, axis):
    count = lax.axis_size(axis)
    flat = value.reshape(-1)
    chunk = -(-flat.size // count)
    chunk = -(-chunk // 128) * 128
    flat = jnp.pad(flat, (0, count * chunk - flat.size))
    parts = lax.all_to_all(flat.reshape(count, chunk), axis, 0, 0, tiled=True)
    total = jnp.sum(parts, axis=0, keepdims=True)
    whole = lax.all_to_all(jnp.broadcast_to(total, (count, chunk)), axis, 0, 0, tiled=True)
    return whole.reshape(-1)[: value.size].reshape(value.shape)


def all_reduce_columns(value, axis):
    count = lax.axis_size(axis)
    rows, columns = value.shape
    if columns % count:
        return all_reduce(value, axis)
    parts = lax.all_to_all(value, axis, 1, 0, tiled=True)
    total = jnp.sum(parts.reshape(count, rows, columns // count), axis=0)
    whole = lax.all_to_all(
        jnp.broadcast_to(total[None], (count, rows, columns // count)), axis, 0, 2, tiled=True
    )
    return whole[0]


def spread_units(units, count, fill):
    per = -(-units.shape[0] // count)
    padding = [(0, count * per - units.shape[0])] + [(0, 0)] * (units.ndim - 1)
    return jnp.pad(units, padding, constant_values=fill).reshape((count, per) + units.shape[1:])


def merge_attention(local_max, local_total, local_weighted, own_score, own_value, axis):
    count = lax.axis_size(axis)
    unit_count = local_max.shape[0]
    spread = jnp.concatenate(
        [
            spread_units(local_max[:, None], count, NEG_FILL),
            spread_units(jnp.concatenate([local_total[:, None], local_weighted], axis=1), count, 0.0),
        ],
        axis=2,
    )
    parts = lax.all_to_all(spread, axis, 0, 0, tiled=True)
    part_max = parts[:, :, 0]
    merged_max = jnp.max(part_max, axis=0)
    rescale = jnp.exp(part_max - merged_max[None, :])
    merged_total = jnp.sum(rescale * parts[:, :, 1], axis=0)
    merged_weighted = jnp.sum(rescale[:, :, None] * parts[:, :, 2:], axis=0)
    row_max = jnp.maximum(merged_max, own_score)
    old_scale = jnp.exp(merged_max - row_max)
    self_weight = jnp.exp(own_score - row_max)
    denominator = merged_total * old_scale + self_weight
    weighted = merged_weighted * old_scale[:, None] + self_weight[:, None] * own_value
    fraction = jnp.concatenate([weighted, denominator[:, None]], axis=1)
    gathered = lax.all_to_all(
        jnp.broadcast_to(fraction.reshape(1, -1), (count, fraction.size)), axis, 0, 0, tiled=True
    ).reshape(-1, fraction.shape[-1])[:unit_count]
    return (gathered[:, :-1] / gathered[:, -1:]).astype(jnp.bfloat16)


def shards(
    hidden,
    attn_gain,
    final_gain,
    query_gain,
    new_key_gain,
    query_weight,
    key_value_weight,
    output_weight,
    head_weight,
    page_cache,
    cache_length,
    page_table,
):
    token_rows = hidden[0].astype(jnp.float32)
    lengths = cache_length[0]
    page_map = page_table[0]
    nearby_cache = page_cache[0]
    request_number = token_rows.shape[0]
    half_rows = request_number // 2
    part_width = query_weight.shape[0]
    nearby_heads = query_weight.shape[1] // HEAD_SIZE
    query_width = query_weight.shape[1]
    scale = 1.0 / HEAD_SIZE**0.5
    shard_index = lax.axis_index("seq")
    normed = norm_rows(token_rows, attn_gain)
    normed_part = lax.dynamic_slice_in_dim(normed, shard_index * part_width, part_width, 1)
    seq_count = lax.axis_size("seq")
    group_width = QUERY_HEADS // KEY_VALUE_HEADS
    unit_count = request_number * nearby_heads
    unit_per = -(-unit_count // seq_count)
    unit_index = jnp.minimum(jnp.arange(seq_count * unit_per), unit_count - 1)
    unit_request = unit_index // nearby_heads
    unit_kv_head = (lax.axis_index("tp") * nearby_heads + unit_index % nearby_heads) // group_width
    query_part = jnp.dot(normed_part, query_weight, preferred_element_type=jnp.float32)
    key_value_part = jnp.dot(normed_part, key_value_weight, preferred_element_type=jnp.float32)
    unit_key_value = key_value_part.reshape(request_number, 2, KEY_VALUE_HEADS, HEAD_SIZE)[
        unit_request, :, unit_kv_head, :
    ]
    outgoing = jnp.concatenate(
        [
            query_part.reshape(seq_count, -1),
            unit_key_value.reshape(seq_count, unit_per * 2 * HEAD_SIZE),
        ],
        axis=1,
    )
    summed = jnp.sum(lax.all_to_all(outgoing, "seq", 0, 0, tiled=True), axis=0)
    query_chunk = summed[: query_width * request_number // seq_count]
    own_key_value = summed[query_chunk.shape[0] :].reshape(unit_per, 2, HEAD_SIZE)
    query_sum = lax.all_to_all(
        jnp.broadcast_to(query_chunk[None], (seq_count,) + query_chunk.shape), "seq", 0, 0, tiled=True
    ).reshape(request_number, query_width)
    query_normed = per_head_norm(
        query_sum.reshape(request_number, nearby_heads, HEAD_SIZE), query_gain
    )
    query_rot = rotate(query_normed, lengths).astype(jnp.bfloat16)
    own_unit = lax.dynamic_slice_in_dim(unit_index, shard_index * unit_per, unit_per, 0)
    own_positions = jnp.take(lengths, own_unit // nearby_heads)
    own_key = rotate(per_head_norm(own_key_value[:, None, 0], new_key_gain), own_positions)
    own_key = own_key[:, 0].astype(jnp.bfloat16).astype(jnp.float32)
    own_value = own_key_value[:, 1].astype(jnp.bfloat16).astype(jnp.float32)
    own_query = query_rot.reshape(unit_count, HEAD_SIZE)[own_unit].astype(jnp.float32)
    own_score = jnp.sum(own_query * own_key, axis=1) * scale
    head_mapping = (lax.axis_index("tp") * nearby_heads + jnp.arange(nearby_heads)) // group_width
    slot_number = nearby_cache.shape[0]
    page_token_count = nearby_cache.shape[1]
    global_slot = shard_index * slot_number + jnp.arange(slot_number)
    matches = page_map[:, :, None] == global_slot[None, None, :]
    owner_mask = jnp.any(matches, axis=1)
    page_number = jnp.sum(
        jnp.where(matches, jnp.arange(page_map.shape[1])[None, :, None], 0), axis=(0, 1)
    )
    owner_req = jnp.sum(jnp.where(owner_mask, jnp.arange(request_number)[:, None], 0), axis=0)
    slot_live = jnp.any(owner_mask, axis=0)
    owner_length = jnp.take(lengths, owner_req)
    positions = page_number[:, None] * page_token_count + jnp.arange(page_token_count)[None, :]
    is_valid = slot_live[:, None] & (positions < owner_length[:, None])
    first_kv = jnp.minimum(head_mapping[0], KEY_VALUE_HEADS - 2)
    second = (head_mapping - first_kv)[None, None, :, None] == 1
    key_pair = lax.dynamic_slice_in_dim(nearby_cache, first_kv * HEAD_SIZE, 2 * HEAD_SIZE, 2)
    value_pair = lax.dynamic_slice_in_dim(
        nearby_cache, (KEY_VALUE_HEADS + first_kv) * HEAD_SIZE, 2 * HEAD_SIZE, 2
    )
    key_heads = jnp.where(second, key_pair[:, :, None, HEAD_SIZE:], key_pair[:, :, None, :HEAD_SIZE])
    value_heads = jnp.where(
        second, value_pair[:, :, None, HEAD_SIZE:], value_pair[:, :, None, :HEAD_SIZE]
    )
    slot_query = jnp.einsum(
        "rs,rhd->shd", owner_mask.astype(jnp.bfloat16), query_rot, preferred_element_type=jnp.float32
    ).astype(jnp.bfloat16)
    scores = (
        jnp.einsum("shd,skhd->shk", slot_query, key_heads, preferred_element_type=jnp.float32)
        * scale
    )
    scores = jnp.where(is_valid[:, None, :], scores, NEG_FILL)
    slot_max = jnp.max(scores, axis=2)
    request_max = jnp.max(jnp.where(owner_mask[:, :, None], slot_max[None, :, :], NEG_FILL), axis=1)
    owner_max = jnp.max(jnp.where(owner_mask[:, :, None], request_max[:, None, :], NEG_FILL), axis=0)
    weights = jnp.where(is_valid[:, None, :], jnp.exp(scores - owner_max[:, :, None]), 0.0).astype(
        jnp.bfloat16
    )
    slot_total = jnp.sum(weights.astype(jnp.float32), axis=2)
    slot_weighted = jnp.einsum(
        "shk,skhd->shd", weights, value_heads, preferred_element_type=jnp.float32
    )
    owner_float = owner_mask.astype(jnp.float32)
    request_total = jnp.dot(owner_float, slot_total, precision=lax.Precision.HIGHEST)
    request_weighted = jnp.einsum(
        "rs,shd->rhd", owner_float, slot_weighted, precision=lax.Precision.HIGHEST
    )
    attended = merge_attention(
        request_max.reshape(unit_count),
        request_total.reshape(unit_count),
        request_weighted.reshape(unit_count, HEAD_SIZE),
        own_score,
        own_value,
        "seq",
    ).reshape(request_number, nearby_heads * HEAD_SIZE)
    output_part = jnp.dot(attended, output_weight, preferred_element_type=jnp.float32)
    output_part = output_part + jnp.where(lax.axis_index("tp") == 0, token_rows, 0.0)
    guide_count = lax.axis_size("guide")
    tp_count = lax.axis_size("tp")
    outgoing = jnp.broadcast_to(
        output_part.reshape(guide_count, 1, half_rows, -1),
        (guide_count, tp_count, half_rows, output_part.shape[1]),
    ).reshape(guide_count * tp_count, half_rows, -1)
    incoming = lax.all_to_all(outgoing, ("guide", "tp"), 0, 0, tiled=True)
    residual = jnp.sum(incoming.reshape(guide_count, tp_count, half_rows, -1), axis=1)
    final_rows = norm_rows(residual, final_gain)
    final_part = lax.dynamic_slice_in_dim(final_rows, shard_index * part_width, part_width, 2)
    both = final_part.reshape(guide_count * half_rows, part_width)
    logit_part = jnp.dot(both, head_weight, preferred_element_type=jnp.float32)
    conditional_part = logit_part[:half_rows]
    unconditional_part = logit_part[half_rows:]
    guided_part = unconditional_part + GUIDE_WEIGHT * (conditional_part - unconditional_part)
    return all_reduce(guided_part, "seq")


def solution(mesh):
    in_specs = (
        P("guide", None, None),
        P(),
        P(),
        P(),
        P(),
        P("seq", "tp"),
        P("seq", None),
        P("tp", None),
        P("seq", "tp"),
        P("guide", "seq", None, None),
        P("guide", None),
        P("guide", None, None),
    )
    out_specs = P("guide", "tp")
    return jax.shard_map(shards, mesh=mesh, in_specs=in_specs, out_specs=out_specs, check_vma=False)
```

```python
import jax
import jax.numpy as jnp
from jax import lax
from jax.sharding import PartitionSpec as P

QUERY_HEADS = 20
KEY_VALUE_HEADS = 5
HEAD_SIZE = 64


GUIDE_WEIGHT = 2.5
NORM_EPS = 1e-06
NEG_FILL = -1e30


def norm_rows(token_rows, scale_gain):
    mean_square = jnp.mean(token_rows * token_rows, axis=-1, keepdims=True)
    return (token_rows * lax.rsqrt(mean_square + NORM_EPS) * scale_gain).astype(jnp.bfloat16)


def per_head_norm(vectors, head_gain):
    mean_square = jnp.mean(vectors * vectors, axis=-1, keepdims=True)
    return vectors * lax.rsqrt(mean_square + NORM_EPS) * head_gain


def rotate(vectors, positions):
    half_dim = vectors.shape[-1] // 2
    frequency = 10000.0 ** (-jnp.arange(half_dim).astype(jnp.float32) / half_dim)
    angles = positions.astype(jnp.float32)[:, None] * frequency[None, :]
    cosine = jnp.cos(angles)[:, None, :]
    sine_part = jnp.sin(angles)[:, None, :]
    first_half = vectors[..., :half_dim]
    second_half = vectors[..., half_dim:]
    return jnp.concatenate(
        [
            first_half * cosine - second_half * sine_part,
            second_half * cosine + first_half * sine_part,
        ],
        axis=-1,
    )


def all_reduce(value, axis):
    count = lax.axis_size(axis)
    flat = value.reshape(-1)
    chunk = -(-flat.size // count)
    chunk = -(-chunk // 128) * 128
    flat = jnp.pad(flat, (0, count * chunk - flat.size))
    parts = lax.all_to_all(flat.reshape(count, chunk), axis, 0, 0, tiled=True)
    total = jnp.sum(parts, axis=0, keepdims=True)
    whole = lax.all_to_all(jnp.broadcast_to(total, (count, chunk)), axis, 0, 0, tiled=True)
    return whole.reshape(-1)[: value.size].reshape(value.shape)


def all_reduce_columns(value, axis):
    count = lax.axis_size(axis)
    rows, columns = value.shape
    if columns % count:
        return all_reduce(value, axis)
    parts = lax.all_to_all(value, axis, 1, 0, tiled=True)
    total = jnp.sum(parts.reshape(count, rows, columns // count), axis=0)
    whole = lax.all_to_all(
        jnp.broadcast_to(total[None], (count, rows, columns // count)), axis, 0, 2, tiled=True
    )
    return whole[0]


def spread_units(units, count, fill):
    per = -(-units.shape[0] // count)
    padding = [(0, count * per - units.shape[0])] + [(0, 0)] * (units.ndim - 1)
    return jnp.pad(units, padding, constant_values=fill).reshape((count, per) + units.shape[1:])


def merge_attention(local_max, local_total, local_weighted, own_score, own_value, axis):
    count = lax.axis_size(axis)
    unit_count = local_max.shape[0]
    spread = jnp.concatenate(
        [
            spread_units(local_max[:, None], count, NEG_FILL),
            spread_units(jnp.concatenate([local_total[:, None], local_weighted], axis=1), count, 0.0),
        ],
        axis=2,
    )
    parts = lax.all_to_all(spread, axis, 0, 0, tiled=True)
    part_max = parts[:, :, 0]
    merged_max = jnp.max(part_max, axis=0)
    rescale = jnp.exp(part_max - merged_max[None, :])
    merged_total = jnp.sum(rescale * parts[:, :, 1], axis=0)
    merged_weighted = jnp.sum(rescale[:, :, None] * parts[:, :, 2:], axis=0)
    row_max = jnp.maximum(merged_max, own_score)
    old_scale = jnp.exp(merged_max - row_max)
    self_weight = jnp.exp(own_score - row_max)
    denominator = merged_total * old_scale + self_weight
    weighted = merged_weighted * old_scale[:, None] + self_weight[:, None] * own_value
    fraction = jnp.concatenate([weighted, denominator[:, None]], axis=1)
    gathered = lax.all_to_all(
        jnp.broadcast_to(fraction.reshape(1, -1), (count, fraction.size)), axis, 0, 0, tiled=True
    ).reshape(-1, fraction.shape[-1])[:unit_count]
    return (gathered[:, :-1] / gathered[:, -1:]).astype(jnp.bfloat16)


def shards(
    hidden,
    attn_gain,
    final_gain,
    query_gain,
    new_key_gain,
    query_weight,
    key_value_weight,
    output_weight,
    head_weight,
    page_cache,
    cache_length,
    page_table,
):
    token_rows = hidden[0].astype(jnp.float32)
    lengths = cache_length[0]
    page_map = page_table[0]
    nearby_cache = page_cache[0]
    request_number = token_rows.shape[0]
    half_rows = request_number // 2
    part_width = query_weight.shape[0]
    nearby_heads = query_weight.shape[1] // HEAD_SIZE
    query_width = query_weight.shape[1]
    scale = 1.0 / HEAD_SIZE**0.5
    shard_index = lax.axis_index("seq")
    normed = norm_rows(token_rows, attn_gain)
    normed_part = lax.dynamic_slice_in_dim(normed, shard_index * part_width, part_width, 1)
    seq_count = lax.axis_size("seq")
    group_width = QUERY_HEADS // KEY_VALUE_HEADS
    unit_count = request_number * nearby_heads
    unit_per = -(-unit_count // seq_count)
    unit_index = jnp.minimum(jnp.arange(seq_count * unit_per), unit_count - 1)
    unit_request = unit_index // nearby_heads
    unit_kv_head = (lax.axis_index("tp") * nearby_heads + unit_index % nearby_heads) // group_width
    query_part = jnp.dot(normed_part, query_weight, preferred_element_type=jnp.float32)
    key_value_part = jnp.dot(normed_part, key_value_weight, preferred_element_type=jnp.float32)
    unit_key_value = key_value_part.reshape(request_number, 2, KEY_VALUE_HEADS, HEAD_SIZE)[
        unit_request, :, unit_kv_head, :
    ]
    outgoing = jnp.concatenate(
        [
            query_part.reshape(seq_count, -1),
            unit_key_value.reshape(seq_count, unit_per * 2 * HEAD_SIZE),
        ],
        axis=1,
    )
    summed = jnp.sum(lax.all_to_all(outgoing, "seq", 0, 0, tiled=True), axis=0)
    query_chunk = summed[: query_width * request_number // seq_count]
    own_key_value = summed[query_chunk.shape[0] :].reshape(unit_per, 2, HEAD_SIZE)
    query_sum = lax.all_to_all(
        jnp.broadcast_to(query_chunk[None], (seq_count,) + query_chunk.shape), "seq", 0, 0, tiled=True
    ).reshape(request_number, query_width)
    query_normed = per_head_norm(
        query_sum.reshape(request_number, nearby_heads, HEAD_SIZE), query_gain
    )
    query_rot = rotate(query_normed, lengths).astype(jnp.bfloat16)
    own_unit = lax.dynamic_slice_in_dim(unit_index, shard_index * unit_per, unit_per, 0)
    own_positions = jnp.take(lengths, own_unit // nearby_heads)
    own_key = rotate(per_head_norm(own_key_value[:, None, 0], new_key_gain), own_positions)
    own_key = own_key[:, 0].astype(jnp.bfloat16).astype(jnp.float32)
    own_value = own_key_value[:, 1].astype(jnp.bfloat16).astype(jnp.float32)
    own_query = query_rot.reshape(unit_count, HEAD_SIZE)[own_unit].astype(jnp.float32)
    own_score = jnp.sum(own_query * own_key, axis=1) * scale
    head_mapping = (lax.axis_index("tp") * nearby_heads + jnp.arange(nearby_heads)) // group_width
    slot_number = nearby_cache.shape[0]
    page_token_count = nearby_cache.shape[1]
    global_slot = shard_index * slot_number + jnp.arange(slot_number)
    matches = page_map[:, :, None] == global_slot[None, None, :]
    owner_mask = jnp.any(matches, axis=1)
    page_number = jnp.sum(
        jnp.where(matches, jnp.arange(page_map.shape[1])[None, :, None], 0), axis=(0, 1)
    )
    owner_req = jnp.sum(jnp.where(owner_mask, jnp.arange(request_number)[:, None], 0), axis=0)
    slot_live = jnp.any(owner_mask, axis=0)
    owner_length = jnp.take(lengths, owner_req)
    positions = page_number[:, None] * page_token_count + jnp.arange(page_token_count)[None, :]
    is_valid = slot_live[:, None] & (positions < owner_length[:, None])
    first_kv = jnp.minimum(head_mapping[0], KEY_VALUE_HEADS - 2)
    second = (head_mapping - first_kv)[None, None, :, None] == 1
    key_pair = lax.dynamic_slice_in_dim(nearby_cache, first_kv * HEAD_SIZE, 2 * HEAD_SIZE, 2)
    value_pair = lax.dynamic_slice_in_dim(
        nearby_cache, (KEY_VALUE_HEADS + first_kv) * HEAD_SIZE, 2 * HEAD_SIZE, 2
    )
    key_heads = jnp.where(second, key_pair[:, :, None, HEAD_SIZE:], key_pair[:, :, None, :HEAD_SIZE])
    value_heads = jnp.where(
        second, value_pair[:, :, None, HEAD_SIZE:], value_pair[:, :, None, :HEAD_SIZE]
    )
    slot_query = jnp.einsum(
        "rs,rhd->shd", owner_mask.astype(jnp.bfloat16), query_rot, preferred_element_type=jnp.float32
    ).astype(jnp.bfloat16)
    scores = (
        jnp.einsum("shd,skhd->shk", slot_query, key_heads, preferred_element_type=jnp.float32)
        * scale
    )
    scores = jnp.where(is_valid[:, None, :], scores, NEG_FILL)
    slot_max = jnp.max(scores, axis=2)
    request_max = jnp.max(jnp.where(owner_mask[:, :, None], slot_max[None, :, :], NEG_FILL), axis=1)
    owner_max = jnp.max(jnp.where(owner_mask[:, :, None], request_max[:, None, :], NEG_FILL), axis=0)
    weights = jnp.where(is_valid[:, None, :], jnp.exp(scores - owner_max[:, :, None]), 0.0).astype(
        jnp.bfloat16
    )
    slot_total = jnp.sum(weights.astype(jnp.float32), axis=2)
    slot_weighted = jnp.einsum(
        "shk,skhd->shd", weights, value_heads, preferred_element_type=jnp.float32
    )
    owner_float = owner_mask.astype(jnp.float32)
    request_total = jnp.dot(owner_float, slot_total, precision=lax.Precision.HIGHEST)
    request_weighted = jnp.einsum(
        "rs,shd->rhd", owner_float, slot_weighted, precision=lax.Precision.HIGHEST
    )
    attended = merge_attention(
        request_max.reshape(unit_count),
        request_total.reshape(unit_count),
        request_weighted.reshape(unit_count, HEAD_SIZE),
        own_score,
        own_value,
        "seq",
    ).reshape(request_number, nearby_heads * HEAD_SIZE)
    guide_count = lax.axis_size("guide")
    tp_count = lax.axis_size("tp")
    spread_rows = jnp.broadcast_to(
        attended.reshape(guide_count, 1, half_rows, -1),
        (guide_count, tp_count, half_rows, attended.shape[1]),
    )
    spread_hidden = jnp.broadcast_to(
        token_rows.reshape(guide_count, 1, half_rows, -1),
        (guide_count, tp_count, half_rows, token_rows.shape[1]),
    )
    outgoing = jnp.einsum(
        "gtrk,kc->gtrc", spread_rows, output_weight, preferred_element_type=jnp.float32
    ) + jnp.where(lax.axis_index("tp") == 0, spread_hidden, 0.0)
    outgoing = outgoing.reshape(guide_count * tp_count, half_rows, -1)
    incoming = lax.all_to_all(outgoing, ("guide", "tp"), 0, 0, tiled=True)
    residual = jnp.sum(incoming.reshape(guide_count, tp_count, half_rows, -1), axis=1)
    final_rows = norm_rows(residual, final_gain)
    final_part = lax.dynamic_slice_in_dim(final_rows, shard_index * part_width, part_width, 2)
    both = final_part.reshape(guide_count * half_rows, part_width)
    logit_part = jnp.dot(both, head_weight, preferred_element_type=jnp.float32)
    conditional_part = logit_part[:half_rows]
    unconditional_part = logit_part[half_rows:]
    guided_part = unconditional_part + GUIDE_WEIGHT * (conditional_part - unconditional_part)
    return all_reduce(guided_part, "seq")


def solution(mesh):
    in_specs = (
        P("guide", None, None),
        P(),
        P(),
        P(),
        P(),
        P("seq", "tp"),
        P("seq", None),
        P("tp", None),
        P("seq", "tp"),
        P("guide", "seq", None, None),
        P("guide", None),
        P("guide", None, None),
    )
    out_specs = P("guide", "tp")
    return jax.shard_map(shards, mesh=mesh, in_specs=in_specs, out_specs=out_specs, check_vma=False)
```

```python
import jax
import jax.numpy as jnp
from jax import lax
from jax.sharding import PartitionSpec as P

QUERY_HEADS = 20
KEY_VALUE_HEADS = 5
HEAD_SIZE = 64


GUIDE_WEIGHT = 2.5
NORM_EPS = 1e-06
NEG_FILL = -1e30


def norm_rows(token_rows, scale_gain):
    mean_square = jnp.mean(token_rows * token_rows, axis=-1, keepdims=True)
    return (token_rows * lax.rsqrt(mean_square + NORM_EPS) * scale_gain).astype(jnp.bfloat16)


def per_head_norm(vectors, head_gain):
    mean_square = jnp.mean(vectors * vectors, axis=-1, keepdims=True)
    return vectors * lax.rsqrt(mean_square + NORM_EPS) * head_gain


def rotate(vectors, positions):
    half_dim = vectors.shape[-1] // 2
    frequency = 10000.0 ** (-jnp.arange(half_dim).astype(jnp.float32) / half_dim)
    angles = positions.astype(jnp.float32)[:, None] * frequency[None, :]
    cosine = jnp.cos(angles)[:, None, :]
    sine_part = jnp.sin(angles)[:, None, :]
    first_half = vectors[..., :half_dim]
    second_half = vectors[..., half_dim:]
    return jnp.concatenate(
        [
            first_half * cosine - second_half * sine_part,
            second_half * cosine + first_half * sine_part,
        ],
        axis=-1,
    )


def all_reduce(value, axis):
    count = lax.axis_size(axis)
    flat = value.reshape(-1)
    chunk = -(-flat.size // count)
    chunk = -(-chunk // 128) * 128
    flat = jnp.pad(flat, (0, count * chunk - flat.size))
    parts = lax.all_to_all(flat.reshape(count, chunk), axis, 0, 0, tiled=True)
    total = jnp.sum(parts, axis=0, keepdims=True)
    whole = lax.all_to_all(jnp.broadcast_to(total, (count, chunk)), axis, 0, 0, tiled=True)
    return whole.reshape(-1)[: value.size].reshape(value.shape)


def all_reduce_columns(value, axis):
    count = lax.axis_size(axis)
    rows, columns = value.shape
    if columns % count:
        return all_reduce(value, axis)
    parts = lax.all_to_all(value, axis, 1, 0, tiled=True)
    total = jnp.sum(parts.reshape(count, rows, columns // count), axis=0)
    whole = lax.all_to_all(
        jnp.broadcast_to(total[None], (count, rows, columns // count)), axis, 0, 2, tiled=True
    )
    return whole[0]


def spread_units(units, count, fill):
    per = -(-units.shape[0] // count)
    padding = [(0, count * per - units.shape[0])] + [(0, 0)] * (units.ndim - 1)
    return jnp.pad(units, padding, constant_values=fill).reshape((count, per) + units.shape[1:])


def merge_attention(local_max, local_total, local_weighted, own_score, own_value, axis):
    count = lax.axis_size(axis)
    unit_count = local_max.shape[0]
    spread = jnp.concatenate(
        [
            spread_units(local_max[:, None], count, NEG_FILL),
            spread_units(jnp.concatenate([local_total[:, None], local_weighted], axis=1), count, 0.0),
        ],
        axis=2,
    )
    parts = lax.all_to_all(spread, axis, 0, 0, tiled=True)
    part_max = parts[:, :, 0]
    merged_max = jnp.max(part_max, axis=0)
    rescale = jnp.exp(part_max - merged_max[None, :])
    merged_total = jnp.sum(rescale * parts[:, :, 1], axis=0)
    merged_weighted = jnp.sum(rescale[:, :, None] * parts[:, :, 2:], axis=0)
    row_max = jnp.maximum(merged_max, own_score)
    old_scale = jnp.exp(merged_max - row_max)
    self_weight = jnp.exp(own_score - row_max)
    denominator = merged_total * old_scale + self_weight
    weighted = merged_weighted * old_scale[:, None] + self_weight[:, None] * own_value
    fraction = jnp.concatenate([weighted, denominator[:, None]], axis=1)
    gathered = lax.all_to_all(
        jnp.broadcast_to(fraction.reshape(1, -1), (count, fraction.size)), axis, 0, 0, tiled=True
    ).reshape(-1, fraction.shape[-1])[:unit_count]
    return (gathered[:, :-1] / gathered[:, -1:]).astype(jnp.bfloat16)


def shards(
    hidden,
    attn_gain,
    final_gain,
    query_gain,
    new_key_gain,
    query_weight,
    key_value_weight,
    output_weight,
    head_weight,
    page_cache,
    cache_length,
    page_table,
):
    token_rows = hidden[0].astype(jnp.float32)
    lengths = cache_length[0]
    page_map = page_table[0]
    nearby_cache = page_cache[0]
    request_number = token_rows.shape[0]
    half_rows = request_number // 2
    part_width = query_weight.shape[0]
    nearby_heads = query_weight.shape[1] // HEAD_SIZE
    query_width = query_weight.shape[1]
    scale = 1.0 / HEAD_SIZE**0.5
    shard_index = lax.axis_index("seq")
    normed = norm_rows(token_rows, attn_gain)
    normed_part = lax.dynamic_slice_in_dim(normed, shard_index * part_width, part_width, 1)
    seq_count = lax.axis_size("seq")
    group_width = QUERY_HEADS // KEY_VALUE_HEADS
    unit_count = request_number * nearby_heads
    unit_per = -(-unit_count // seq_count)
    unit_index = jnp.minimum(jnp.arange(seq_count * unit_per), unit_count - 1)
    unit_request = unit_index // nearby_heads
    unit_kv_head = (lax.axis_index("tp") * nearby_heads + unit_index % nearby_heads) // group_width
    query_part = jnp.dot(normed_part, query_weight, preferred_element_type=jnp.float32)
    key_value_part = jnp.dot(normed_part, key_value_weight, preferred_element_type=jnp.float32)
    unit_key_value = key_value_part.reshape(request_number, 2, KEY_VALUE_HEADS, HEAD_SIZE)[
        unit_request, :, unit_kv_head, :
    ]
    outgoing = jnp.concatenate(
        [
            query_part.reshape(seq_count, -1),
            unit_key_value.reshape(seq_count, unit_per * 2 * HEAD_SIZE),
        ],
        axis=1,
    )
    received = lax.all_to_all(outgoing, "seq", 0, 0, tiled=True)
    chunk_width = query_width * request_number // seq_count
    own_key_value = jnp.sum(received[:, chunk_width:], axis=0).reshape(unit_per, 2, HEAD_SIZE)
    query_sum = lax.all_to_all(
        jnp.dot(
            jnp.ones((seq_count, seq_count), jnp.float32),
            received[:, :chunk_width],
            precision=lax.Precision.HIGHEST,
            preferred_element_type=jnp.float32,
        ),
        "seq",
        0,
        0,
        tiled=True,
    ).reshape(request_number, query_width)
    query_normed = per_head_norm(
        query_sum.reshape(request_number, nearby_heads, HEAD_SIZE), query_gain
    )
    query_rot = rotate(query_normed, lengths).astype(jnp.bfloat16)
    own_unit = lax.dynamic_slice_in_dim(unit_index, shard_index * unit_per, unit_per, 0)
    own_positions = jnp.take(lengths, own_unit // nearby_heads)
    own_key = rotate(per_head_norm(own_key_value[:, None, 0], new_key_gain), own_positions)
    own_key = own_key[:, 0].astype(jnp.bfloat16).astype(jnp.float32)
    own_value = own_key_value[:, 1].astype(jnp.bfloat16).astype(jnp.float32)
    own_query = query_rot.reshape(unit_count, HEAD_SIZE)[own_unit].astype(jnp.float32)
    own_score = jnp.sum(own_query * own_key, axis=1) * scale
    head_mapping = (lax.axis_index("tp") * nearby_heads + jnp.arange(nearby_heads)) // group_width
    slot_number = nearby_cache.shape[0]
    page_token_count = nearby_cache.shape[1]
    global_slot = shard_index * slot_number + jnp.arange(slot_number)
    matches = page_map[:, :, None] == global_slot[None, None, :]
    owner_mask = jnp.any(matches, axis=1)
    page_number = jnp.sum(
        jnp.where(matches, jnp.arange(page_map.shape[1])[None, :, None], 0), axis=(0, 1)
    )
    owner_req = jnp.sum(jnp.where(owner_mask, jnp.arange(request_number)[:, None], 0), axis=0)
    slot_live = jnp.any(owner_mask, axis=0)
    owner_length = jnp.take(lengths, owner_req)
    positions = page_number[:, None] * page_token_count + jnp.arange(page_token_count)[None, :]
    is_valid = slot_live[:, None] & (positions < owner_length[:, None])
    first_kv = jnp.minimum(head_mapping[0], KEY_VALUE_HEADS - 2)
    second = (head_mapping - first_kv)[None, None, :, None] == 1
    key_pair = lax.dynamic_slice_in_dim(nearby_cache, first_kv * HEAD_SIZE, 2 * HEAD_SIZE, 2)
    value_pair = lax.dynamic_slice_in_dim(
        nearby_cache, (KEY_VALUE_HEADS + first_kv) * HEAD_SIZE, 2 * HEAD_SIZE, 2
    )
    key_heads = jnp.where(second, key_pair[:, :, None, HEAD_SIZE:], key_pair[:, :, None, :HEAD_SIZE])
    value_heads = jnp.where(
        second, value_pair[:, :, None, HEAD_SIZE:], value_pair[:, :, None, :HEAD_SIZE]
    )
    slot_query = jnp.einsum(
        "rs,rhd->shd", owner_mask.astype(jnp.bfloat16), query_rot, preferred_element_type=jnp.float32
    ).astype(jnp.bfloat16)
    scores = (
        jnp.einsum("shd,skhd->shk", slot_query, key_heads, preferred_element_type=jnp.float32)
        * scale
    )
    scores = jnp.where(is_valid[:, None, :], scores, NEG_FILL)
    slot_max = jnp.max(scores, axis=2)
    request_max = jnp.max(jnp.where(owner_mask[:, :, None], slot_max[None, :, :], NEG_FILL), axis=1)
    owner_max = jnp.max(jnp.where(owner_mask[:, :, None], request_max[:, None, :], NEG_FILL), axis=0)
    weights = jnp.where(is_valid[:, None, :], jnp.exp(scores - owner_max[:, :, None]), 0.0).astype(
        jnp.bfloat16
    )
    slot_total = jnp.sum(weights.astype(jnp.float32), axis=2)
    slot_weighted = jnp.einsum(
        "shk,skhd->shd", weights, value_heads, preferred_element_type=jnp.float32
    )
    owner_float = owner_mask.astype(jnp.float32)
    request_total = jnp.dot(owner_float, slot_total, precision=lax.Precision.HIGHEST)
    request_weighted = jnp.einsum(
        "rs,shd->rhd", owner_float, slot_weighted, precision=lax.Precision.HIGHEST
    )
    attended = merge_attention(
        request_max.reshape(unit_count),
        request_total.reshape(unit_count),
        request_weighted.reshape(unit_count, HEAD_SIZE),
        own_score,
        own_value,
        "seq",
    ).reshape(request_number, nearby_heads * HEAD_SIZE)
    output_part = jnp.dot(attended, output_weight, preferred_element_type=jnp.float32)
    output_part = output_part + jnp.where(lax.axis_index("tp") == 0, token_rows, 0.0)
    guide_count = lax.axis_size("guide")
    tp_count = lax.axis_size("tp")
    outgoing = jnp.broadcast_to(
        output_part.reshape(guide_count, 1, half_rows, -1),
        (guide_count, tp_count, half_rows, output_part.shape[1]),
    ).reshape(guide_count * tp_count, half_rows, -1)
    incoming = lax.all_to_all(outgoing, ("guide", "tp"), 0, 0, tiled=True)
    residual = jnp.sum(incoming.reshape(guide_count, tp_count, half_rows, -1), axis=1)
    final_rows = norm_rows(residual, final_gain)
    final_part = lax.dynamic_slice_in_dim(final_rows, shard_index * part_width, part_width, 2)
    both = final_part.reshape(guide_count * half_rows, part_width)
    logit_part = jnp.dot(both, head_weight, preferred_element_type=jnp.float32)
    conditional_part = logit_part[:half_rows]
    unconditional_part = logit_part[half_rows:]
    guided_part = unconditional_part + GUIDE_WEIGHT * (conditional_part - unconditional_part)
    return all_reduce(guided_part, "seq")


def solution(mesh):
    in_specs = (
        P("guide", None, None),
        P(),
        P(),
        P(),
        P(),
        P("seq", "tp"),
        P("seq", None),
        P("tp", None),
        P("seq", "tp"),
        P("guide", "seq", None, None),
        P("guide", None),
        P("guide", None, None),
    )
    out_specs = P("guide", "tp")
    return jax.shard_map(shards, mesh=mesh, in_specs=in_specs, out_specs=out_specs, check_vma=False)
```

```python
import jax
import jax.numpy as jnp
from jax import lax
from jax.sharding import PartitionSpec as P

QUERY_HEADS = 20
KEY_VALUE_HEADS = 5
HEAD_SIZE = 64


GUIDE_WEIGHT = 2.5
NORM_EPS = 1e-06
NEG_FILL = -1e30


def norm_rows(token_rows, scale_gain):
    mean_square = jnp.mean(token_rows * token_rows, axis=-1, keepdims=True)
    return (token_rows * lax.rsqrt(mean_square + NORM_EPS) * scale_gain).astype(jnp.bfloat16)


def per_head_norm(vectors, head_gain):
    mean_square = jnp.mean(vectors * vectors, axis=-1, keepdims=True)
    return vectors * lax.rsqrt(mean_square + NORM_EPS) * head_gain


def rotate(vectors, positions):
    half_dim = vectors.shape[-1] // 2
    frequency = 10000.0 ** (-jnp.arange(half_dim).astype(jnp.float32) / half_dim)
    angles = positions.astype(jnp.float32)[:, None] * frequency[None, :]
    cosine = jnp.cos(angles)[:, None, :]
    sine_part = jnp.sin(angles)[:, None, :]
    first_half = vectors[..., :half_dim]
    second_half = vectors[..., half_dim:]
    return jnp.concatenate(
        [
            first_half * cosine - second_half * sine_part,
            second_half * cosine + first_half * sine_part,
        ],
        axis=-1,
    )


def all_reduce(value, axis):
    count = lax.axis_size(axis)
    flat = value.reshape(-1)
    chunk = -(-flat.size // count)
    chunk = -(-chunk // 128) * 128
    flat = jnp.pad(flat, (0, count * chunk - flat.size))
    parts = lax.all_to_all(flat.reshape(count, chunk), axis, 0, 0, tiled=True)
    total = jnp.sum(parts, axis=0, keepdims=True)
    whole = lax.all_to_all(jnp.broadcast_to(total, (count, chunk)), axis, 0, 0, tiled=True)
    return whole.reshape(-1)[: value.size].reshape(value.shape)


def all_reduce_columns(value, axis):
    count = lax.axis_size(axis)
    rows, columns = value.shape
    if columns % count:
        return all_reduce(value, axis)
    parts = lax.all_to_all(value, axis, 1, 0, tiled=True)
    total = jnp.sum(parts.reshape(count, rows, columns // count), axis=0)
    whole = lax.all_to_all(
        jnp.broadcast_to(total[None], (count, rows, columns // count)), axis, 0, 2, tiled=True
    )
    return whole[0]


def spread_units(units, count, fill):
    per = -(-units.shape[0] // count)
    padding = [(0, count * per - units.shape[0])] + [(0, 0)] * (units.ndim - 1)
    return jnp.pad(units, padding, constant_values=fill).reshape((count, per) + units.shape[1:])


def merge_attention(local_max, local_total, local_weighted, own_score, own_value, axis):
    count = lax.axis_size(axis)
    unit_count = local_max.shape[0]
    spread = jnp.concatenate(
        [
            spread_units(local_max[:, None], count, NEG_FILL),
            spread_units(jnp.concatenate([local_total[:, None], local_weighted], axis=1), count, 0.0),
        ],
        axis=2,
    )
    parts = lax.all_to_all(spread, axis, 0, 0, tiled=True)
    part_max = parts[:, :, 0]
    merged_max = jnp.max(part_max, axis=0)
    rescale = jnp.exp(part_max - merged_max[None, :])
    merged_total = jnp.sum(rescale * parts[:, :, 1], axis=0)
    merged_weighted = jnp.sum(rescale[:, :, None] * parts[:, :, 2:], axis=0)
    row_max = jnp.maximum(merged_max, own_score)
    old_scale = jnp.exp(merged_max - row_max)
    self_weight = jnp.exp(own_score - row_max)
    denominator = merged_total * old_scale + self_weight
    weighted = merged_weighted * old_scale[:, None] + self_weight[:, None] * own_value
    fraction = jnp.concatenate([weighted, denominator[:, None]], axis=1)
    gathered = lax.all_to_all(
        jnp.broadcast_to(fraction.reshape(1, -1), (count, fraction.size)), axis, 0, 0, tiled=True
    ).reshape(-1, fraction.shape[-1])[:unit_count]
    return (gathered[:, :-1] / gathered[:, -1:]).astype(jnp.bfloat16)


def shards(
    hidden,
    attn_gain,
    final_gain,
    query_gain,
    new_key_gain,
    query_weight,
    key_value_weight,
    output_weight,
    head_weight,
    page_cache,
    cache_length,
    page_table,
):
    token_rows = hidden[0].astype(jnp.float32)
    lengths = cache_length[0]
    page_map = page_table[0]
    nearby_cache = page_cache[0]
    request_number = token_rows.shape[0]
    half_rows = request_number // 2
    part_width = query_weight.shape[0]
    nearby_heads = query_weight.shape[1] // HEAD_SIZE
    query_width = query_weight.shape[1]
    scale = 1.0 / HEAD_SIZE**0.5
    shard_index = lax.axis_index("seq")
    normed = norm_rows(token_rows, attn_gain)
    normed_part = lax.dynamic_slice_in_dim(normed, shard_index * part_width, part_width, 1)
    seq_count = lax.axis_size("seq")
    group_width = QUERY_HEADS // KEY_VALUE_HEADS
    unit_count = request_number * nearby_heads
    unit_per = -(-unit_count // seq_count)
    unit_index = jnp.minimum(jnp.arange(seq_count * unit_per), unit_count - 1)
    unit_request = unit_index // nearby_heads
    unit_kv_head = (lax.axis_index("tp") * nearby_heads + unit_index % nearby_heads) // group_width
    query_part = jnp.dot(normed_part, query_weight, preferred_element_type=jnp.float32)
    key_value_part = jnp.dot(normed_part, key_value_weight, preferred_element_type=jnp.float32)
    unit_key_value = key_value_part.reshape(request_number, 2, KEY_VALUE_HEADS, HEAD_SIZE)[
        unit_request, :, unit_kv_head, :
    ]
    outgoing = jnp.concatenate(
        [
            query_part.reshape(seq_count, -1),
            unit_key_value.reshape(seq_count, unit_per * 2 * HEAD_SIZE),
        ],
        axis=1,
    )
    summed = jnp.sum(lax.all_to_all(outgoing, "seq", 0, 0, tiled=True), axis=0)
    query_chunk = summed[: query_width * request_number // seq_count]
    own_key_value = summed[query_chunk.shape[0] :].reshape(unit_per, 2, HEAD_SIZE)
    query_sum = lax.all_to_all(
        jnp.broadcast_to(query_chunk[None], (seq_count,) + query_chunk.shape), "seq", 0, 0, tiled=True
    ).reshape(request_number, query_width)
    query_normed = per_head_norm(
        query_sum.reshape(request_number, nearby_heads, HEAD_SIZE), query_gain
    )
    query_rot = rotate(query_normed, lengths).astype(jnp.bfloat16)
    own_unit = lax.dynamic_slice_in_dim(unit_index, shard_index * unit_per, unit_per, 0)
    own_positions = jnp.take(lengths, own_unit // nearby_heads)
    own_key = rotate(per_head_norm(own_key_value[:, None, 0], new_key_gain), own_positions)
    own_key = own_key[:, 0].astype(jnp.bfloat16).astype(jnp.float32)
    own_value = own_key_value[:, 1].astype(jnp.bfloat16).astype(jnp.float32)
    own_query = query_rot.reshape(unit_count, HEAD_SIZE)[own_unit].astype(jnp.float32)
    own_score = jnp.sum(own_query * own_key, axis=1) * scale
    head_mapping = (lax.axis_index("tp") * nearby_heads + jnp.arange(nearby_heads)) // group_width
    slot_number = nearby_cache.shape[0]
    page_token_count = nearby_cache.shape[1]
    global_slot = shard_index * slot_number + jnp.arange(slot_number)
    matches = page_map[:, :, None] == global_slot[None, None, :]
    owner_mask = jnp.any(matches, axis=1)
    page_number = jnp.sum(
        jnp.where(matches, jnp.arange(page_map.shape[1])[None, :, None], 0), axis=(0, 1)
    )
    owner_req = jnp.sum(jnp.where(owner_mask, jnp.arange(request_number)[:, None], 0), axis=0)
    slot_live = jnp.any(owner_mask, axis=0)
    owner_length = jnp.take(lengths, owner_req)
    positions = page_number[:, None] * page_token_count + jnp.arange(page_token_count)[None, :]
    is_valid = slot_live[:, None] & (positions < owner_length[:, None])
    first_kv = jnp.minimum(head_mapping[0], KEY_VALUE_HEADS - 2)
    second = (head_mapping - first_kv)[None, None, :, None] == 1
    key_pair = lax.dynamic_slice_in_dim(nearby_cache, first_kv * HEAD_SIZE, 2 * HEAD_SIZE, 2)
    value_pair = lax.dynamic_slice_in_dim(
        nearby_cache, (KEY_VALUE_HEADS + first_kv) * HEAD_SIZE, 2 * HEAD_SIZE, 2
    )
    key_heads = jnp.where(second, key_pair[:, :, None, HEAD_SIZE:], key_pair[:, :, None, :HEAD_SIZE])
    value_heads = jnp.where(
        second, value_pair[:, :, None, HEAD_SIZE:], value_pair[:, :, None, :HEAD_SIZE]
    )
    slot_query = jnp.einsum(
        "rs,rhd->shd", owner_mask.astype(jnp.bfloat16), query_rot, preferred_element_type=jnp.float32
    ).astype(jnp.bfloat16)
    scores = (
        jnp.einsum("shd,skhd->shk", slot_query, key_heads, preferred_element_type=jnp.float32)
        * scale
    )
    scores = jnp.where(is_valid[:, None, :], scores, NEG_FILL)
    slot_max = jnp.max(scores, axis=2)
    request_max = jnp.max(jnp.where(owner_mask[:, :, None], slot_max[None, :, :], NEG_FILL), axis=1)
    owner_max = jnp.max(jnp.where(owner_mask[:, :, None], request_max[:, None, :], NEG_FILL), axis=0)
    weights = jnp.where(is_valid[:, None, :], jnp.exp(scores - owner_max[:, :, None]), 0.0).astype(
        jnp.bfloat16
    )
    slot_total = jnp.sum(weights.astype(jnp.float32), axis=2)
    slot_weighted = jnp.einsum(
        "shk,skhd->shd", weights, value_heads, preferred_element_type=jnp.float32
    )
    owner_float = owner_mask.astype(jnp.float32)
    request_total = jnp.dot(owner_float, slot_total, precision=lax.Precision.HIGHEST)
    request_weighted = jnp.einsum(
        "rs,shd->rhd", owner_float, slot_weighted, precision=lax.Precision.HIGHEST
    )
    attended = merge_attention(
        request_max.reshape(unit_count),
        request_total.reshape(unit_count),
        request_weighted.reshape(unit_count, HEAD_SIZE),
        own_score,
        own_value,
        "seq",
    ).reshape(request_number, nearby_heads * HEAD_SIZE)
    output_part = jnp.dot(attended, output_weight, preferred_element_type=jnp.float32)
    output_part = output_part + jnp.where(lax.axis_index("tp") == 0, token_rows, 0.0)
    guide_count = lax.axis_size("guide")
    tp_count = lax.axis_size("tp")
    outgoing = jnp.broadcast_to(
        output_part.reshape(guide_count, 1, half_rows, -1),
        (guide_count, tp_count, half_rows, output_part.shape[1]),
    ).reshape(guide_count * tp_count, half_rows, -1)
    incoming = lax.all_to_all(outgoing, ("guide", "tp"), 0, 0, tiled=True)
    residual = jnp.sum(incoming.reshape(guide_count, tp_count, half_rows, -1), axis=1)
    final_rows = norm_rows(residual, final_gain)
    final_part = lax.dynamic_slice_in_dim(final_rows, shard_index * part_width, part_width, 2)
    both = final_part.reshape(guide_count * half_rows, part_width)
    seq_count = lax.axis_size("seq")
    vocab = head_weight.shape[1]
    vocab_padded = -(-vocab * half_rows // (seq_count * 128)) * seq_count * 128 // half_rows
    padded_weight = jnp.pad(head_weight, ((0, 0), (0, vocab_padded - vocab)))
    logit_part = jnp.dot(both, padded_weight, preferred_element_type=jnp.float32)
    conditional_part = logit_part[:half_rows]
    unconditional_part = logit_part[half_rows:]
    guided_part = unconditional_part + GUIDE_WEIGHT * (conditional_part - unconditional_part)
    return all_reduce(guided_part, "seq")[:, :vocab]


def solution(mesh):
    in_specs = (
        P("guide", None, None),
        P(),
        P(),
        P(),
        P(),
        P("seq", "tp"),
        P("seq", None),
        P("tp", None),
        P("seq", "tp"),
        P("guide", "seq", None, None),
        P("guide", None),
        P("guide", None, None),
    )
    out_specs = P("guide", "tp")
    return jax.shard_map(shards, mesh=mesh, in_specs=in_specs, out_specs=out_specs, check_vma=False)
```

```python
import jax
import jax.numpy as jnp
from jax import lax
from jax.sharding import PartitionSpec as P

QUERY_HEADS = 20
KEY_VALUE_HEADS = 5
HEAD_SIZE = 64


GUIDE_WEIGHT = 2.5
NORM_EPS = 1e-06
NEG_FILL = -1e30


def norm_rows(token_rows, scale_gain):
    mean_square = jnp.mean(token_rows * token_rows, axis=-1, keepdims=True)
    return (token_rows * lax.rsqrt(mean_square + NORM_EPS) * scale_gain).astype(jnp.bfloat16)


def per_head_norm(vectors, head_gain):
    mean_square = jnp.mean(vectors * vectors, axis=-1, keepdims=True)
    return vectors * lax.rsqrt(mean_square + NORM_EPS) * head_gain


def rotate(vectors, positions):
    half_dim = vectors.shape[-1] // 2
    frequency = 10000.0 ** (-jnp.arange(half_dim).astype(jnp.float32) / half_dim)
    angles = positions.astype(jnp.float32)[:, None] * frequency[None, :]
    cosine = jnp.cos(angles)[:, None, :]
    sine_part = jnp.sin(angles)[:, None, :]
    first_half = vectors[..., :half_dim]
    second_half = vectors[..., half_dim:]
    return jnp.concatenate(
        [
            first_half * cosine - second_half * sine_part,
            second_half * cosine + first_half * sine_part,
        ],
        axis=-1,
    )


def all_reduce(value, axis):
    count = lax.axis_size(axis)
    flat = value.reshape(-1)
    chunk = -(-flat.size // count)
    flat = jnp.pad(flat, (0, count * chunk - flat.size))
    parts = lax.all_to_all(flat.reshape(count, chunk), axis, 0, 0, tiled=True)
    total = jnp.sum(parts, axis=0, keepdims=True)
    whole = lax.all_to_all(jnp.broadcast_to(total, (count, chunk)), axis, 0, 0, tiled=True)
    return whole.reshape(-1)[: value.size].reshape(value.shape)


def all_reduce_columns(value, axis):
    count = lax.axis_size(axis)
    rows, columns = value.shape
    if columns % count:
        return all_reduce(value, axis)
    parts = lax.all_to_all(value, axis, 1, 0, tiled=True)
    total = jnp.sum(parts.reshape(count, rows, columns // count), axis=0)
    whole = lax.all_to_all(
        jnp.broadcast_to(total[None], (count, rows, columns // count)), axis, 0, 2, tiled=True
    )
    return whole[0]


def spread_units(units, count, fill):
    per = -(-units.shape[0] // count)
    padding = [(0, count * per - units.shape[0])] + [(0, 0)] * (units.ndim - 1)
    return jnp.pad(units, padding, constant_values=fill).reshape((count, per) + units.shape[1:])


def merge_attention(local_max, local_total, local_weighted, own_score, own_value, axis):
    count = lax.axis_size(axis)
    unit_count = local_max.shape[0]
    spread = jnp.concatenate(
        [
            spread_units(local_max[:, None], count, NEG_FILL),
            spread_units(jnp.concatenate([local_total[:, None], local_weighted], axis=1), count, 0.0),
        ],
        axis=2,
    )
    parts = lax.all_to_all(spread, axis, 0, 0, tiled=True)
    part_max = parts[:, :, 0]
    merged_max = jnp.max(part_max, axis=0)
    rescale = jnp.exp(part_max - merged_max[None, :])
    merged_total = jnp.sum(rescale * parts[:, :, 1], axis=0)
    merged_weighted = jnp.sum(rescale[:, :, None] * parts[:, :, 2:], axis=0)
    row_max = jnp.maximum(merged_max, own_score)
    old_scale = jnp.exp(merged_max - row_max)
    self_weight = jnp.exp(own_score - row_max)
    denominator = merged_total * old_scale + self_weight
    weighted = merged_weighted * old_scale[:, None] + self_weight[:, None] * own_value
    fraction = jnp.concatenate([weighted, denominator[:, None]], axis=1)
    gathered = lax.all_to_all(
        jnp.broadcast_to(fraction.reshape(1, -1), (count, fraction.size)), axis, 0, 0, tiled=True
    ).reshape(-1, fraction.shape[-1])[:unit_count]
    return (gathered[:, :-1] / gathered[:, -1:]).astype(jnp.bfloat16)


def shards(
    hidden,
    attn_gain,
    final_gain,
    query_gain,
    new_key_gain,
    query_weight,
    key_value_weight,
    output_weight,
    head_weight,
    page_cache,
    cache_length,
    page_table,
):
    token_rows = hidden[0].astype(jnp.float32)
    lengths = cache_length[0]
    page_map = page_table[0]
    nearby_cache = page_cache[0]
    request_number = token_rows.shape[0]
    half_rows = request_number // 2
    part_width = query_weight.shape[0]
    nearby_heads = query_weight.shape[1] // HEAD_SIZE
    query_width = query_weight.shape[1]
    scale = 1.0 / HEAD_SIZE**0.5
    shard_index = lax.axis_index("seq")
    normed = norm_rows(token_rows, attn_gain)
    normed_part = lax.dynamic_slice_in_dim(normed, shard_index * part_width, part_width, 1)
    seq_count = lax.axis_size("seq")
    group_width = QUERY_HEADS // KEY_VALUE_HEADS
    unit_count = request_number * nearby_heads
    unit_per = -(-unit_count // seq_count)
    unit_index = jnp.minimum(jnp.arange(seq_count * unit_per), unit_count - 1)
    unit_request = unit_index // nearby_heads
    unit_kv_head = (lax.axis_index("tp") * nearby_heads + unit_index % nearby_heads) // group_width
    query_part = jnp.dot(normed_part, query_weight, preferred_element_type=jnp.float32)
    key_value_part = jnp.dot(normed_part, key_value_weight, preferred_element_type=jnp.float32)
    unit_key_value = key_value_part.reshape(request_number, 2, KEY_VALUE_HEADS, HEAD_SIZE)[
        unit_request, :, unit_kv_head, :
    ]
    outgoing = jnp.concatenate(
        [
            query_part.reshape(seq_count, -1),
            unit_key_value.reshape(seq_count, unit_per * 2 * HEAD_SIZE),
        ],
        axis=1,
    )
    summed = jnp.sum(lax.all_to_all(outgoing, "seq", 0, 0, tiled=True), axis=0)
    query_chunk = summed[: query_width * request_number // seq_count]
    own_key_value = summed[query_chunk.shape[0] :].reshape(unit_per, 2, HEAD_SIZE)
    query_sum = lax.all_to_all(
        jnp.broadcast_to(query_chunk[None], (seq_count,) + query_chunk.shape), "seq", 0, 0, tiled=True
    ).reshape(request_number, query_width)
    query_normed = per_head_norm(
        query_sum.reshape(request_number, nearby_heads, HEAD_SIZE), query_gain
    )
    query_rot = rotate(query_normed, lengths).astype(jnp.bfloat16)
    own_unit = lax.dynamic_slice_in_dim(unit_index, shard_index * unit_per, unit_per, 0)
    own_positions = jnp.take(lengths, own_unit // nearby_heads)
    own_key = rotate(per_head_norm(own_key_value[:, None, 0], new_key_gain), own_positions)
    own_key = own_key[:, 0].astype(jnp.bfloat16).astype(jnp.float32)
    own_value = own_key_value[:, 1].astype(jnp.bfloat16).astype(jnp.float32)
    own_query = query_rot.reshape(unit_count, HEAD_SIZE)[own_unit].astype(jnp.float32)
    own_score = jnp.sum(own_query * own_key, axis=1) * scale
    head_mapping = (lax.axis_index("tp") * nearby_heads + jnp.arange(nearby_heads)) // group_width
    slot_number = nearby_cache.shape[0]
    page_token_count = nearby_cache.shape[1]
    global_slot = shard_index * slot_number + jnp.arange(slot_number)
    matches = page_map[:, :, None] == global_slot[None, None, :]
    owner_mask = jnp.any(matches, axis=1)
    page_number = jnp.sum(
        jnp.where(matches, jnp.arange(page_map.shape[1])[None, :, None], 0), axis=(0, 1)
    )
    owner_req = jnp.sum(jnp.where(owner_mask, jnp.arange(request_number)[:, None], 0), axis=0)
    slot_live = jnp.any(owner_mask, axis=0)
    owner_length = jnp.take(lengths, owner_req)
    positions = page_number[:, None] * page_token_count + jnp.arange(page_token_count)[None, :]
    is_valid = slot_live[:, None] & (positions < owner_length[:, None])
    first_kv = jnp.minimum(head_mapping[0], KEY_VALUE_HEADS - 2)
    second = (head_mapping - first_kv)[None, None, :, None] == 1
    key_pair = lax.dynamic_slice_in_dim(nearby_cache, first_kv * HEAD_SIZE, 2 * HEAD_SIZE, 2)
    value_pair = lax.dynamic_slice_in_dim(
        nearby_cache, (KEY_VALUE_HEADS + first_kv) * HEAD_SIZE, 2 * HEAD_SIZE, 2
    )
    key_heads = jnp.where(second, key_pair[:, :, None, HEAD_SIZE:], key_pair[:, :, None, :HEAD_SIZE])
    value_heads = jnp.where(
        second, value_pair[:, :, None, HEAD_SIZE:], value_pair[:, :, None, :HEAD_SIZE]
    )
    slot_query = jnp.einsum(
        "rs,rhd->shd", owner_mask.astype(jnp.bfloat16), query_rot, preferred_element_type=jnp.float32
    ).astype(jnp.bfloat16)
    scores = (
        jnp.einsum("shd,skhd->shk", slot_query, key_heads, preferred_element_type=jnp.float32)
        * scale
    )
    scores = jnp.where(is_valid[:, None, :], scores, NEG_FILL)
    slot_max = jnp.max(scores, axis=2)
    request_max = jnp.max(jnp.where(owner_mask[:, :, None], slot_max[None, :, :], NEG_FILL), axis=1)
    owner_max = jnp.max(jnp.where(owner_mask[:, :, None], request_max[:, None, :], NEG_FILL), axis=0)
    weights = jnp.where(is_valid[:, None, :], jnp.exp(scores - owner_max[:, :, None]), 0.0).astype(
        jnp.bfloat16
    )
    slot_total = jnp.sum(weights.astype(jnp.float32), axis=2)
    slot_weighted = jnp.einsum(
        "shk,skhd->shd", weights, value_heads, preferred_element_type=jnp.float32
    )
    owner_float = owner_mask.astype(jnp.float32)
    request_total = jnp.dot(owner_float, slot_total, precision=lax.Precision.HIGHEST)
    request_weighted = jnp.einsum(
        "rs,shd->rhd", owner_float, slot_weighted, precision=lax.Precision.HIGHEST
    )
    attended = merge_attention(
        request_max.reshape(unit_count),
        request_total.reshape(unit_count),
        request_weighted.reshape(unit_count, HEAD_SIZE),
        own_score,
        own_value,
        "seq",
    ).reshape(request_number, nearby_heads * HEAD_SIZE)
    output_part = jnp.dot(attended, output_weight, preferred_element_type=jnp.float32)
    output_part = output_part + jnp.where(lax.axis_index("tp") == 0, token_rows, 0.0)
    guide_count = lax.axis_size("guide")
    tp_count = lax.axis_size("tp")
    outgoing = jnp.broadcast_to(
        output_part.reshape(guide_count, 1, half_rows, -1),
        (guide_count, tp_count, half_rows, output_part.shape[1]),
    ).reshape(guide_count * tp_count, half_rows, -1)
    incoming = lax.all_to_all(outgoing, ("guide", "tp"), 0, 0, tiled=True)
    residual = jnp.sum(incoming.reshape(guide_count, tp_count, half_rows, -1), axis=1)
    final_rows = norm_rows(residual, final_gain)
    final_part = lax.dynamic_slice_in_dim(final_rows, shard_index * part_width, part_width, 2)
    both = final_part.reshape(guide_count * half_rows, part_width)
    logit_part = jnp.dot(both, head_weight, preferred_element_type=jnp.float32)
    conditional_part = logit_part[:half_rows]
    unconditional_part = logit_part[half_rows:]
    guided_part = unconditional_part + GUIDE_WEIGHT * (conditional_part - unconditional_part)
    return all_reduce(guided_part, "seq")


def solution(mesh):
    in_specs = (
        P("guide", None, None),
        P(),
        P(),
        P(),
        P(),
        P("seq", "tp"),
        P("seq", None),
        P("tp", None),
        P("seq", "tp"),
        P("guide", "seq", None, None),
        P("guide", None),
        P("guide", None, None),
    )
    out_specs = P("guide", "tp")
    return jax.shard_map(shards, mesh=mesh, in_specs=in_specs, out_specs=out_specs, check_vma=False)
```
